32 devices in a mesh: member: 2 (over x), wide: 8 (over z, y), narrow: 2 (over core).
Axes of the slice: x: 2, y: 2, z: 4, core: 2. Of those that a mesh axis runs over, the one named last changes fastest.
Arguments:
- noise: bfloat16 [256, 512, 512], P('member', 'wide', 'narrow'), parts along dimension 0, may hold values from -6 to 6
- root_z: bfloat16 [128, 128], replicated, may hold values from -0.5 to 0.5
- root_x: bfloat16 [512, 512], replicated, may hold values from -0.25 to 0.25
- root_y: bfloat16 [512, 512], replicated, may hold values from -0.25 to 0.25
- pressure_start: bfloat16 [256, 512, 512], P('member', 'wide', 'narrow'), parts along dimension 0, may hold values from -4 to 4
- well_x: int32 [512], P('member'), parts along dimension 0, may hold values from 0 to 511
- well_y: int32 [512], P('member'), parts along dimension 0, may hold values from 0 to 511
- well_z: int32 [512], P('member'), parts along dimension 0, may hold values from 0 to 127
- well_rate: float32 [512], P('member'), parts along dimension 0, may hold values from -20 to 20
Outputs:
- log_perm: bfloat16 [256, 512, 512], P('member', 'wide', 'narrow'), parts along dimension 0
- pressure: float32 [256, 512, 512], P('member', 'wide', 'narrow'), parts along dimension 0
The draws below stay inside these ranges and needn't reach their ends.
There are 2 independent parts, one for each index of `member`. The reference program is written for one: setup_inputs(seed, part) draws one part's arguments, and reference() takes and returns one part's arrays. A program takes and returns all parts, laid end to end along the dimension named above; an argument that names none is the same for every part. Nothing has to cross between parts.
All inputs are finite; a program needn't handle non-finite values.
Results may differ from the reference program's by a relative error of at most 0.002.
The reference program's roundings to bfloat16 on the way (of `first` and `second`) count: a program that leaves them out, or rounds other values in their place, can miss the bound.
Values may be sent and summed in bfloat16 or wider, within the bound.
No kernel may reach another device: no remote copies, remote signals or barrier semaphores. Data moves between devices by JAX's collectives and lax.ppermute only.
A program may use at most 128 MiB of HBM per device.

```python
import jax
import jax.numpy as jnp

NX = 512
NY = 512
NZ = 128
STEPS = 2
WELLS = 256


def place_ends(entries, own_key, least, high):
    extent = entries.shape
    place = [jax.random.randint(jax.random.fold_in(own_key, axis), (), 0, extent[axis]) for axis in range(len(extent))]
    entries = entries.at[tuple(place)].set(least)
    longest = extent.index(max(extent))
    place[longest] = (place[longest] + 1) % extent[longest]
    return entries.at[tuple(place)].set(high)


def steps_of(own_key, extent, cuts, low, largest):
    level, own = 1.0, jax.random.fold_in(own_key, 6)
    for position, parts in cuts:
        heights = jnp.exp(jax.random.uniform(jax.random.fold_in(own, position), (parts,), jnp.float32, low / len(cuts), largest / len(cuts)))
        level = level * jnp.repeat(heights, extent[position] // parts).reshape([-1 if axis == position else 1 for axis in range(len(extent))])
    return level


def normal_values(stream_key, shape, spread, reach, pieces=(), dtype=jnp.bfloat16):
    entries = jax.random.normal(stream_key, shape, jnp.float32) * spread
    if len(pieces) > 0:
        entries = steps_of(stream_key, shape, pieces, -0.22, 0.18) * entries
    return jnp.clip(entries, min=-reach, max=reach).astype(dtype)


def setup_inputs(seed: int = 0, part: int = 0) -> dict:
    arg_keys = jax.random.split(jax.random.key(seed), 10)
    own_keys = jax.random.split(jax.random.fold_in(arg_keys[9], part), 10)
    noise = normal_values(own_keys[0], (NZ, NX, NY), 1.0, 6.0, ((1, 8), (2, 2)))
    root_z = normal_values(arg_keys[1], (NZ, NZ), NZ ** -0.5, 0.5)
    root_x = normal_values(arg_keys[2], (NX, NX), NX ** -0.5, 0.25)
    root_y = normal_values(arg_keys[3], (NY, NY), NY ** -0.5, 0.25)
    pressure_start = normal_values(own_keys[4], (NZ, NX, NY), 1.0, 4.0, ((1, 8), (2, 2)))
    well_x = place_ends(jax.random.randint(own_keys[5], (WELLS,), 0, NX), jax.random.fold_in(own_keys[5], 1), 0, NX - 1).astype(jnp.int32)
    well_y = place_ends(jax.random.randint(own_keys[6], (WELLS,), 0, NY), jax.random.fold_in(own_keys[6], 1), 0, NY - 1).astype(jnp.int32)
    well_z = place_ends(jax.random.randint(own_keys[7], (WELLS,), 0, NZ), jax.random.fold_in(own_keys[7], 1), 0, NZ - 1).astype(jnp.int32)
    well_rate = jnp.clip(jax.random.uniform(own_keys[8], (WELLS,), jnp.float32, -20.0, 20.0), -20.0, 20.0)
    return dict(noise=noise, root_z=root_z, root_x=root_x, root_y=root_y, pressure_start=pressure_start, well_x=well_x, well_y=well_y, well_z=well_z, well_rate=well_rate)


STEP_SIZE = 0.03
CAP_LOG = 1.5


def permeability(values):
    return jnp.exp(CAP_LOG * jnp.tanh(values / CAP_LOG))


def neighbours(padded):
    return [padded[2:, 1:-1, 1:-1], padded[:-2, 1:-1, 1:-1],
            padded[1:-1, 2:, 1:-1], padded[1:-1, :-2, 1:-1],
            padded[1:-1, 1:-1, 2:], padded[1:-1, 1:-1, :-2]]


def advance(pressure, around, trans, flow):
    flux = jnp.zeros_like(pressure)
    for factor, other in zip(trans, around):
        flux = flux + factor * (other - pressure)
    return pressure + STEP_SIZE * (flux + flow) / (1.0 + 0.5 * pressure * pressure)


def reference(noise, root_z, root_x, root_y, pressure_start, well_x, well_y, well_z, well_rate):
    depth = noise.shape[0]
    first = jnp.dot(root_z, noise.reshape(depth, -1), preferred_element_type=jnp.float32)
    first = first.reshape(noise.shape).astype(jnp.bfloat16)
    second = jnp.einsum('ia,zay->ziy', root_x.astype(jnp.float32), first.astype(jnp.float32)).astype(jnp.bfloat16)
    log_perm = jnp.einsum('zxb,jb->zxj', second.astype(jnp.float32), root_y.astype(jnp.float32)).astype(jnp.bfloat16)
    perm = jnp.pad(permeability(log_perm.astype(jnp.float32)), 1)
    centre = perm[1:-1, 1:-1, 1:-1]
    trans = [2.0 * centre * other / (centre + other) for other in neighbours(perm)]
    flow = jnp.zeros(noise.shape, jnp.float32).at[well_z, well_x, well_y].add(well_rate.astype(jnp.float32))
    pressure = pressure_start.astype(jnp.float32)
    for step in range(STEPS):
        pressure = advance(pressure, neighbours(jnp.pad(pressure, 1)), trans, flow)
    return log_perm, pressure
```

```python
import jax
import jax.numpy as jnp
from jax import lax
from jax.experimental import pallas as pl
from jax.experimental.pallas import tpu as pltpu
from jax.sharding import PartitionSpec as P

STEPS = 2


STEP_SIZE = 0.03
CAP_LOG = 1.5
CHUNK_Z = 8


def permeability(values):
    return jnp.exp(CAP_LOG * jnp.tanh(values / CAP_LOG))


def harmonic(a, b):
    return 2.0 * a * b / (a + b)


def halos(block, dtype):
    forward_w = [(i, i + 1) for i in range(lax.axis_size("wide") - 1)]
    backward_w = [(j, i) for i, j in forward_w]
    forward_n = [(i, i + 1) for i in range(lax.axis_size("narrow") - 1)]
    backward_n = [(j, i) for i, j in forward_n]
    block = block.astype(dtype)
    x_lo = lax.ppermute(block[:, -1:, :], "wide", forward_w)
    x_hi = lax.ppermute(block[:, :1, :], "wide", backward_w)
    y_lo = lax.ppermute(block[:, :, -1:], "narrow", forward_n)
    y_hi = lax.ppermute(block[:, :, :1], "narrow", backward_n)
    return x_lo, x_hi, y_lo, y_hi


def step_kernel(
    lpm_ref, lpb_ref, lpa_ref, kxl_ref, kxh_ref, kyl_ref, kyh_ref,
    pm_ref, pb_ref, pa_ref, qxl_ref, qxh_ref, qyl_ref, qyh_ref, f_ref, o_ref,
):
    c = pl.program_id(0)
    last = pl.num_programs(0) - 1
    tz, nx, ny = pm_ref.shape
    f32 = jnp.float32

    below = jnp.where(c == 0, 0.0, permeability(lpb_ref[...].astype(f32)))
    above = jnp.where(c == last, 0.0, permeability(lpa_ref[...].astype(f32)))
    centre = permeability(lpm_ref[...].astype(f32))
    ext = jnp.concatenate([below, centre, above], axis=0)
    faces = harmonic(ext[:-1], ext[1:])
    t_zm = faces[:-1]
    t_zp = faces[1:]

    xi = lax.broadcasted_iota(jnp.int32, (tz, nx, ny), 1)
    yi = lax.broadcasted_iota(jnp.int32, (tz, nx, ny), 2)

    fx = harmonic(centre, pltpu.roll(centre, nx - 1, 1))
    t_xp = jnp.where(xi == nx - 1, harmonic(centre[:, nx - 1 :, :], kxh_ref[...]), fx)
    t_xm = jnp.where(xi == 0, harmonic(centre[:, :1, :], kxl_ref[...]), pltpu.roll(fx, 1, 1))
    fy = harmonic(centre, pltpu.roll(centre, ny - 1, 2))
    t_yp = jnp.where(yi == ny - 1, harmonic(centre[:, :, ny - 1 :], kyh_ref[...]), fy)
    t_ym = jnp.where(yi == 0, harmonic(centre[:, :, :1], kyl_ref[...]), pltpu.roll(fy, 1, 2))

    p = pm_ref[...].astype(f32)
    pext = jnp.concatenate([pb_ref[...].astype(f32), p, pa_ref[...].astype(f32)], axis=0)
    n_xp = jnp.where(xi == nx - 1, qxh_ref[...].astype(f32), pltpu.roll(p, nx - 1, 1))
    n_xm = jnp.where(xi == 0, qxl_ref[...].astype(f32), pltpu.roll(p, 1, 1))
    n_yp = jnp.where(yi == ny - 1, qyh_ref[...].astype(f32), pltpu.roll(p, ny - 1, 2))
    n_ym = jnp.where(yi == 0, qyl_ref[...].astype(f32), pltpu.roll(p, 1, 2))

    flux = t_zp * (pext[2:] - p)
    flux = flux + t_zm * (pext[:-2] - p)
    flux = flux + t_xp * (n_xp - p)
    flux = flux + t_xm * (n_xm - p)
    flux = flux + t_yp * (n_yp - p)
    flux = flux + t_ym * (n_ym - p)
    o_ref[...] = p + STEP_SIZE * (flux + f_ref[...]) / (1.0 + 0.5 * p * p)


def advance(log_perm, perm_halos, pressure, pressure_halos, flow):
    depth, nx, ny = pressure.shape
    tz = CHUNK_Z
    grid = (depth // tz,)
    main = pl.BlockSpec((tz, nx, ny), lambda c: (c, 0, 0))
    below = pl.BlockSpec((1, nx, ny), lambda c: (jnp.maximum(c * tz - 1, 0), 0, 0))
    above = pl.BlockSpec((1, nx, ny), lambda c: (jnp.minimum(c * tz + tz, depth - 1), 0, 0))
    row = pl.BlockSpec((tz, 1, ny), lambda c: (c, 0, 0))
    col = pl.BlockSpec((tz, nx, 1), lambda c: (c, 0, 0))
    side = [row, row, col, col]
    return pl.pallas_call(
        step_kernel,
        out_shape=jax.ShapeDtypeStruct((depth, nx, ny), jnp.float32),
        grid=grid,
        in_specs=[main, below, above] + side + [main, below, above] + side + [main],
        out_specs=main,
        compiler_params=pltpu.CompilerParams(dimension_semantics=("arbitrary",)),
    )(log_perm, log_perm, log_perm, *perm_halos, pressure, pressure, pressure, *pressure_halos, flow)


def body(noise, root_z, root_x, root_y, pressure_start, well_x, well_y, well_z, well_rate):
    depth, rows_x, rows_y = noise.shape
    first = jnp.dot(
        root_z, noise.reshape(depth, rows_x * rows_y), preferred_element_type=jnp.float32
    )
    first = first.reshape(depth, rows_x, rows_y).astype(jnp.bfloat16)
    second = jnp.einsum(
        "ia,zay->ziy",
        root_x,
        lax.all_to_all(first, "wide", split_axis=0, concat_axis=1, tiled=True),
        preferred_element_type=jnp.float32,
    ).astype(jnp.bfloat16)
    third = jnp.einsum(
        "zxb,jb->zxj",
        lax.all_to_all(second, "narrow", split_axis=1, concat_axis=2, tiled=True),
        root_y,
        preferred_element_type=jnp.float32,
    ).astype(jnp.bfloat16)
    homeward = lax.all_to_all(third, "narrow", split_axis=2, concat_axis=1, tiled=True)
    log_perm = lax.all_to_all(homeward, "wide", split_axis=1, concat_axis=0, tiled=True)

    wide_at = lax.axis_index("wide")
    narrow_at = lax.axis_index("narrow")
    last_w = lax.axis_size("wide") - 1
    last_n = lax.axis_size("narrow") - 1

    local_x = well_x - wide_at * rows_x
    local_y = well_y - narrow_at * rows_y
    valid = (local_x >= 0) & (local_x < rows_x) & (local_y >= 0) & (local_y < rows_y)
    rates = jnp.where(valid, well_rate, 0.0).astype(jnp.float32)
    wells = well_x.shape[0]
    cells = well_z * rows_x + local_x
    pick_rows = jnp.where(
        lax.broadcasted_iota(jnp.int32, (depth * rows_x, wells), 0) == cells[None, :],
        rates[None, :],
        0.0,
    )
    pick_cols = (
        lax.broadcasted_iota(jnp.int32, (wells, rows_y), 1) == local_y[:, None]
    ).astype(jnp.float32)
    flow = jnp.dot(
        pick_rows, pick_cols, precision=lax.Precision.HIGHEST, preferred_element_type=jnp.float32
    ).reshape(depth, rows_x, rows_y)

    x_lo, x_hi, y_lo, y_hi = halos(log_perm, jnp.bfloat16)
    f32 = jnp.float32
    perm_halos = (
        jnp.where(wide_at > 0, permeability(x_lo.astype(f32)), 0.0),
        jnp.where(wide_at < last_w, permeability(x_hi.astype(f32)), 0.0),
        jnp.where(narrow_at > 0, permeability(y_lo.astype(f32)), 0.0),
        jnp.where(narrow_at < last_n, permeability(y_hi.astype(f32)), 0.0),
    )

    pressure = pressure_start
    for step in range(STEPS):
        pressure_halos = halos(pressure, pressure.dtype)
        pressure = advance(log_perm, perm_halos, pressure, pressure_halos, flow)
    return (log_perm, pressure)


def solution(mesh):
    in_specs = (
        P("member", "wide", "narrow"),
        P(),
        P(),
        P(),
        P("member", "wide", "narrow"),
        P("member"),
        P("member"),
        P("member"),
        P("member"),
    )
    out_specs = (P("member", "wide", "narrow"), P("member", "wide", "narrow"))
    return jax.shard_map(body, mesh=mesh, in_specs=in_specs, out_specs=out_specs, check_vma=False)
```

```python
import jax
import jax.numpy as jnp
from jax import lax
from jax.experimental import pallas as pl
from jax.experimental.pallas import tpu as pltpu
from jax.sharding import PartitionSpec as P

STEPS = 2


STEP_SIZE = 0.03
CAP_LOG = 1.5
CHUNK_Z = 8


def permeability(values):
    return jnp.exp(CAP_LOG * jnp.tanh(values / CAP_LOG))


def harmonic(a, b):
    return 2.0 * a * b / (a + b)


def halos(block, dtype):
    forward_w = [(i, i + 1) for i in range(lax.axis_size("wide") - 1)]
    backward_w = [(j, i) for i, j in forward_w]
    forward_n = [(i, i + 1) for i in range(lax.axis_size("narrow") - 1)]
    backward_n = [(j, i) for i, j in forward_n]
    block = block.astype(dtype)
    x_lo = lax.ppermute(block[:, -1:, :], "wide", forward_w)
    x_hi = lax.ppermute(block[:, :1, :], "wide", backward_w)
    y_lo = lax.ppermute(block[:, :, -1:], "narrow", forward_n)
    y_hi = lax.ppermute(block[:, :, :1], "narrow", backward_n)
    return x_lo, x_hi, y_lo, y_hi


def step_kernel(
    lpm_ref, lpb_ref, lpa_ref, kxl_ref, kxh_ref, kyl_ref, kyh_ref,
    pm_ref, pb_ref, pa_ref, qxl_ref, qxh_ref, qyl_ref, qyh_ref, f_ref, o_ref,
):
    c = pl.program_id(0)
    last = pl.num_programs(0) - 1
    tz, nx, ny = pm_ref.shape
    f32 = jnp.float32

    below = jnp.where(c == 0, 0.0, permeability(lpb_ref[...].astype(f32)))
    above = jnp.where(c == last, 0.0, permeability(lpa_ref[...].astype(f32)))
    centre = permeability(lpm_ref[...].astype(f32))
    ext = jnp.concatenate([below, centre, above], axis=0)
    faces = harmonic(ext[:-1], ext[1:])
    t_zm = faces[:-1]
    t_zp = faces[1:]

    xi = lax.broadcasted_iota(jnp.int32, (tz, nx, ny), 1)
    yi = lax.broadcasted_iota(jnp.int32, (tz, nx, ny), 2)

    fx = harmonic(centre, pltpu.roll(centre, nx - 1, 1))
    t_xp = jnp.where(xi == nx - 1, harmonic(centre[:, nx - 1 :, :], kxh_ref[...]), fx)
    t_xm = jnp.where(xi == 0, harmonic(centre[:, :1, :], kxl_ref[...]), pltpu.roll(fx, 1, 1))
    fy = harmonic(centre, pltpu.roll(centre, ny - 1, 2))
    t_yp = jnp.where(yi == ny - 1, harmonic(centre[:, :, ny - 1 :], kyh_ref[...]), fy)
    t_ym = jnp.where(yi == 0, harmonic(centre[:, :, :1], kyl_ref[...]), pltpu.roll(fy, 1, 2))

    p = pm_ref[...].astype(f32)
    pext = jnp.concatenate([pb_ref[...].astype(f32), p, pa_ref[...].astype(f32)], axis=0)
    n_xp = jnp.where(xi == nx - 1, qxh_ref[...].astype(f32), pltpu.roll(p, nx - 1, 1))
    n_xm = jnp.where(xi == 0, qxl_ref[...].astype(f32), pltpu.roll(p, 1, 1))
    n_yp = jnp.where(yi == ny - 1, qyh_ref[...].astype(f32), pltpu.roll(p, ny - 1, 2))
    n_ym = jnp.where(yi == 0, qyl_ref[...].astype(f32), pltpu.roll(p, 1, 2))

    flux = t_zp * (pext[2:] - p)
    flux = flux + t_zm * (pext[:-2] - p)
    flux = flux + t_xp * (n_xp - p)
    flux = flux + t_xm * (n_xm - p)
    flux = flux + t_yp * (n_yp - p)
    flux = flux + t_ym * (n_ym - p)
    o_ref[...] = p + STEP_SIZE * (flux + f_ref[...]) / (1.0 + 0.5 * p * p)


def advance(log_perm, perm_halos, pressure, pressure_halos, flow):
    depth, nx, ny = pressure.shape
    tz = CHUNK_Z
    grid = (depth // tz,)
    main = pl.BlockSpec((tz, nx, ny), lambda c: (c, 0, 0))
    below = pl.BlockSpec((1, nx, ny), lambda c: (jnp.maximum(c * tz - 1, 0), 0, 0))
    above = pl.BlockSpec((1, nx, ny), lambda c: (jnp.minimum(c * tz + tz, depth - 1), 0, 0))
    row = pl.BlockSpec((tz, 1, ny), lambda c: (c, 0, 0))
    col = pl.BlockSpec((tz, nx, 1), lambda c: (c, 0, 0))
    side = [row, row, col, col]
    return pl.pallas_call(
        step_kernel,
        out_shape=jax.ShapeDtypeStruct((depth, nx, ny), jnp.float32),
        grid=grid,
        in_specs=[main, below, above] + side + [main, below, above] + side + [main],
        out_specs=main,
        compiler_params=pltpu.CompilerParams(dimension_semantics=("arbitrary",)),
    )(log_perm, log_perm, log_perm, *perm_halos, pressure, pressure, pressure, *pressure_halos, flow)


def body(noise, root_z, root_x, root_y, pressure_start, well_x, well_y, well_z, well_rate):
    depth, rows_x, rows_y = noise.shape
    first = jnp.dot(
        root_z, noise.reshape(depth, rows_x * rows_y), preferred_element_type=jnp.float32
    )
    first = first.reshape(depth, rows_x, rows_y).astype(jnp.bfloat16)
    count_w = lax.axis_size("wide")
    count_n = lax.axis_size("narrow")
    groups = count_w * count_n
    planes = depth // groups
    gathered = lax.all_to_all(
        first.reshape(groups, planes, rows_x, rows_y),
        ("wide", "narrow"), split_axis=0, concat_axis=0, tiled=True,
    ).reshape(count_w, count_n, planes, rows_x, rows_y)
    gathered = gathered.transpose(2, 0, 3, 1, 4).reshape(planes, count_w * rows_x, count_n * rows_y)
    second = jnp.einsum(
        "ia,zay->ziy", root_x, gathered, preferred_element_type=jnp.float32
    ).astype(jnp.bfloat16)
    third = jnp.einsum(
        "zxb,jb->zxj", second, root_y, preferred_element_type=jnp.float32
    ).astype(jnp.bfloat16)
    outgoing = third.reshape(planes, count_w, rows_x, count_n, rows_y).transpose(1, 3, 0, 2, 4)
    log_perm = lax.all_to_all(
        outgoing.reshape(groups, planes, rows_x, rows_y),
        ("wide", "narrow"), split_axis=0, concat_axis=0, tiled=True,
    ).reshape(depth, rows_x, rows_y)

    wide_at = lax.axis_index("wide")
    narrow_at = lax.axis_index("narrow")
    last_w = lax.axis_size("wide") - 1
    last_n = lax.axis_size("narrow") - 1

    local_x = well_x - wide_at * rows_x
    local_y = well_y - narrow_at * rows_y
    valid = (local_x >= 0) & (local_x < rows_x) & (local_y >= 0) & (local_y < rows_y)
    rates = jnp.where(valid, well_rate, 0.0).astype(jnp.float32)
    wells = well_x.shape[0]
    cells = well_z * rows_x + local_x
    pick_rows = jnp.where(
        lax.broadcasted_iota(jnp.int32, (depth * rows_x, wells), 0) == cells[None, :],
        rates[None, :],
        0.0,
    )
    pick_cols = (
        lax.broadcasted_iota(jnp.int32, (wells, rows_y), 1) == local_y[:, None]
    ).astype(jnp.float32)
    flow = jnp.dot(
        pick_rows, pick_cols, precision=lax.Precision.HIGHEST, preferred_element_type=jnp.float32
    ).reshape(depth, rows_x, rows_y)

    x_lo, x_hi, y_lo, y_hi = halos(log_perm, jnp.bfloat16)
    f32 = jnp.float32
    perm_halos = (
        jnp.where(wide_at > 0, permeability(x_lo.astype(f32)), 0.0),
        jnp.where(wide_at < last_w, permeability(x_hi.astype(f32)), 0.0),
        jnp.where(narrow_at > 0, permeability(y_lo.astype(f32)), 0.0),
        jnp.where(narrow_at < last_n, permeability(y_hi.astype(f32)), 0.0),
    )

    pressure = pressure_start
    for step in range(STEPS):
        pressure_halos = halos(pressure, pressure.dtype)
        pressure = advance(log_perm, perm_halos, pressure, pressure_halos, flow)
    return (log_perm, pressure)


def solution(mesh):
    in_specs = (
        P("member", "wide", "narrow"),
        P(),
        P(),
        P(),
        P("member", "wide", "narrow"),
        P("member"),
        P("member"),
        P("member"),
        P("member"),
    )
    out_specs = (P("member", "wide", "narrow"), P("member", "wide", "narrow"))
    return jax.shard_map(body, mesh=mesh, in_specs=in_specs, out_specs=out_specs, check_vma=False)
```

```python
import jax
import jax.numpy as jnp
from jax import lax
from jax.experimental import pallas as pl
from jax.experimental.pallas import tpu as pltpu
from jax.sharding import PartitionSpec as P

STEPS = 2


STEP_SIZE = 0.03
CAP_LOG = 1.5
CHUNK_Z = 8


def permeability(values):
    return jnp.exp(CAP_LOG * jnp.tanh(values / CAP_LOG))


def harmonic(a, b):
    return 2.0 * a * b / (a + b)


def block_edges(block):
    return block[:, :1, :], block[:, -1:, :], block[:, :, :1], block[:, :, -1:]


def halos(edges):
    forward_w = [(i, i + 1) for i in range(lax.axis_size("wide") - 1)]
    backward_w = [(j, i) for i, j in forward_w]
    forward_n = [(i, i + 1) for i in range(lax.axis_size("narrow") - 1)]
    backward_n = [(j, i) for i, j in forward_n]
    first_x, last_x, first_y, last_y = edges
    x_lo = lax.ppermute(last_x, "wide", forward_w)
    x_hi = lax.ppermute(first_x, "wide", backward_w)
    y_lo = lax.ppermute(last_y, "narrow", forward_n)
    y_hi = lax.ppermute(first_y, "narrow", backward_n)
    return x_lo, x_hi, y_lo, y_hi


def step_kernel(
    inside_ref, lpm_ref, lpb_ref, lpa_ref, lxl_ref, lxh_ref, lyl_ref, lyh_ref,
    pm_ref, pb_ref, pa_ref, qxl_ref, qxh_ref, qyl_ref, qyh_ref, f_ref,
    o_ref, exl_ref, exh_ref, eyl_ref, eyh_ref,
):
    c = pl.program_id(0)
    last = pl.num_programs(0) - 1
    tz, nx, ny = pm_ref.shape
    f32 = jnp.float32

    def side_perm(ref, k):
        return jnp.where(inside_ref[k] > 0, permeability(ref[...].astype(f32)), 0.0)

    kxl = side_perm(lxl_ref, 0)
    kxh = side_perm(lxh_ref, 1)
    kyl = side_perm(lyl_ref, 2)
    kyh = side_perm(lyh_ref, 3)

    below = jnp.where(c == 0, 0.0, permeability(lpb_ref[...].astype(f32)))
    above = jnp.where(c == last, 0.0, permeability(lpa_ref[...].astype(f32)))
    centre = permeability(lpm_ref[...].astype(f32))
    ext = jnp.concatenate([below, centre, above], axis=0)
    faces = harmonic(ext[:-1], ext[1:])
    t_zm = faces[:-1]
    t_zp = faces[1:]

    xi = lax.broadcasted_iota(jnp.int32, (tz, nx, ny), 1)
    yi = lax.broadcasted_iota(jnp.int32, (tz, nx, ny), 2)

    fx = harmonic(centre, pltpu.roll(centre, nx - 1, 1))
    t_xp = jnp.where(xi == nx - 1, harmonic(centre[:, nx - 1 :, :], kxh), fx)
    t_xm = jnp.where(xi == 0, harmonic(centre[:, :1, :], kxl), pltpu.roll(fx, 1, 1))
    fy = harmonic(centre, pltpu.roll(centre, ny - 1, 2))
    t_yp = jnp.where(yi == ny - 1, harmonic(centre[:, :, ny - 1 :], kyh), fy)
    t_ym = jnp.where(yi == 0, harmonic(centre[:, :, :1], kyl), pltpu.roll(fy, 1, 2))

    p = pm_ref[...].astype(f32)
    pext = jnp.concatenate([pb_ref[...].astype(f32), p, pa_ref[...].astype(f32)], axis=0)
    n_xp = jnp.where(xi == nx - 1, qxh_ref[...].astype(f32), pltpu.roll(p, nx - 1, 1))
    n_xm = jnp.where(xi == 0, qxl_ref[...].astype(f32), pltpu.roll(p, 1, 1))
    n_yp = jnp.where(yi == ny - 1, qyh_ref[...].astype(f32), pltpu.roll(p, ny - 1, 2))
    n_ym = jnp.where(yi == 0, qyl_ref[...].astype(f32), pltpu.roll(p, 1, 2))

    flux = t_zp * (pext[2:] - p)
    flux = flux + t_zm * (pext[:-2] - p)
    flux = flux + t_xp * (n_xp - p)
    flux = flux + t_xm * (n_xm - p)
    flux = flux + t_yp * (n_yp - p)
    flux = flux + t_ym * (n_ym - p)
    new = p + STEP_SIZE * (flux + f_ref[...]) / (1.0 + 0.5 * p * p)
    o_ref[...] = new
    exl_ref[...] = new[:, :1, :]
    exh_ref[...] = new[:, nx - 1 :, :]
    eyl_ref[...] = new[:, :, :1]
    eyh_ref[...] = new[:, :, ny - 1 :]


def advance(inside, log_perm, perm_halos, pressure, pressure_halos, flow):
    depth, nx, ny = pressure.shape
    tz = CHUNK_Z
    grid = (depth // tz,)
    main = pl.BlockSpec((tz, nx, ny), lambda c: (c, 0, 0))
    below = pl.BlockSpec((1, nx, ny), lambda c: (jnp.maximum(c * tz - 1, 0), 0, 0))
    above = pl.BlockSpec((1, nx, ny), lambda c: (jnp.minimum(c * tz + tz, depth - 1), 0, 0))
    row = pl.BlockSpec((tz, 1, ny), lambda c: (c, 0, 0))
    col = pl.BlockSpec((tz, nx, 1), lambda c: (c, 0, 0))
    side = [row, row, col, col]
    smem = pl.BlockSpec(memory_space=pltpu.SMEM)
    f32 = jnp.float32
    out_shape = (
        jax.ShapeDtypeStruct((depth, nx, ny), f32),
        jax.ShapeDtypeStruct((depth, 1, ny), f32),
        jax.ShapeDtypeStruct((depth, 1, ny), f32),
        jax.ShapeDtypeStruct((depth, nx, 1), f32),
        jax.ShapeDtypeStruct((depth, nx, 1), f32),
    )
    new, x_lo, x_hi, y_lo, y_hi = pl.pallas_call(
        step_kernel,
        out_shape=out_shape,
        grid=grid,
        in_specs=[smem, main, below, above] + side + [main, below, above] + side + [main],
        out_specs=[main] + side,
        compiler_params=pltpu.CompilerParams(dimension_semantics=("arbitrary",)),
    )(inside, log_perm, log_perm, log_perm, *perm_halos, pressure, pressure, pressure, *pressure_halos, flow)
    return new, (x_lo, x_hi, y_lo, y_hi)


def body(noise, root_z, root_x, root_y, pressure_start, well_x, well_y, well_z, well_rate):
    depth, rows_x, rows_y = noise.shape
    first = jnp.dot(
        root_z, noise.reshape(depth, rows_x * rows_y), preferred_element_type=jnp.float32
    )
    first = first.reshape(depth, rows_x, rows_y).astype(jnp.bfloat16)
    count_w = lax.axis_size("wide")
    count_n = lax.axis_size("narrow")
    groups = count_w * count_n
    planes = depth // groups
    gathered = lax.all_to_all(
        first.reshape(groups, planes, rows_x, rows_y),
        ("wide", "narrow"), split_axis=0, concat_axis=0, tiled=True,
    ).reshape(count_w, count_n, planes, rows_x, rows_y)
    gathered = gathered.transpose(2, 0, 3, 1, 4).reshape(planes, count_w * rows_x, count_n * rows_y)
    second = jnp.einsum(
        "ia,zay->ziy", root_x, gathered, preferred_element_type=jnp.float32
    ).astype(jnp.bfloat16)
    third = jnp.einsum(
        "zxb,jb->zxj", second, root_y, preferred_element_type=jnp.float32
    ).astype(jnp.bfloat16)
    outgoing = third.reshape(planes, count_w, rows_x, count_n, rows_y).transpose(1, 3, 0, 2, 4)
    log_perm = lax.all_to_all(
        outgoing.reshape(groups, planes, rows_x, rows_y),
        ("wide", "narrow"), split_axis=0, concat_axis=0, tiled=True,
    ).reshape(depth, rows_x, rows_y)

    wide_at = lax.axis_index("wide")
    narrow_at = lax.axis_index("narrow")
    last_w = lax.axis_size("wide") - 1
    last_n = lax.axis_size("narrow") - 1

    local_x = well_x - wide_at * rows_x
    local_y = well_y - narrow_at * rows_y
    valid = (local_x >= 0) & (local_x < rows_x) & (local_y >= 0) & (local_y < rows_y)
    rates = jnp.where(valid, well_rate, 0.0).astype(jnp.float32)
    wells = well_x.shape[0]
    cells = well_z * rows_x + local_x
    pick_rows = jnp.where(
        lax.broadcasted_iota(jnp.int32, (depth * rows_x, wells), 0) == cells[None, :],
        rates[None, :],
        0.0,
    )
    pick_cols = (
        lax.broadcasted_iota(jnp.int32, (wells, rows_y), 1) == local_y[:, None]
    ).astype(jnp.float32)
    flow = jnp.dot(
        pick_rows, pick_cols, precision=lax.Precision.HIGHEST, preferred_element_type=jnp.float32
    ).reshape(depth, rows_x, rows_y)

    inside = jnp.stack(
        [wide_at > 0, wide_at < last_w, narrow_at > 0, narrow_at < last_n]
    ).astype(jnp.int32)
    perm_halos = halos(block_edges(log_perm))
    pressure = pressure_start
    edges = block_edges(pressure_start)
    for step in range(STEPS):
        pressure, edges = advance(inside, log_perm, perm_halos, pressure, halos(edges), flow)
    return (log_perm, pressure)


def solution(mesh):
    in_specs = (
        P("member", "wide", "narrow"),
        P(),
        P(),
        P(),
        P("member", "wide", "narrow"),
        P("member"),
        P("member"),
        P("member"),
        P("member"),
    )
    out_specs = (P("member", "wide", "narrow"), P("member", "wide", "narrow"))
    return jax.shard_map(body, mesh=mesh, in_specs=in_specs, out_specs=out_specs, check_vma=False)
```

```python
import jax
import jax.numpy as jnp
from jax import lax
from jax.experimental import pallas as pl
from jax.experimental.pallas import tpu as pltpu
from jax.sharding import PartitionSpec as P

STEPS = 2


STEP_SIZE = 0.03
CAP_LOG = 1.5
CHUNK_Z = 8


def permeability(values):
    return jnp.exp(CAP_LOG * jnp.tanh(values / CAP_LOG))


def harmonic(a, b):
    return 2.0 * a * b / (a + b)


def block_edges(block):
    f32 = jnp.float32
    return block[:, :1, :], block[:, -1:, :], block[:, :, 0].astype(f32), block[:, :, -1].astype(f32)


def halos(edges):
    forward_w = [(i, i + 1) for i in range(lax.axis_size("wide") - 1)]
    backward_w = [(j, i) for i, j in forward_w]
    forward_n = [(i, i + 1) for i in range(lax.axis_size("narrow") - 1)]
    backward_n = [(j, i) for i, j in forward_n]
    first_x, last_x, first_y, last_y = edges
    x_lo = lax.ppermute(last_x, "wide", forward_w)
    x_hi = lax.ppermute(first_x, "wide", backward_w)
    y_lo = lax.ppermute(last_y, "narrow", forward_n)
    y_hi = lax.ppermute(first_y, "narrow", backward_n)
    return x_lo, x_hi, y_lo, y_hi


def to_columns(rows):
    tz, nx = rows.shape
    eye = lax.broadcasted_iota(jnp.int32, (nx, nx), 0) == lax.broadcasted_iota(jnp.int32, (nx, nx), 1)
    ones = jnp.ones((nx, 128), jnp.float32)
    cols = []
    for k in range(tz):
        diag = jnp.where(eye, jnp.broadcast_to(rows[k : k + 1, :], (nx, nx)), 0.0)
        full = jnp.dot(diag, ones, precision=lax.Precision.HIGHEST, preferred_element_type=jnp.float32)
        cols.append(full[:, :1][None])
    return jnp.concatenate(cols, axis=0)


def to_rows(block):
    tz, nx, ny = block.shape
    lane = lax.broadcasted_iota(jnp.int32, (8, ny), 1)
    pick = lax.broadcasted_iota(jnp.int32, (8, ny), 0)
    sel = jnp.where(((pick == 0) & (lane == 0)) | ((pick == 1) & (lane == ny - 1)), 1.0, 0.0)
    first, last = [], []
    for k in range(tz):
        both = lax.dot_general(
            sel, block[k], (((1,), (1,)), ((), ())),
            precision=lax.Precision.HIGHEST, preferred_element_type=jnp.float32,
        )
        first.append(both[0:1])
        last.append(both[1:2])
    return jnp.concatenate(first, axis=0), jnp.concatenate(last, axis=0)


def step_kernel(
    inside_ref, lpm_ref, lpb_ref, lpa_ref, lxl_ref, lxh_ref, lyl_ref, lyh_ref,
    pm_ref, pb_ref, pa_ref, qxl_ref, qxh_ref, qyl_ref, qyh_ref, f_ref,
    o_ref, exl_ref, exh_ref, eyl_ref, eyh_ref,
):
    c = pl.program_id(0)
    last = pl.num_programs(0) - 1
    tz, nx, ny = pm_ref.shape
    f32 = jnp.float32

    def side_perm(ref, k):
        return jnp.where(inside_ref[k] > 0, permeability(ref[...].astype(f32)), 0.0)

    kxl = side_perm(lxl_ref, 0)
    kxh = side_perm(lxh_ref, 1)
    kyl = to_columns(side_perm(lyl_ref, 2))
    kyh = to_columns(side_perm(lyh_ref, 3))

    below = jnp.where(c == 0, 0.0, permeability(lpb_ref[...].astype(f32)))
    above = jnp.where(c == last, 0.0, permeability(lpa_ref[...].astype(f32)))
    centre = permeability(lpm_ref[...].astype(f32))
    ext = jnp.concatenate([below, centre, above], axis=0)
    faces = harmonic(ext[:-1], ext[1:])
    t_zm = faces[:-1]
    t_zp = faces[1:]

    xi = lax.broadcasted_iota(jnp.int32, (tz, nx, ny), 1)
    yi = lax.broadcasted_iota(jnp.int32, (tz, nx, ny), 2)

    fx = harmonic(centre, pltpu.roll(centre, nx - 1, 1))
    t_xp = jnp.where(xi == nx - 1, harmonic(centre[:, nx - 1 :, :], kxh), fx)
    t_xm = jnp.where(xi == 0, harmonic(centre[:, :1, :], kxl), pltpu.roll(fx, 1, 1))
    fy = harmonic(centre, pltpu.roll(centre, ny - 1, 2))
    t_yp = jnp.where(yi == ny - 1, harmonic(centre[:, :, ny - 1 :], kyh), fy)
    t_ym = jnp.where(yi == 0, harmonic(centre[:, :, :1], kyl), pltpu.roll(fy, 1, 2))

    p = pm_ref[...].astype(f32)
    pext = jnp.concatenate([pb_ref[...].astype(f32), p, pa_ref[...].astype(f32)], axis=0)
    n_xp = jnp.where(xi == nx - 1, qxh_ref[...].astype(f32), pltpu.roll(p, nx - 1, 1))
    n_xm = jnp.where(xi == 0, qxl_ref[...].astype(f32), pltpu.roll(p, 1, 1))
    n_yp = jnp.where(yi == ny - 1, to_columns(qyh_ref[...]), pltpu.roll(p, ny - 1, 2))
    n_ym = jnp.where(yi == 0, to_columns(qyl_ref[...]), pltpu.roll(p, 1, 2))

    flux = t_zp * (pext[2:] - p)
    flux = flux + t_zm * (pext[:-2] - p)
    flux = flux + t_xp * (n_xp - p)
    flux = flux + t_xm * (n_xm - p)
    flux = flux + t_yp * (n_yp - p)
    flux = flux + t_ym * (n_ym - p)
    new = p + STEP_SIZE * (flux + f_ref[...]) / (1.0 + 0.5 * p * p)
    o_ref[...] = new
    exl_ref[...] = new[:, :1, :]
    exh_ref[...] = new[:, nx - 1 :, :]
    eyl_ref[...], eyh_ref[...] = to_rows(new)


def advance(inside, log_perm, perm_halos, pressure, pressure_halos, flow):
    depth, nx, ny = pressure.shape
    tz = CHUNK_Z
    grid = (depth // tz,)
    main = pl.BlockSpec((tz, nx, ny), lambda c: (c, 0, 0))
    below = pl.BlockSpec((1, nx, ny), lambda c: (jnp.maximum(c * tz - 1, 0), 0, 0))
    above = pl.BlockSpec((1, nx, ny), lambda c: (jnp.minimum(c * tz + tz, depth - 1), 0, 0))
    row = pl.BlockSpec((tz, 1, ny), lambda c: (c, 0, 0))
    col = pl.BlockSpec((tz, nx), lambda c: (c, 0))
    side = [row, row, col, col]
    smem = pl.BlockSpec(memory_space=pltpu.SMEM)
    f32 = jnp.float32
    out_shape = (
        jax.ShapeDtypeStruct((depth, nx, ny), f32),
        jax.ShapeDtypeStruct((depth, 1, ny), f32),
        jax.ShapeDtypeStruct((depth, 1, ny), f32),
        jax.ShapeDtypeStruct((depth, nx), f32),
        jax.ShapeDtypeStruct((depth, nx), f32),
    )
    new, x_lo, x_hi, y_lo, y_hi = pl.pallas_call(
        step_kernel,
        out_shape=out_shape,
        grid=grid,
        in_specs=[smem, main, below, above] + side + [main, below, above] + side + [main],
        out_specs=[main] + side,
        compiler_params=pltpu.CompilerParams(dimension_semantics=("arbitrary",)),
    )(inside, log_perm, log_perm, log_perm, *perm_halos, pressure, pressure, pressure, *pressure_halos, flow)
    return new, (x_lo, x_hi, y_lo, y_hi)


def body(noise, root_z, root_x, root_y, pressure_start, well_x, well_y, well_z, well_rate):
    depth, rows_x, rows_y = noise.shape
    first = jnp.dot(
        root_z, noise.reshape(depth, rows_x * rows_y), preferred_element_type=jnp.float32
    )
    first = first.reshape(depth, rows_x, rows_y).astype(jnp.bfloat16)
    count_w = lax.axis_size("wide")
    count_n = lax.axis_size("narrow")
    groups = count_w * count_n
    planes = depth // groups
    gathered = lax.all_to_all(
        first.reshape(groups, planes, rows_x, rows_y),
        ("wide", "narrow"), split_axis=0, concat_axis=0, tiled=True,
    ).reshape(count_w, count_n, planes, rows_x, rows_y)
    gathered = gathered.transpose(2, 0, 3, 1, 4).reshape(planes, count_w * rows_x, count_n * rows_y)
    second = jnp.einsum(
        "ia,zay->ziy", root_x, gathered, preferred_element_type=jnp.float32
    ).astype(jnp.bfloat16)
    third = jnp.einsum(
        "zxb,jb->zxj", second, root_y, preferred_element_type=jnp.float32
    ).astype(jnp.bfloat16)
    outgoing = third.reshape(planes, count_w, rows_x, count_n, rows_y).transpose(1, 3, 0, 2, 4)
    log_perm = lax.all_to_all(
        outgoing.reshape(groups, planes, rows_x, rows_y),
        ("wide", "narrow"), split_axis=0, concat_axis=0, tiled=True,
    ).reshape(depth, rows_x, rows_y)

    wide_at = lax.axis_index("wide")
    narrow_at = lax.axis_index("narrow")
    last_w = lax.axis_size("wide") - 1
    last_n = lax.axis_size("narrow") - 1

    local_x = well_x - wide_at * rows_x
    local_y = well_y - narrow_at * rows_y
    valid = (local_x >= 0) & (local_x < rows_x) & (local_y >= 0) & (local_y < rows_y)
    rates = jnp.where(valid, well_rate, 0.0).astype(jnp.float32)
    wells = well_x.shape[0]
    cells = well_z * rows_x + local_x
    pick_rows = jnp.where(
        lax.broadcasted_iota(jnp.int32, (depth * rows_x, wells), 0) == cells[None, :],
        rates[None, :],
        0.0,
    )
    pick_cols = (
        lax.broadcasted_iota(jnp.int32, (wells, rows_y), 1) == local_y[:, None]
    ).astype(jnp.float32)
    flow = jnp.dot(
        pick_rows, pick_cols, precision=lax.Precision.HIGHEST, preferred_element_type=jnp.float32
    ).reshape(depth, rows_x, rows_y)

    inside = jnp.stack(
        [wide_at > 0, wide_at < last_w, narrow_at > 0, narrow_at < last_n]
    ).astype(jnp.int32)
    perm_halos = halos(block_edges(log_perm))
    pressure = pressure_start
    edges = block_edges(pressure_start)
    for step in range(STEPS):
        pressure, edges = advance(inside, log_perm, perm_halos, pressure, halos(edges), flow)
    return (log_perm, pressure)


def solution(mesh):
    in_specs = (
        P("member", "wide", "narrow"),
        P(),
        P(),
        P(),
        P("member", "wide", "narrow"),
        P("member"),
        P("member"),
        P("member"),
        P("member"),
    )
    out_specs = (P("member", "wide", "narrow"), P("member", "wide", "narrow"))
    return jax.shard_map(body, mesh=mesh, in_specs=in_specs, out_specs=out_specs, check_vma=False)
```

```python
import jax
import jax.numpy as jnp
from jax import lax
from jax.experimental import pallas as pl
from jax.experimental.pallas import tpu as pltpu
from jax.sharding import PartitionSpec as P

STEPS = 2


STEP_SIZE = 0.03
CAP_LOG = 1.5
CHUNK_Z = 8


def permeability(values):
    return jnp.exp(CAP_LOG * jnp.tanh(values / CAP_LOG))


def harmonic(a, b):
    return 2.0 * a * b / (a + b)


def halos(edges):
    forward_w = [(i, i + 1) for i in range(lax.axis_size("wide") - 1)]
    backward_w = [(j, i) for i, j in forward_w]
    forward_n = [(i, i + 1) for i in range(lax.axis_size("narrow") - 1)]
    backward_n = [(j, i) for i, j in forward_n]
    first_x, last_x, first_y, last_y = edges
    x_lo = lax.ppermute(last_x, "wide", forward_w)
    x_hi = lax.ppermute(first_x, "wide", backward_w)
    y_lo = lax.ppermute(last_y, "narrow", forward_n)
    y_hi = lax.ppermute(first_y, "narrow", backward_n)
    return x_lo, x_hi, y_lo, y_hi


def to_columns(rows):
    tz, nx = rows.shape
    eye = jnp.where(
        lax.broadcasted_iota(jnp.int32, (nx, nx), 0) == lax.broadcasted_iota(jnp.int32, (nx, nx), 1),
        1.0, 0.0,
    )
    cols = lax.dot_general(
        eye, rows, (((1,), (1,)), ((), ())),
        precision=lax.Precision.HIGHEST, preferred_element_type=jnp.float32,
    )
    return jnp.concatenate([cols[:, k : k + 1][None] for k in range(tz)], axis=0)


def x_rows(ref):
    return jnp.concatenate([ref[k : k + 1, :][None] for k in range(ref.shape[0])], axis=0)


def store_x_rows(ref, rows):
    for k in range(ref.shape[0]):
        ref[k : k + 1, :] = rows[k]


def to_rows(block):
    tz, nx, ny = block.shape
    lane = lax.broadcasted_iota(jnp.int32, (nx, 128), 1)
    pick = jnp.where(
        lax.broadcasted_iota(jnp.int32, (tz, 128), 0) == lax.broadcasted_iota(jnp.int32, (tz, 128), 1),
        1.0, 0.0,
    )
    result = []
    for column in (0, ny - 1):
        gathered = jnp.zeros((nx, 128), jnp.float32)
        for k in range(tz):
            gathered = jnp.where(lane == k, block[k, :, column : column + 1], gathered)
        result.append(
            lax.dot_general(
                pick, gathered, (((1,), (1,)), ((), ())),
                precision=lax.Precision.HIGHEST, preferred_element_type=jnp.float32,
            )
        )
    return result[0], result[1]


def edge_kernel(block_ref, xl_ref, xh_ref, yl_ref, yh_ref):
    block = block_ref[...].astype(jnp.float32)
    store_x_rows(xl_ref, block[:, :1, :])
    store_x_rows(xh_ref, block[:, -1:, :])
    yl_ref[...], yh_ref[...] = to_rows(block)


def block_edges(block):
    depth, nx, ny = block.shape
    tz = CHUNK_Z
    f32 = jnp.float32
    row = pl.BlockSpec((tz, ny), lambda c: (c, 0))
    col = pl.BlockSpec((tz, nx), lambda c: (c, 0))
    return pl.pallas_call(
        edge_kernel,
        out_shape=(
            jax.ShapeDtypeStruct((depth, ny), f32),
            jax.ShapeDtypeStruct((depth, ny), f32),
            jax.ShapeDtypeStruct((depth, nx), f32),
            jax.ShapeDtypeStruct((depth, nx), f32),
        ),
        grid=(depth // tz,),
        in_specs=[pl.BlockSpec((tz, nx, ny), lambda c: (c, 0, 0))],
        out_specs=[row, row, col, col],
        compiler_params=pltpu.CompilerParams(dimension_semantics=("arbitrary",)),
    )(block)


def step_kernel(
    inside_ref, lpm_ref, lpb_ref, lpa_ref, lxl_ref, lxh_ref, lyl_ref, lyh_ref,
    pm_ref, pb_ref, pa_ref, qxl_ref, qxh_ref, qyl_ref, qyh_ref, f_ref,
    o_ref, exl_ref, exh_ref, eyl_ref, eyh_ref,
):
    c = pl.program_id(0)
    last = pl.num_programs(0) - 1
    tz, nx, ny = pm_ref.shape
    f32 = jnp.float32

    def side_perm(ref, k):
        return jnp.where(inside_ref[k] > 0, permeability(ref[...].astype(f32)), 0.0)

    kxl = jnp.where(inside_ref[0] > 0, permeability(x_rows(lxl_ref)), 0.0)
    kxh = jnp.where(inside_ref[1] > 0, permeability(x_rows(lxh_ref)), 0.0)
    kyl = to_columns(side_perm(lyl_ref, 2))
    kyh = to_columns(side_perm(lyh_ref, 3))

    below = jnp.where(c == 0, 0.0, permeability(lpb_ref[...].astype(f32)))
    above = jnp.where(c == last, 0.0, permeability(lpa_ref[...].astype(f32)))
    centre = permeability(lpm_ref[...].astype(f32))
    ext = jnp.concatenate([below, centre, above], axis=0)
    faces = harmonic(ext[:-1], ext[1:])
    t_zm = faces[:-1]
    t_zp = faces[1:]

    xi = lax.broadcasted_iota(jnp.int32, (tz, nx, ny), 1)
    yi = lax.broadcasted_iota(jnp.int32, (tz, nx, ny), 2)

    fx = harmonic(centre, pltpu.roll(centre, nx - 1, 1))
    t_xp = jnp.where(xi == nx - 1, harmonic(centre[:, nx - 1 :, :], kxh), fx)
    t_xm = jnp.where(xi == 0, harmonic(centre[:, :1, :], kxl), pltpu.roll(fx, 1, 1))
    fy = harmonic(centre, pltpu.roll(centre, ny - 1, 2))
    t_yp = jnp.where(yi == ny - 1, harmonic(centre[:, :, ny - 1 :], kyh), fy)
    t_ym = jnp.where(yi == 0, harmonic(centre[:, :, :1], kyl), pltpu.roll(fy, 1, 2))

    p = pm_ref[...].astype(f32)
    pext = jnp.concatenate([pb_ref[...].astype(f32), p, pa_ref[...].astype(f32)], axis=0)
    n_xp = jnp.where(xi == nx - 1, x_rows(qxh_ref), pltpu.roll(p, nx - 1, 1))
    n_xm = jnp.where(xi == 0, x_rows(qxl_ref), pltpu.roll(p, 1, 1))
    n_yp = jnp.where(yi == ny - 1, to_columns(qyh_ref[...]), pltpu.roll(p, ny - 1, 2))
    n_ym = jnp.where(yi == 0, to_columns(qyl_ref[...]), pltpu.roll(p, 1, 2))

    flux = t_zp * (pext[2:] - p)
    flux = flux + t_zm * (pext[:-2] - p)
    flux = flux + t_xp * (n_xp - p)
    flux = flux + t_xm * (n_xm - p)
    flux = flux + t_yp * (n_yp - p)
    flux = flux + t_ym * (n_ym - p)
    new = p + STEP_SIZE * (flux + f_ref[...]) / (1.0 + 0.5 * p * p)
    o_ref[...] = new
    store_x_rows(exl_ref, new[:, :1, :])
    store_x_rows(exh_ref, new[:, nx - 1 :, :])
    eyl_ref[...], eyh_ref[...] = to_rows(new)


def advance(inside, log_perm, perm_halos, pressure, pressure_halos, flow):
    depth, nx, ny = pressure.shape
    tz = CHUNK_Z
    grid = (depth // tz,)
    main = pl.BlockSpec((tz, nx, ny), lambda c: (c, 0, 0))
    below = pl.BlockSpec((1, nx, ny), lambda c: (jnp.maximum(c * tz - 1, 0), 0, 0))
    above = pl.BlockSpec((1, nx, ny), lambda c: (jnp.minimum(c * tz + tz, depth - 1), 0, 0))
    row = pl.BlockSpec((tz, ny), lambda c: (c, 0))
    col = pl.BlockSpec((tz, nx), lambda c: (c, 0))
    side = [row, row, col, col]
    smem = pl.BlockSpec(memory_space=pltpu.SMEM)
    f32 = jnp.float32
    out_shape = (
        jax.ShapeDtypeStruct((depth, nx, ny), f32),
        jax.ShapeDtypeStruct((depth, ny), f32),
        jax.ShapeDtypeStruct((depth, ny), f32),
        jax.ShapeDtypeStruct((depth, nx), f32),
        jax.ShapeDtypeStruct((depth, nx), f32),
    )
    new, x_lo, x_hi, y_lo, y_hi = pl.pallas_call(
        step_kernel,
        out_shape=out_shape,
        grid=grid,
        in_specs=[smem, main, below, above] + side + [main, below, above] + side + [main],
        out_specs=[main] + side,
        compiler_params=pltpu.CompilerParams(dimension_semantics=("arbitrary",)),
    )(inside, log_perm, log_perm, log_perm, *perm_halos, pressure, pressure, pressure, *pressure_halos, flow)
    return new, (x_lo, x_hi, y_lo, y_hi)


def body(noise, root_z, root_x, root_y, pressure_start, well_x, well_y, well_z, well_rate):
    depth, rows_x, rows_y = noise.shape
    first = jnp.dot(
        root_z, noise.reshape(depth, rows_x * rows_y), preferred_element_type=jnp.float32
    )
    first = first.reshape(depth, rows_x, rows_y).astype(jnp.bfloat16)
    count_w = lax.axis_size("wide")
    count_n = lax.axis_size("narrow")
    groups = count_w * count_n
    planes = depth // groups
    gathered = lax.all_to_all(
        first.reshape(groups, planes, rows_x, rows_y),
        ("wide", "narrow"), split_axis=0, concat_axis=0, tiled=True,
    ).reshape(count_w, count_n, planes, rows_x, rows_y)
    gathered = gathered.transpose(2, 0, 3, 1, 4).reshape(planes, count_w * rows_x, count_n * rows_y)
    second = jnp.einsum(
        "ia,zay->ziy", root_x, gathered, preferred_element_type=jnp.float32
    ).astype(jnp.bfloat16)
    third = jnp.einsum(
        "zxb,jb->zxj", second, root_y, preferred_element_type=jnp.float32
    ).astype(jnp.bfloat16)
    outgoing = third.reshape(planes, count_w, rows_x, count_n, rows_y).transpose(1, 3, 0, 2, 4)
    log_perm = lax.all_to_all(
        outgoing.reshape(groups, planes, rows_x, rows_y),
        ("wide", "narrow"), split_axis=0, concat_axis=0, tiled=True,
    ).reshape(depth, rows_x, rows_y)

    wide_at = lax.axis_index("wide")
    narrow_at = lax.axis_index("narrow")
    last_w = lax.axis_size("wide") - 1
    last_n = lax.axis_size("narrow") - 1

    local_x = well_x - wide_at * rows_x
    local_y = well_y - narrow_at * rows_y
    valid = (local_x >= 0) & (local_x < rows_x) & (local_y >= 0) & (local_y < rows_y)
    rates = jnp.where(valid, well_rate, 0.0).astype(jnp.float32)
    wells = well_x.shape[0]
    cells = well_z * rows_x + local_x
    pick_rows = jnp.where(
        lax.broadcasted_iota(jnp.int32, (depth * rows_x, wells), 0) == cells[None, :],
        rates[None, :],
        0.0,
    )
    pick_cols = (
        lax.broadcasted_iota(jnp.int32, (wells, rows_y), 1) == local_y[:, None]
    ).astype(jnp.float32)
    flow = jnp.dot(
        pick_rows, pick_cols, precision=lax.Precision.HIGHEST, preferred_element_type=jnp.float32
    ).reshape(depth, rows_x, rows_y)

    inside = jnp.stack(
        [wide_at > 0, wide_at < last_w, narrow_at > 0, narrow_at < last_n]
    ).astype(jnp.int32)
    perm_halos = halos(block_edges(log_perm))
    pressure = pressure_start
    edges = block_edges(pressure_start)
    for step in range(STEPS):
        pressure, edges = advance(inside, log_perm, perm_halos, pressure, halos(edges), flow)
    return (log_perm, pressure)


def solution(mesh):
    in_specs = (
        P("member", "wide", "narrow"),
        P(),
        P(),
        P(),
        P("member", "wide", "narrow"),
        P("member"),
        P("member"),
        P("member"),
        P("member"),
    )
    out_specs = (P("member", "wide", "narrow"), P("member", "wide", "narrow"))
    return jax.shard_map(body, mesh=mesh, in_specs=in_specs, out_specs=out_specs, check_vma=False)
```

```python
import functools

import jax
import jax.numpy as jnp
from jax import lax
from jax.experimental import pallas as pl
from jax.experimental.pallas import tpu as pltpu
from jax.sharding import PartitionSpec as P

STEPS = 2


STEP_SIZE = 0.03
CAP_LOG = 1.5
CHUNK_Z = 8


def permeability(values):
    return jnp.exp(CAP_LOG * jnp.tanh(values / CAP_LOG))


def harmonic(a, b):
    return 2.0 * a * b / (a + b)


def halos(edges):
    forward_w = [(i, i + 1) for i in range(lax.axis_size("wide") - 1)]
    backward_w = [(j, i) for i, j in forward_w]
    forward_n = [(i, i + 1) for i in range(lax.axis_size("narrow") - 1)]
    backward_n = [(j, i) for i, j in forward_n]
    first_x, last_x, first_y, last_y = edges
    x_lo = lax.ppermute(last_x, "wide", forward_w)
    x_hi = lax.ppermute(first_x, "wide", backward_w)
    y_lo = lax.ppermute(last_y, "narrow", forward_n)
    y_hi = lax.ppermute(first_y, "narrow", backward_n)
    return x_lo, x_hi, y_lo, y_hi


def to_columns(rows):
    tz, nx = rows.shape
    eye = jnp.where(
        lax.broadcasted_iota(jnp.int32, (nx, nx), 0) == lax.broadcasted_iota(jnp.int32, (nx, nx), 1),
        1.0, 0.0,
    )
    cols = lax.dot_general(
        eye, rows, (((1,), (1,)), ((), ())),
        precision=lax.Precision.HIGHEST, preferred_element_type=jnp.float32,
    )
    return jnp.concatenate([cols[:, k : k + 1][None] for k in range(tz)], axis=0)


def x_rows(ref):
    return jnp.concatenate([ref[k : k + 1, :][None] for k in range(ref.shape[0])], axis=0)


def store_x_rows(ref, rows):
    for k in range(ref.shape[0]):
        ref[k : k + 1, :] = rows[k]


def to_rows(block):
    tz, nx, ny = block.shape
    lane = lax.broadcasted_iota(jnp.int32, (nx, 128), 1)
    pick = jnp.where(
        lax.broadcasted_iota(jnp.int32, (tz, 128), 0) == lax.broadcasted_iota(jnp.int32, (tz, 128), 1),
        1.0, 0.0,
    )
    result = []
    for column in (0, ny - 1):
        gathered = jnp.zeros((nx, 128), jnp.float32)
        for k in range(tz):
            gathered = jnp.where(lane == k, block[k, :, column : column + 1], gathered)
        result.append(
            lax.dot_general(
                pick, gathered, (((1,), (1,)), ((), ())),
                precision=lax.Precision.HIGHEST, preferred_element_type=jnp.float32,
            )
        )
    return result[0], result[1]


def edge_kernel(block_ref, xl_ref, xh_ref, yl_ref, yh_ref):
    block = block_ref[...].astype(jnp.float32)
    store_x_rows(xl_ref, block[:, :1, :])
    store_x_rows(xh_ref, block[:, -1:, :])
    yl_ref[...], yh_ref[...] = to_rows(block)


def block_edges(block):
    depth, nx, ny = block.shape
    tz = CHUNK_Z
    f32 = jnp.float32
    row = pl.BlockSpec((tz, ny), lambda c: (c, 0))
    col = pl.BlockSpec((tz, nx), lambda c: (c, 0))
    return pl.pallas_call(
        edge_kernel,
        out_shape=(
            jax.ShapeDtypeStruct((depth, ny), f32),
            jax.ShapeDtypeStruct((depth, ny), f32),
            jax.ShapeDtypeStruct((depth, nx), f32),
            jax.ShapeDtypeStruct((depth, nx), f32),
        ),
        grid=(depth // tz,),
        in_specs=[pl.BlockSpec((tz, nx, ny), lambda c: (c, 0, 0))],
        out_specs=[row, row, col, col],
        compiler_params=pltpu.CompilerParams(dimension_semantics=("arbitrary",)),
    )(block)


def step_kernel(
    inside_ref, lpm_ref, lpb_ref, lpa_ref, lxl_ref, lxh_ref, lyl_ref, lyh_ref,
    pm_ref, pb_ref, pa_ref, qxl_ref, qxh_ref, qyl_ref, qyh_ref, f_ref,
    o_ref, exl_ref, exh_ref, eyl_ref, eyh_ref,
):
    c = pl.program_id(0)
    last = pl.num_programs(0) - 1
    tz, nx, ny = pm_ref.shape
    f32 = jnp.float32

    def side_perm(ref, k):
        return jnp.where(inside_ref[k] > 0, permeability(ref[...].astype(f32)), 0.0)

    kxl = jnp.where(inside_ref[0] > 0, permeability(x_rows(lxl_ref)), 0.0)
    kxh = jnp.where(inside_ref[1] > 0, permeability(x_rows(lxh_ref)), 0.0)
    kyl = to_columns(side_perm(lyl_ref, 2))
    kyh = to_columns(side_perm(lyh_ref, 3))

    below = jnp.where(c == 0, 0.0, permeability(lpb_ref[...].astype(f32)))
    above = jnp.where(c == last, 0.0, permeability(lpa_ref[...].astype(f32)))
    centre = permeability(lpm_ref[...].astype(f32))
    ext = jnp.concatenate([below, centre, above], axis=0)
    faces = harmonic(ext[:-1], ext[1:])
    t_zm = faces[:-1]
    t_zp = faces[1:]

    xi = lax.broadcasted_iota(jnp.int32, (tz, nx, ny), 1)
    yi = lax.broadcasted_iota(jnp.int32, (tz, nx, ny), 2)

    fx = harmonic(centre, pltpu.roll(centre, nx - 1, 1))
    t_xp = jnp.where(xi == nx - 1, harmonic(centre[:, nx - 1 :, :], kxh), fx)
    t_xm = jnp.where(xi == 0, harmonic(centre[:, :1, :], kxl), pltpu.roll(fx, 1, 1))
    fy = harmonic(centre, pltpu.roll(centre, ny - 1, 2))
    t_yp = jnp.where(yi == ny - 1, harmonic(centre[:, :, ny - 1 :], kyh), fy)
    t_ym = jnp.where(yi == 0, harmonic(centre[:, :, :1], kyl), pltpu.roll(fy, 1, 2))

    p = pm_ref[...].astype(f32)
    pext = jnp.concatenate([pb_ref[...].astype(f32), p, pa_ref[...].astype(f32)], axis=0)
    n_xp = jnp.where(xi == nx - 1, x_rows(qxh_ref), pltpu.roll(p, nx - 1, 1))
    n_xm = jnp.where(xi == 0, x_rows(qxl_ref), pltpu.roll(p, 1, 1))
    n_yp = jnp.where(yi == ny - 1, to_columns(qyh_ref[...]), pltpu.roll(p, ny - 1, 2))
    n_ym = jnp.where(yi == 0, to_columns(qyl_ref[...]), pltpu.roll(p, 1, 2))

    flux = t_zp * (pext[2:] - p)
    flux = flux + t_zm * (pext[:-2] - p)
    flux = flux + t_xp * (n_xp - p)
    flux = flux + t_xm * (n_xm - p)
    flux = flux + t_yp * (n_yp - p)
    flux = flux + t_ym * (n_ym - p)
    new = p + STEP_SIZE * (flux + f_ref[...]) / (1.0 + 0.5 * p * p)
    o_ref[...] = new
    store_x_rows(exl_ref, new[:, :1, :])
    store_x_rows(exh_ref, new[:, nx - 1 :, :])
    eyl_ref[...], eyh_ref[...] = to_rows(new)


def advance(inside, log_perm, perm_halos, pressure, pressure_halos, flow):
    depth, nx, ny = pressure.shape
    tz = CHUNK_Z
    grid = (depth // tz,)
    main = pl.BlockSpec((tz, nx, ny), lambda c: (c, 0, 0))
    below = pl.BlockSpec((1, nx, ny), lambda c: (jnp.maximum(c * tz - 1, 0), 0, 0))
    above = pl.BlockSpec((1, nx, ny), lambda c: (jnp.minimum(c * tz + tz, depth - 1), 0, 0))
    row = pl.BlockSpec((tz, ny), lambda c: (c, 0))
    col = pl.BlockSpec((tz, nx), lambda c: (c, 0))
    side = [row, row, col, col]
    smem = pl.BlockSpec(memory_space=pltpu.SMEM)
    f32 = jnp.float32
    out_shape = (
        jax.ShapeDtypeStruct((depth, nx, ny), f32),
        jax.ShapeDtypeStruct((depth, ny), f32),
        jax.ShapeDtypeStruct((depth, ny), f32),
        jax.ShapeDtypeStruct((depth, nx), f32),
        jax.ShapeDtypeStruct((depth, nx), f32),
    )
    new, x_lo, x_hi, y_lo, y_hi = pl.pallas_call(
        step_kernel,
        out_shape=out_shape,
        grid=grid,
        in_specs=[smem, main, below, above] + side + [main, below, above] + side + [main],
        out_specs=[main] + side,
        compiler_params=pltpu.CompilerParams(dimension_semantics=("arbitrary",)),
    )(inside, log_perm, log_perm, log_perm, *perm_halos, pressure, pressure, pressure, *pressure_halos, flow)
    return new, (x_lo, x_hi, y_lo, y_hi)


def line_kernel(g_ref, rx_ref, ry_ref, o_ref, *, count_w, count_n):
    f32 = jnp.float32
    nx = g_ref.shape[2]
    ny = g_ref.shape[3]
    rx = rx_ref[...]
    halves = []
    for n in range(count_n):
        lines = jnp.concatenate([g_ref[w * count_n + n, 0] for w in range(count_w)], axis=0)
        halves.append(jnp.dot(rx, lines, preferred_element_type=f32).astype(jnp.bfloat16))
    second = jnp.concatenate(halves, axis=1)
    third = lax.dot_general(
        second, ry_ref[...], (((1,), (1,)), ((), ())), preferred_element_type=f32
    ).astype(jnp.bfloat16)
    for w in range(count_w):
        for n in range(count_n):
            o_ref[w * count_n + n, 0] = third[w * nx : (w + 1) * nx, n * ny : (n + 1) * ny]


def line_transforms(gathered, root_x, root_y, count_w, count_n):
    groups, planes, nx, ny = gathered.shape
    block = pl.BlockSpec((groups, 1, nx, ny), lambda z: (0, z, 0, 0))
    whole_x = pl.BlockSpec(root_x.shape, lambda z: (0, 0))
    whole_y = pl.BlockSpec(root_y.shape, lambda z: (0, 0))
    return pl.pallas_call(
        functools.partial(line_kernel, count_w=count_w, count_n=count_n),
        out_shape=jax.ShapeDtypeStruct(gathered.shape, jnp.bfloat16),
        grid=(planes,),
        in_specs=[block, whole_x, whole_y],
        out_specs=block,
        compiler_params=pltpu.CompilerParams(dimension_semantics=("arbitrary",)),
    )(gathered, root_x, root_y)


def body(noise, root_z, root_x, root_y, pressure_start, well_x, well_y, well_z, well_rate):
    depth, rows_x, rows_y = noise.shape
    first = jnp.dot(
        root_z, noise.reshape(depth, rows_x * rows_y), preferred_element_type=jnp.float32
    )
    first = first.reshape(depth, rows_x, rows_y).astype(jnp.bfloat16)
    count_w = lax.axis_size("wide")
    count_n = lax.axis_size("narrow")
    groups = count_w * count_n
    planes = depth // groups
    gathered = lax.all_to_all(
        first.reshape(groups, planes, rows_x, rows_y),
        ("wide", "narrow"), split_axis=0, concat_axis=0, tiled=True,
    )
    outgoing = line_transforms(gathered, root_x, root_y, count_w, count_n)
    log_perm = lax.all_to_all(
        outgoing, ("wide", "narrow"), split_axis=0, concat_axis=0, tiled=True,
    ).reshape(depth, rows_x, rows_y)

    wide_at = lax.axis_index("wide")
    narrow_at = lax.axis_index("narrow")
    last_w = lax.axis_size("wide") - 1
    last_n = lax.axis_size("narrow") - 1

    local_x = well_x - wide_at * rows_x
    local_y = well_y - narrow_at * rows_y
    valid = (local_x >= 0) & (local_x < rows_x) & (local_y >= 0) & (local_y < rows_y)
    rates = jnp.where(valid, well_rate, 0.0).astype(jnp.float32)
    wells = well_x.shape[0]
    cells = well_z * rows_x + local_x
    pick_rows = jnp.where(
        lax.broadcasted_iota(jnp.int32, (depth * rows_x, wells), 0) == cells[None, :],
        rates[None, :],
        0.0,
    )
    pick_cols = (
        lax.broadcasted_iota(jnp.int32, (wells, rows_y), 1) == local_y[:, None]
    ).astype(jnp.float32)
    flow = jnp.dot(
        pick_rows, pick_cols, precision=lax.Precision.HIGHEST, preferred_element_type=jnp.float32
    ).reshape(depth, rows_x, rows_y)

    inside = jnp.stack(
        [wide_at > 0, wide_at < last_w, narrow_at > 0, narrow_at < last_n]
    ).astype(jnp.int32)
    perm_halos = halos(block_edges(log_perm))
    pressure = pressure_start
    edges = block_edges(pressure_start)
    for step in range(STEPS):
        pressure, edges = advance(inside, log_perm, perm_halos, pressure, halos(edges), flow)
    return (log_perm, pressure)


def solution(mesh):
    in_specs = (
        P("member", "wide", "narrow"),
        P(),
        P(),
        P(),
        P("member", "wide", "narrow"),
        P("member"),
        P("member"),
        P("member"),
        P("member"),
    )
    out_specs = (P("member", "wide", "narrow"), P("member", "wide", "narrow"))
    return jax.shard_map(body, mesh=mesh, in_specs=in_specs, out_specs=out_specs, check_vma=False)
```

```python
import functools

import jax
import jax.numpy as jnp
from jax import lax
from jax.experimental import pallas as pl
from jax.experimental.pallas import tpu as pltpu
from jax.sharding import PartitionSpec as P

STEPS = 2


STEP_SIZE = 0.03
CAP_LOG = 1.5
CHUNK_Z = 8


def permeability(values):
    return jnp.exp(CAP_LOG * jnp.tanh(values / CAP_LOG))


def harmonic(a, b):
    return 2.0 * a * b / (a + b)


def halos(edges):
    forward_w = [(i, i + 1) for i in range(lax.axis_size("wide") - 1)]
    backward_w = [(j, i) for i, j in forward_w]
    forward_n = [(i, i + 1) for i in range(lax.axis_size("narrow") - 1)]
    backward_n = [(j, i) for i, j in forward_n]
    first_x, last_x, first_y, last_y = edges
    x_lo = lax.ppermute(last_x, "wide", forward_w)
    x_hi = lax.ppermute(first_x, "wide", backward_w)
    y_lo = lax.ppermute(last_y, "narrow", forward_n)
    y_hi = lax.ppermute(first_y, "narrow", backward_n)
    return x_lo, x_hi, y_lo, y_hi


def to_columns(rows):
    tz, nx = rows.shape
    eye = jnp.where(
        lax.broadcasted_iota(jnp.int32, (nx, nx), 0) == lax.broadcasted_iota(jnp.int32, (nx, nx), 1),
        1.0, 0.0,
    )
    cols = lax.dot_general(
        eye, rows, (((1,), (1,)), ((), ())),
        precision=lax.Precision.HIGHEST, preferred_element_type=jnp.float32,
    )
    return jnp.concatenate([cols[:, k : k + 1][None] for k in range(tz)], axis=0)


def x_rows(ref):
    return jnp.concatenate([ref[k : k + 1, :][None] for k in range(ref.shape[0])], axis=0)


def store_x_rows(ref, rows):
    for k in range(ref.shape[0]):
        ref[k : k + 1, :] = rows[k]


def to_rows(block):
    tz, nx, ny = block.shape
    lane = lax.broadcasted_iota(jnp.int32, (nx, 128), 1)
    pick = jnp.where(
        lax.broadcasted_iota(jnp.int32, (tz, 128), 0) == lax.broadcasted_iota(jnp.int32, (tz, 128), 1),
        1.0, 0.0,
    )
    result = []
    for column in (0, ny - 1):
        gathered = jnp.zeros((nx, 128), jnp.float32)
        for k in range(tz):
            gathered = jnp.where(lane == k, block[k, :, column : column + 1], gathered)
        result.append(
            lax.dot_general(
                pick, gathered, (((1,), (1,)), ((), ())),
                precision=lax.Precision.HIGHEST, preferred_element_type=jnp.float32,
            )
        )
    return result[0], result[1]


def edge_kernel(block_ref, xl_ref, xh_ref, yl_ref, yh_ref):
    block = block_ref[...].astype(jnp.float32)
    store_x_rows(xl_ref, block[:, :1, :])
    store_x_rows(xh_ref, block[:, -1:, :])
    yl_ref[...], yh_ref[...] = to_rows(block)


def block_edges(block):
    depth, nx, ny = block.shape
    tz = CHUNK_Z
    f32 = jnp.float32
    row = pl.BlockSpec((tz, ny), lambda c: (c, 0))
    col = pl.BlockSpec((tz, nx), lambda c: (c, 0))
    return pl.pallas_call(
        edge_kernel,
        out_shape=(
            jax.ShapeDtypeStruct((depth, ny), f32),
            jax.ShapeDtypeStruct((depth, ny), f32),
            jax.ShapeDtypeStruct((depth, nx), f32),
            jax.ShapeDtypeStruct((depth, nx), f32),
        ),
        grid=(depth // tz,),
        in_specs=[pl.BlockSpec((tz, nx, ny), lambda c: (c, 0, 0))],
        out_specs=[row, row, col, col],
        compiler_params=pltpu.CompilerParams(dimension_semantics=("arbitrary",)),
    )(block)


def step_kernel(
    inside_ref, lpm_ref, lpb_ref, lpa_ref, lxl_ref, lxh_ref, lyl_ref, lyh_ref,
    pm_ref, pb_ref, pa_ref, qxl_ref, qxh_ref, qyl_ref, qyh_ref, f_ref,
    o_ref, exl_ref, exh_ref, eyl_ref, eyh_ref,
):
    c = pl.program_id(0)
    last = pl.num_programs(0) - 1
    tz, nx, ny = pm_ref.shape
    f32 = jnp.float32

    def side_perm(ref, k):
        return jnp.where(inside_ref[k] > 0, permeability(ref[...].astype(f32)), 0.0)

    kxl = side_perm(lxl_ref, 0)
    kxh = side_perm(lxh_ref, 1)
    kyl = to_columns(side_perm(lyl_ref, 2))
    kyh = to_columns(side_perm(lyh_ref, 3))
    qyl = to_columns(qyl_ref[...])
    qyh = to_columns(qyh_ref[...])

    xi = lax.broadcasted_iota(jnp.int32, (nx, ny), 0)
    yi = lax.broadcasted_iota(jnp.int32, (nx, ny), 1)
    lane = lax.broadcasted_iota(jnp.int32, (nx, 128), 1)

    below = jnp.where(c == 0, 0.0, permeability(lpb_ref[0].astype(f32)))
    above = jnp.where(c == last, 0.0, permeability(lpa_ref[0].astype(f32)))
    p_below = pb_ref[0].astype(f32)
    p_above = pa_ref[0].astype(f32)

    centre = permeability(lpm_ref[0].astype(f32))
    t_zm = harmonic(centre, below)
    p = pm_ref[0].astype(f32)
    p_prev = p_below
    first_y = jnp.zeros((nx, 128), f32)
    last_y = jnp.zeros((nx, 128), f32)
    for k in range(tz):
        if k + 1 < tz:
            nxt = permeability(lpm_ref[k + 1].astype(f32))
            p_next = pm_ref[k + 1].astype(f32)
        else:
            nxt = above
            p_next = p_above
        t_zp = harmonic(centre, nxt)

        fx = harmonic(centre, pltpu.roll(centre, nx - 1, 0))
        t_xp = jnp.where(xi == nx - 1, harmonic(centre[nx - 1 :, :], kxh[k : k + 1, :]), fx)
        t_xm = jnp.where(xi == 0, harmonic(centre[:1, :], kxl[k : k + 1, :]), pltpu.roll(fx, 1, 0))
        fy = harmonic(centre, pltpu.roll(centre, ny - 1, 1))
        t_yp = jnp.where(yi == ny - 1, harmonic(centre[:, ny - 1 :], kyh[k]), fy)
        t_ym = jnp.where(yi == 0, harmonic(centre[:, :1], kyl[k]), pltpu.roll(fy, 1, 1))

        n_xp = jnp.where(xi == nx - 1, qxh_ref[k : k + 1, :], pltpu.roll(p, nx - 1, 0))
        n_xm = jnp.where(xi == 0, qxl_ref[k : k + 1, :], pltpu.roll(p, 1, 0))
        n_yp = jnp.where(yi == ny - 1, qyh[k], pltpu.roll(p, ny - 1, 1))
        n_ym = jnp.where(yi == 0, qyl[k], pltpu.roll(p, 1, 1))

        flux = t_zp * (p_next - p)
        flux = flux + t_zm * (p_prev - p)
        flux = flux + t_xp * (n_xp - p)
        flux = flux + t_xm * (n_xm - p)
        flux = flux + t_yp * (n_yp - p)
        flux = flux + t_ym * (n_ym - p)
        new = p + STEP_SIZE * (flux + f_ref[k]) / (1.0 + 0.5 * p * p)
        o_ref[k] = new
        exl_ref[k : k + 1, :] = new[:1, :]
        exh_ref[k : k + 1, :] = new[nx - 1 :, :]
        first_y = jnp.where(lane == k, new[:, :1], first_y)
        last_y = jnp.where(lane == k, new[:, ny - 1 :], last_y)

        centre, t_zm, p_prev, p = nxt, t_zp, p, p_next

    pick = jnp.where(
        lax.broadcasted_iota(jnp.int32, (tz, 128), 0) == lax.broadcasted_iota(jnp.int32, (tz, 128), 1),
        1.0, 0.0,
    )
    for ref, gathered in ((eyl_ref, first_y), (eyh_ref, last_y)):
        ref[...] = lax.dot_general(
            pick, gathered, (((1,), (1,)), ((), ())),
            precision=lax.Precision.HIGHEST, preferred_element_type=f32,
        )


def advance(inside, log_perm, perm_halos, pressure, pressure_halos, flow):
    depth, nx, ny = pressure.shape
    tz = CHUNK_Z
    grid = (depth // tz,)
    main = pl.BlockSpec((tz, nx, ny), lambda c: (c, 0, 0))
    below = pl.BlockSpec((1, nx, ny), lambda c: (jnp.maximum(c * tz - 1, 0), 0, 0))
    above = pl.BlockSpec((1, nx, ny), lambda c: (jnp.minimum(c * tz + tz, depth - 1), 0, 0))
    row = pl.BlockSpec((tz, ny), lambda c: (c, 0))
    col = pl.BlockSpec((tz, nx), lambda c: (c, 0))
    side = [row, row, col, col]
    smem = pl.BlockSpec(memory_space=pltpu.SMEM)
    f32 = jnp.float32
    out_shape = (
        jax.ShapeDtypeStruct((depth, nx, ny), f32),
        jax.ShapeDtypeStruct((depth, ny), f32),
        jax.ShapeDtypeStruct((depth, ny), f32),
        jax.ShapeDtypeStruct((depth, nx), f32),
        jax.ShapeDtypeStruct((depth, nx), f32),
    )
    new, x_lo, x_hi, y_lo, y_hi = pl.pallas_call(
        step_kernel,
        out_shape=out_shape,
        grid=grid,
        in_specs=[smem, main, below, above] + side + [main, below, above] + side + [main],
        out_specs=[main] + side,
        compiler_params=pltpu.CompilerParams(dimension_semantics=("arbitrary",)),
    )(inside, log_perm, log_perm, log_perm, *perm_halos, pressure, pressure, pressure, *pressure_halos, flow)
    return new, (x_lo, x_hi, y_lo, y_hi)


def line_kernel(g_ref, rx_ref, ry_ref, o_ref, *, count_w, count_n):
    f32 = jnp.float32
    nx = g_ref.shape[2]
    ny = g_ref.shape[3]
    rx = rx_ref[...]
    halves = []
    for n in range(count_n):
        lines = jnp.concatenate([g_ref[w * count_n + n, 0] for w in range(count_w)], axis=0)
        halves.append(jnp.dot(rx, lines, preferred_element_type=f32).astype(jnp.bfloat16))
    second = jnp.concatenate(halves, axis=1)
    third = lax.dot_general(
        second, ry_ref[...], (((1,), (1,)), ((), ())), preferred_element_type=f32
    ).astype(jnp.bfloat16)
    for w in range(count_w):
        for n in range(count_n):
            o_ref[w * count_n + n, 0] = third[w * nx : (w + 1) * nx, n * ny : (n + 1) * ny]


def line_transforms(gathered, root_x, root_y, count_w, count_n):
    groups, planes, nx, ny = gathered.shape
    block = pl.BlockSpec((groups, 1, nx, ny), lambda z: (0, z, 0, 0))
    whole_x = pl.BlockSpec(root_x.shape, lambda z: (0, 0))
    whole_y = pl.BlockSpec(root_y.shape, lambda z: (0, 0))
    return pl.pallas_call(
        functools.partial(line_kernel, count_w=count_w, count_n=count_n),
        out_shape=jax.ShapeDtypeStruct(gathered.shape, jnp.bfloat16),
        grid=(planes,),
        in_specs=[block, whole_x, whole_y],
        out_specs=block,
        compiler_params=pltpu.CompilerParams(dimension_semantics=("arbitrary",)),
    )(gathered, root_x, root_y)


def body(noise, root_z, root_x, root_y, pressure_start, well_x, well_y, well_z, well_rate):
    depth, rows_x, rows_y = noise.shape
    first = jnp.dot(
        root_z, noise.reshape(depth, rows_x * rows_y), preferred_element_type=jnp.float32
    )
    first = first.reshape(depth, rows_x, rows_y).astype(jnp.bfloat16)
    count_w = lax.axis_size("wide")
    count_n = lax.axis_size("narrow")
    groups = count_w * count_n
    planes = depth // groups
    gathered = lax.all_to_all(
        first.reshape(groups, planes, rows_x, rows_y),
        ("wide", "narrow"), split_axis=0, concat_axis=0, tiled=True,
    )
    outgoing = line_transforms(gathered, root_x, root_y, count_w, count_n)
    log_perm = lax.all_to_all(
        outgoing, ("wide", "narrow"), split_axis=0, concat_axis=0, tiled=True,
    ).reshape(depth, rows_x, rows_y)

    wide_at = lax.axis_index("wide")
    narrow_at = lax.axis_index("narrow")
    last_w = lax.axis_size("wide") - 1
    last_n = lax.axis_size("narrow") - 1

    local_x = well_x - wide_at * rows_x
    local_y = well_y - narrow_at * rows_y
    valid = (local_x >= 0) & (local_x < rows_x) & (local_y >= 0) & (local_y < rows_y)
    rates = jnp.where(valid, well_rate, 0.0).astype(jnp.float32)
    wells = well_x.shape[0]
    cells = well_z * rows_x + local_x
    pick_rows = jnp.where(
        lax.broadcasted_iota(jnp.int32, (depth * rows_x, wells), 0) == cells[None, :],
        rates[None, :],
        0.0,
    )
    pick_cols = (
        lax.broadcasted_iota(jnp.int32, (wells, rows_y), 1) == local_y[:, None]
    ).astype(jnp.float32)
    flow = jnp.dot(
        pick_rows, pick_cols, precision=lax.Precision.HIGHEST, preferred_element_type=jnp.float32
    ).reshape(depth, rows_x, rows_y)

    inside = jnp.stack(
        [wide_at > 0, wide_at < last_w, narrow_at > 0, narrow_at < last_n]
    ).astype(jnp.int32)
    perm_halos = halos(block_edges(log_perm))
    pressure = pressure_start
    edges = block_edges(pressure_start)
    for step in range(STEPS):
        pressure, edges = advance(inside, log_perm, perm_halos, pressure, halos(edges), flow)
    return (log_perm, pressure)


def solution(mesh):
    in_specs = (
        P("member", "wide", "narrow"),
        P(),
        P(),
        P(),
        P("member", "wide", "narrow"),
        P("member"),
        P("member"),
        P("member"),
        P("member"),
    )
    out_specs = (P("member", "wide", "narrow"), P("member", "wide", "narrow"))
    return jax.shard_map(body, mesh=mesh, in_specs=in_specs, out_specs=out_specs, check_vma=False)
```

```python
import functools

import jax
import jax.numpy as jnp
from jax import lax
from jax.experimental import pallas as pl
from jax.experimental.pallas import tpu as pltpu
from jax.sharding import PartitionSpec as P

STEPS = 2


STEP_SIZE = 0.03
CAP_LOG = 1.5
CHUNK_Z = 8
EDGE_Z = 32


def permeability(values):
    return jnp.exp(CAP_LOG * jnp.tanh(values / CAP_LOG))


def harmonic(a, b):
    return 2.0 * a * b / (a + b)


def halos(edges):
    forward_w = [(i, i + 1) for i in range(lax.axis_size("wide") - 1)]
    backward_w = [(j, i) for i, j in forward_w]
    forward_n = [(i, i + 1) for i in range(lax.axis_size("narrow") - 1)]
    backward_n = [(j, i) for i, j in forward_n]
    first_x, last_x, first_y, last_y = edges
    x_lo = lax.ppermute(last_x, "wide", forward_w)
    x_hi = lax.ppermute(first_x, "wide", backward_w)
    y_lo = lax.ppermute(last_y, "narrow", forward_n)
    y_hi = lax.ppermute(first_y, "narrow", backward_n)
    return x_lo, x_hi, y_lo, y_hi


def to_columns(rows):
    tz, nx = rows.shape
    eye = jnp.where(
        lax.broadcasted_iota(jnp.int32, (nx, nx), 0) == lax.broadcasted_iota(jnp.int32, (nx, nx), 1),
        1.0, 0.0,
    )
    cols = lax.dot_general(
        eye, rows, (((1,), (1,)), ((), ())),
        precision=lax.Precision.HIGHEST, preferred_element_type=jnp.float32,
    )
    return jnp.concatenate([cols[:, k : k + 1][None] for k in range(tz)], axis=0)


def x_rows(ref):
    return jnp.concatenate([ref[k : k + 1, :][None] for k in range(ref.shape[0])], axis=0)


def store_x_rows(ref, rows):
    for k in range(ref.shape[0]):
        ref[k : k + 1, :] = rows[k]


def to_rows(block):
    tz, nx, ny = block.shape
    lane = lax.broadcasted_iota(jnp.int32, (nx, 128), 1)
    pick = jnp.where(
        lax.broadcasted_iota(jnp.int32, (tz, 128), 0) == lax.broadcasted_iota(jnp.int32, (tz, 128), 1),
        1.0, 0.0,
    )
    result = []
    for column in (0, ny - 1):
        gathered = jnp.zeros((nx, 128), jnp.float32)
        for k in range(tz):
            gathered = jnp.where(lane == k, block[k, :, column : column + 1], gathered)
        result.append(
            lax.dot_general(
                pick, gathered, (((1,), (1,)), ((), ())),
                precision=lax.Precision.HIGHEST, preferred_element_type=jnp.float32,
            )
        )
    return result[0], result[1]


def edge_kernel(block_ref, xl_ref, xh_ref, yl_ref, yh_ref, *copy_ref):
    block = block_ref[...]
    if copy_ref:
        copy_ref[0][...] = block
    block = block.astype(jnp.float32)
    store_x_rows(xl_ref, block[:, :1, :])
    store_x_rows(xh_ref, block[:, -1:, :])
    yl_ref[...], yh_ref[...] = to_rows(block)


def block_edges(block, keep=False):
    depth, nx, ny = block.shape
    tz = EDGE_Z
    f32 = jnp.float32
    whole = pl.BlockSpec((tz, nx, ny), lambda c: (c, 0, 0))
    row = pl.BlockSpec((tz, ny), lambda c: (c, 0))
    col = pl.BlockSpec((tz, nx), lambda c: (c, 0))
    out_shape = [
        jax.ShapeDtypeStruct((depth, ny), f32),
        jax.ShapeDtypeStruct((depth, ny), f32),
        jax.ShapeDtypeStruct((depth, nx), f32),
        jax.ShapeDtypeStruct((depth, nx), f32),
    ]
    out_specs = [row, row, col, col]
    if keep:
        out_shape.append(jax.ShapeDtypeStruct(block.shape, block.dtype))
        out_specs.append(whole)
    return pl.pallas_call(
        edge_kernel,
        out_shape=tuple(out_shape),
        grid=(depth // tz,),
        in_specs=[whole],
        out_specs=out_specs,
        compiler_params=pltpu.CompilerParams(dimension_semantics=("arbitrary",)),
    )(block)


def step_kernel(
    inside_ref, lpm_ref, lpb_ref, lpa_ref, lxl_ref, lxh_ref, lyl_ref, lyh_ref,
    pm_ref, pb_ref, pa_ref, qxl_ref, qxh_ref, qyl_ref, qyh_ref, f_ref,
    o_ref, exl_ref, exh_ref, eyl_ref, eyh_ref,
):
    c = pl.program_id(0)
    last = pl.num_programs(0) - 1
    tz, nx, ny = pm_ref.shape
    f32 = jnp.float32

    def side_perm(ref, k):
        return jnp.where(inside_ref[k] > 0, permeability(ref[...].astype(f32)), 0.0)

    kxl = jnp.where(inside_ref[0] > 0, permeability(x_rows(lxl_ref)), 0.0)
    kxh = jnp.where(inside_ref[1] > 0, permeability(x_rows(lxh_ref)), 0.0)
    kyl = to_columns(side_perm(lyl_ref, 2))
    kyh = to_columns(side_perm(lyh_ref, 3))

    below = jnp.where(c == 0, 0.0, permeability(lpb_ref[...].astype(f32)))
    above = jnp.where(c == last, 0.0, permeability(lpa_ref[...].astype(f32)))
    centre = permeability(lpm_ref[...].astype(f32))
    ext = jnp.concatenate([below, centre, above], axis=0)
    faces = harmonic(ext[:-1], ext[1:])
    t_zm = faces[:-1]
    t_zp = faces[1:]

    xi = lax.broadcasted_iota(jnp.int32, (tz, nx, ny), 1)
    yi = lax.broadcasted_iota(jnp.int32, (tz, nx, ny), 2)

    fx = harmonic(centre, pltpu.roll(centre, nx - 1, 1))
    t_xp = jnp.where(xi == nx - 1, harmonic(centre[:, nx - 1 :, :], kxh), fx)
    t_xm = jnp.where(xi == 0, harmonic(centre[:, :1, :], kxl), pltpu.roll(fx, 1, 1))
    fy = harmonic(centre, pltpu.roll(centre, ny - 1, 2))
    t_yp = jnp.where(yi == ny - 1, harmonic(centre[:, :, ny - 1 :], kyh), fy)
    t_ym = jnp.where(yi == 0, harmonic(centre[:, :, :1], kyl), pltpu.roll(fy, 1, 2))

    p = pm_ref[...].astype(f32)
    pext = jnp.concatenate([pb_ref[...].astype(f32), p, pa_ref[...].astype(f32)], axis=0)
    n_xp = jnp.where(xi == nx - 1, x_rows(qxh_ref), pltpu.roll(p, nx - 1, 1))
    n_xm = jnp.where(xi == 0, x_rows(qxl_ref), pltpu.roll(p, 1, 1))
    n_yp = jnp.where(yi == ny - 1, to_columns(qyh_ref[...]), pltpu.roll(p, ny - 1, 2))
    n_ym = jnp.where(yi == 0, to_columns(qyl_ref[...]), pltpu.roll(p, 1, 2))

    flux = t_zp * (pext[2:] - p)
    flux = flux + t_zm * (pext[:-2] - p)
    flux = flux + t_xp * (n_xp - p)
    flux = flux + t_xm * (n_xm - p)
    flux = flux + t_yp * (n_yp - p)
    flux = flux + t_ym * (n_ym - p)
    new = p + STEP_SIZE * (flux + f_ref[...]) / (1.0 + 0.5 * p * p)
    o_ref[...] = new
    store_x_rows(exl_ref, new[:, :1, :])
    store_x_rows(exh_ref, new[:, nx - 1 :, :])
    eyl_ref[...], eyh_ref[...] = to_rows(new)


def advance(inside, log_perm, perm_halos, pressure, pressure_halos, flow):
    depth, nx, ny = pressure.shape
    tz = CHUNK_Z
    grid = (depth // tz,)
    main = pl.BlockSpec((tz, nx, ny), lambda c: (c, 0, 0))
    below = pl.BlockSpec((1, nx, ny), lambda c: (jnp.maximum(c * tz - 1, 0), 0, 0))
    above = pl.BlockSpec((1, nx, ny), lambda c: (jnp.minimum(c * tz + tz, depth - 1), 0, 0))
    row = pl.BlockSpec((tz, ny), lambda c: (c, 0))
    col = pl.BlockSpec((tz, nx), lambda c: (c, 0))
    side = [row, row, col, col]
    smem = pl.BlockSpec(memory_space=pltpu.SMEM)
    f32 = jnp.float32
    out_shape = (
        jax.ShapeDtypeStruct((depth, nx, ny), f32),
        jax.ShapeDtypeStruct((depth, ny), f32),
        jax.ShapeDtypeStruct((depth, ny), f32),
        jax.ShapeDtypeStruct((depth, nx), f32),
        jax.ShapeDtypeStruct((depth, nx), f32),
    )
    new, x_lo, x_hi, y_lo, y_hi = pl.pallas_call(
        step_kernel,
        out_shape=out_shape,
        grid=grid,
        in_specs=[smem, main, below, above] + side + [main, below, above] + side + [main],
        out_specs=[main] + side,
        compiler_params=pltpu.CompilerParams(dimension_semantics=("arbitrary",)),
    )(inside, log_perm, log_perm, log_perm, *perm_halos, pressure, pressure, pressure, *pressure_halos, flow)
    return new, (x_lo, x_hi, y_lo, y_hi)


def line_kernel(g_ref, rx_ref, ry_ref, o_ref, *, count_w, count_n):
    f32 = jnp.float32
    nx = g_ref.shape[2]
    ny = g_ref.shape[3]
    rx = rx_ref[...]
    halves = []
    for n in range(count_n):
        lines = jnp.concatenate([g_ref[w * count_n + n, 0] for w in range(count_w)], axis=0)
        halves.append(jnp.dot(rx, lines, preferred_element_type=f32).astype(jnp.bfloat16))
    second = jnp.concatenate(halves, axis=1)
    third = lax.dot_general(
        second, ry_ref[...], (((1,), (1,)), ((), ())), preferred_element_type=f32
    ).astype(jnp.bfloat16)
    for w in range(count_w):
        for n in range(count_n):
            o_ref[w * count_n + n, 0] = third[w * nx : (w + 1) * nx, n * ny : (n + 1) * ny]


def line_transforms(gathered, root_x, root_y, count_w, count_n):
    groups, planes, nx, ny = gathered.shape
    block = pl.BlockSpec((groups, 1, nx, ny), lambda z: (0, z, 0, 0))
    whole_x = pl.BlockSpec(root_x.shape, lambda z: (0, 0))
    whole_y = pl.BlockSpec(root_y.shape, lambda z: (0, 0))
    return pl.pallas_call(
        functools.partial(line_kernel, count_w=count_w, count_n=count_n),
        out_shape=jax.ShapeDtypeStruct(gathered.shape, jnp.bfloat16),
        grid=(planes,),
        in_specs=[block, whole_x, whole_y],
        out_specs=block,
        compiler_params=pltpu.CompilerParams(dimension_semantics=("arbitrary",)),
    )(gathered, root_x, root_y)


def body(noise, root_z, root_x, root_y, pressure_start, well_x, well_y, well_z, well_rate):
    depth, rows_x, rows_y = noise.shape
    first = jnp.dot(
        root_z, noise.reshape(depth, rows_x * rows_y), preferred_element_type=jnp.float32
    )
    first = first.reshape(depth, rows_x, rows_y).astype(jnp.bfloat16)
    count_w = lax.axis_size("wide")
    count_n = lax.axis_size("narrow")
    groups = count_w * count_n
    planes = depth // groups
    gathered = lax.all_to_all(
        first.reshape(groups, planes, rows_x, rows_y),
        ("wide", "narrow"), split_axis=0, concat_axis=0, tiled=True,
    )
    outgoing = line_transforms(gathered, root_x, root_y, count_w, count_n)
    log_perm = lax.all_to_all(
        outgoing, ("wide", "narrow"), split_axis=0, concat_axis=0, tiled=True,
    ).reshape(depth, rows_x, rows_y)

    wide_at = lax.axis_index("wide")
    narrow_at = lax.axis_index("narrow")
    last_w = lax.axis_size("wide") - 1
    last_n = lax.axis_size("narrow") - 1

    local_x = well_x - wide_at * rows_x
    local_y = well_y - narrow_at * rows_y
    valid = (local_x >= 0) & (local_x < rows_x) & (local_y >= 0) & (local_y < rows_y)
    rates = jnp.where(valid, well_rate, 0.0).astype(jnp.float32)
    wells = well_x.shape[0]
    cells = well_z * rows_x + local_x
    pick_rows = jnp.where(
        lax.broadcasted_iota(jnp.int32, (depth * rows_x, wells), 0) == cells[None, :],
        rates[None, :],
        0.0,
    )
    pick_cols = (
        lax.broadcasted_iota(jnp.int32, (wells, rows_y), 1) == local_y[:, None]
    ).astype(jnp.float32)
    flow = jnp.dot(
        pick_rows, pick_cols, precision=lax.Precision.HIGHEST, preferred_element_type=jnp.float32
    ).reshape(depth, rows_x, rows_y)

    inside = jnp.stack(
        [wide_at > 0, wide_at < last_w, narrow_at > 0, narrow_at < last_n]
    ).astype(jnp.int32)
    edges = block_edges(pressure_start)
    flow, edges = lax.optimization_barrier((flow, edges))
    *lp_edges, log_perm = block_edges(log_perm, keep=True)
    perm_halos = halos(lp_edges)
    pressure = pressure_start
    for step in range(STEPS):
        pressure, edges = advance(inside, log_perm, perm_halos, pressure, halos(edges), flow)
    return (log_perm, pressure)


def solution(mesh):
    in_specs = (
        P("member", "wide", "narrow"),
        P(),
        P(),
        P(),
        P("member", "wide", "narrow"),
        P("member"),
        P("member"),
        P("member"),
        P("member"),
    )
    out_specs = (P("member", "wide", "narrow"), P("member", "wide", "narrow"))
    return jax.shard_map(body, mesh=mesh, in_specs=in_specs, out_specs=out_specs, check_vma=False)
```

```python
import functools

import jax
import jax.numpy as jnp
from jax import lax
from jax.experimental import pallas as pl
from jax.experimental.pallas import tpu as pltpu
from jax.sharding import PartitionSpec as P

STEPS = 2


STEP_SIZE = 0.03
CAP_LOG = 1.5
CHUNK_Z = 8
EDGE_Z = 32
DEPTH_X = 16


def permeability(values):
    return jnp.exp(CAP_LOG * jnp.tanh(values / CAP_LOG))


def harmonic(a, b):
    return 2.0 * a * b / (a + b)


def halos(edges):
    forward_w = [(i, i + 1) for i in range(lax.axis_size("wide") - 1)]
    backward_w = [(j, i) for i, j in forward_w]
    forward_n = [(i, i + 1) for i in range(lax.axis_size("narrow") - 1)]
    backward_n = [(j, i) for i, j in forward_n]
    first_x, last_x, first_y, last_y = edges
    x_lo = lax.ppermute(last_x, "wide", forward_w)
    x_hi = lax.ppermute(first_x, "wide", backward_w)
    y_lo = lax.ppermute(last_y, "narrow", forward_n)
    y_hi = lax.ppermute(first_y, "narrow", backward_n)
    return x_lo, x_hi, y_lo, y_hi


def to_columns(rows):
    tz, nx = rows.shape
    eye = jnp.where(
        lax.broadcasted_iota(jnp.int32, (nx, nx), 0) == lax.broadcasted_iota(jnp.int32, (nx, nx), 1),
        1.0, 0.0,
    )
    cols = lax.dot_general(
        eye, rows, (((1,), (1,)), ((), ())),
        precision=lax.Precision.HIGHEST, preferred_element_type=jnp.float32,
    )
    return jnp.concatenate([cols[:, k : k + 1][None] for k in range(tz)], axis=0)


def x_rows(ref):
    return jnp.concatenate([ref[k : k + 1, :][None] for k in range(ref.shape[0])], axis=0)


def store_x_rows(ref, rows):
    for k in range(ref.shape[0]):
        ref[k : k + 1, :] = rows[k]


def to_rows(block):
    tz, nx, ny = block.shape
    lane = lax.broadcasted_iota(jnp.int32, (nx, 128), 1)
    pick = jnp.where(
        lax.broadcasted_iota(jnp.int32, (tz, 128), 0) == lax.broadcasted_iota(jnp.int32, (tz, 128), 1),
        1.0, 0.0,
    )
    result = []
    for column in (0, ny - 1):
        gathered = jnp.zeros((nx, 128), jnp.float32)
        for k in range(tz):
            gathered = jnp.where(lane == k, block[k, :, column : column + 1], gathered)
        result.append(
            lax.dot_general(
                pick, gathered, (((1,), (1,)), ((), ())),
                precision=lax.Precision.HIGHEST, preferred_element_type=jnp.float32,
            )
        )
    return result[0], result[1]


def edge_kernel(block_ref, xl_ref, xh_ref, yl_ref, yh_ref, *copy_ref):
    block = block_ref[...]
    if copy_ref:
        copy_ref[0][...] = block
    block = block.astype(jnp.float32)
    store_x_rows(xl_ref, block[:, :1, :])
    store_x_rows(xh_ref, block[:, -1:, :])
    yl_ref[...], yh_ref[...] = to_rows(block)


def block_edges(block, keep=False):
    depth, nx, ny = block.shape
    tz = EDGE_Z
    f32 = jnp.float32
    whole = pl.BlockSpec((tz, nx, ny), lambda c: (c, 0, 0))
    row = pl.BlockSpec((tz, ny), lambda c: (c, 0))
    col = pl.BlockSpec((tz, nx), lambda c: (c, 0))
    out_shape = [
        jax.ShapeDtypeStruct((depth, ny), f32),
        jax.ShapeDtypeStruct((depth, ny), f32),
        jax.ShapeDtypeStruct((depth, nx), f32),
        jax.ShapeDtypeStruct((depth, nx), f32),
    ]
    out_specs = [row, row, col, col]
    if keep:
        out_shape.append(jax.ShapeDtypeStruct(block.shape, block.dtype))
        out_specs.append(whole)
    return pl.pallas_call(
        edge_kernel,
        out_shape=tuple(out_shape),
        grid=(depth // tz,),
        in_specs=[whole],
        out_specs=out_specs,
        compiler_params=pltpu.CompilerParams(dimension_semantics=("arbitrary",)),
    )(block)


def step_kernel(
    inside_ref, lpm_ref, lpb_ref, lpa_ref, lxl_ref, lxh_ref, lyl_ref, lyh_ref,
    pm_ref, pb_ref, pa_ref, qxl_ref, qxh_ref, qyl_ref, qyh_ref, f_ref,
    o_ref, exl_ref, exh_ref, eyl_ref, eyh_ref,
):
    c = pl.program_id(0)
    last = pl.num_programs(0) - 1
    tz, nx, ny = pm_ref.shape
    f32 = jnp.float32

    def side_perm(ref, k):
        return jnp.where(inside_ref[k] > 0, permeability(ref[...].astype(f32)), 0.0)

    kxl = jnp.where(inside_ref[0] > 0, permeability(x_rows(lxl_ref)), 0.0)
    kxh = jnp.where(inside_ref[1] > 0, permeability(x_rows(lxh_ref)), 0.0)
    kyl = to_columns(side_perm(lyl_ref, 2))
    kyh = to_columns(side_perm(lyh_ref, 3))

    below = jnp.where(c == 0, 0.0, permeability(lpb_ref[...].astype(f32)))
    above = jnp.where(c == last, 0.0, permeability(lpa_ref[...].astype(f32)))
    centre = permeability(lpm_ref[...].astype(f32))
    ext = jnp.concatenate([below, centre, above], axis=0)
    faces = harmonic(ext[:-1], ext[1:])
    t_zm = faces[:-1]
    t_zp = faces[1:]

    xi = lax.broadcasted_iota(jnp.int32, (tz, nx, ny), 1)
    yi = lax.broadcasted_iota(jnp.int32, (tz, nx, ny), 2)

    fx = harmonic(centre, pltpu.roll(centre, nx - 1, 1))
    t_xp = jnp.where(xi == nx - 1, harmonic(centre[:, nx - 1 :, :], kxh), fx)
    t_xm = jnp.where(xi == 0, harmonic(centre[:, :1, :], kxl), pltpu.roll(fx, 1, 1))
    fy = harmonic(centre, pltpu.roll(centre, ny - 1, 2))
    t_yp = jnp.where(yi == ny - 1, harmonic(centre[:, :, ny - 1 :], kyh), fy)
    t_ym = jnp.where(yi == 0, harmonic(centre[:, :, :1], kyl), pltpu.roll(fy, 1, 2))

    p = pm_ref[...].astype(f32)
    pext = jnp.concatenate([pb_ref[...].astype(f32), p, pa_ref[...].astype(f32)], axis=0)
    n_xp = jnp.where(xi == nx - 1, x_rows(qxh_ref), pltpu.roll(p, nx - 1, 1))
    n_xm = jnp.where(xi == 0, x_rows(qxl_ref), pltpu.roll(p, 1, 1))
    n_yp = jnp.where(yi == ny - 1, to_columns(qyh_ref[...]), pltpu.roll(p, ny - 1, 2))
    n_ym = jnp.where(yi == 0, to_columns(qyl_ref[...]), pltpu.roll(p, 1, 2))

    flux = t_zp * (pext[2:] - p)
    flux = flux + t_zm * (pext[:-2] - p)
    flux = flux + t_xp * (n_xp - p)
    flux = flux + t_xm * (n_xm - p)
    flux = flux + t_yp * (n_yp - p)
    flux = flux + t_ym * (n_ym - p)
    new = p + STEP_SIZE * (flux + f_ref[...]) / (1.0 + 0.5 * p * p)
    o_ref[...] = new
    store_x_rows(exl_ref, new[:, :1, :])
    store_x_rows(exh_ref, new[:, nx - 1 :, :])
    eyl_ref[...], eyh_ref[...] = to_rows(new)


def advance(inside, log_perm, perm_halos, pressure, pressure_halos, flow):
    depth, nx, ny = pressure.shape
    tz = CHUNK_Z
    grid = (depth // tz,)
    main = pl.BlockSpec((tz, nx, ny), lambda c: (c, 0, 0))
    below = pl.BlockSpec((1, nx, ny), lambda c: (jnp.maximum(c * tz - 1, 0), 0, 0))
    above = pl.BlockSpec((1, nx, ny), lambda c: (jnp.minimum(c * tz + tz, depth - 1), 0, 0))
    row = pl.BlockSpec((tz, ny), lambda c: (c, 0))
    col = pl.BlockSpec((tz, nx), lambda c: (c, 0))
    side = [row, row, col, col]
    smem = pl.BlockSpec(memory_space=pltpu.SMEM)
    f32 = jnp.float32
    out_shape = (
        jax.ShapeDtypeStruct((depth, nx, ny), f32),
        jax.ShapeDtypeStruct((depth, ny), f32),
        jax.ShapeDtypeStruct((depth, ny), f32),
        jax.ShapeDtypeStruct((depth, nx), f32),
        jax.ShapeDtypeStruct((depth, nx), f32),
    )
    new, x_lo, x_hi, y_lo, y_hi = pl.pallas_call(
        step_kernel,
        out_shape=out_shape,
        grid=grid,
        in_specs=[smem, main, below, above] + side + [main, below, above] + side + [main],
        out_specs=[main] + side,
        compiler_params=pltpu.CompilerParams(dimension_semantics=("arbitrary",)),
    )(inside, log_perm, log_perm, log_perm, *perm_halos, pressure, pressure, pressure, *pressure_halos, flow)
    return new, (x_lo, x_hi, y_lo, y_hi)


def depth_kernel(rz_ref, n_ref, o_ref):
    rz = rz_ref[...]
    for i in range(n_ref.shape[1]):
        o_ref[:, i, :] = jnp.dot(rz, n_ref[:, i, :], preferred_element_type=jnp.float32).astype(
            jnp.bfloat16
        )


def depth_transform(root_z, noise):
    depth, nx, ny = noise.shape
    bx = min(nx, DEPTH_X)
    block = pl.BlockSpec((depth, bx, ny), lambda i: (0, i, 0))
    return pl.pallas_call(
        depth_kernel,
        out_shape=jax.ShapeDtypeStruct(noise.shape, jnp.bfloat16),
        grid=(nx // bx,),
        in_specs=[pl.BlockSpec(root_z.shape, lambda i: (0, 0)), block],
        out_specs=block,
        compiler_params=pltpu.CompilerParams(dimension_semantics=("arbitrary",)),
    )(root_z, noise)


def line_kernel(g_ref, rx_ref, ry_ref, o_ref, *, count_w, count_n):
    f32 = jnp.float32
    nx = g_ref.shape[2]
    ny = g_ref.shape[3]
    rx = rx_ref[...]
    halves = []
    for n in range(count_n):
        lines = jnp.concatenate([g_ref[w * count_n + n, 0] for w in range(count_w)], axis=0)
        halves.append(jnp.dot(rx, lines, preferred_element_type=f32).astype(jnp.bfloat16))
    second = jnp.concatenate(halves, axis=1)
    third = lax.dot_general(
        second, ry_ref[...], (((1,), (1,)), ((), ())), preferred_element_type=f32
    ).astype(jnp.bfloat16)
    for w in range(count_w):
        for n in range(count_n):
            o_ref[w * count_n + n, 0] = third[w * nx : (w + 1) * nx, n * ny : (n + 1) * ny]


def line_transforms(gathered, root_x, root_y, count_w, count_n):
    groups, planes, nx, ny = gathered.shape
    block = pl.BlockSpec((groups, 1, nx, ny), lambda z: (0, z, 0, 0))
    whole_x = pl.BlockSpec(root_x.shape, lambda z: (0, 0))
    whole_y = pl.BlockSpec(root_y.shape, lambda z: (0, 0))
    return pl.pallas_call(
        functools.partial(line_kernel, count_w=count_w, count_n=count_n),
        out_shape=jax.ShapeDtypeStruct(gathered.shape, jnp.bfloat16),
        grid=(planes,),
        in_specs=[block, whole_x, whole_y],
        out_specs=block,
        compiler_params=pltpu.CompilerParams(dimension_semantics=("arbitrary",)),
    )(gathered, root_x, root_y)


def body(noise, root_z, root_x, root_y, pressure_start, well_x, well_y, well_z, well_rate):
    depth, rows_x, rows_y = noise.shape
    first = depth_transform(root_z, noise)
    count_w = lax.axis_size("wide")
    count_n = lax.axis_size("narrow")
    groups = count_w * count_n
    planes = depth // groups
    gathered = lax.all_to_all(
        first.reshape(groups, planes, rows_x, rows_y),
        ("wide", "narrow"), split_axis=0, concat_axis=0, tiled=True,
    )
    outgoing = line_transforms(gathered, root_x, root_y, count_w, count_n)
    log_perm = lax.all_to_all(
        outgoing, ("wide", "narrow"), split_axis=0, concat_axis=0, tiled=True,
    ).reshape(depth, rows_x, rows_y)

    wide_at = lax.axis_index("wide")
    narrow_at = lax.axis_index("narrow")
    last_w = lax.axis_size("wide") - 1
    last_n = lax.axis_size("narrow") - 1

    local_x = well_x - wide_at * rows_x
    local_y = well_y - narrow_at * rows_y
    valid = (local_x >= 0) & (local_x < rows_x) & (local_y >= 0) & (local_y < rows_y)
    rates = jnp.where(valid, well_rate, 0.0).astype(jnp.float32)
    wells = well_x.shape[0]
    cells = well_z * rows_x + local_x
    pick_rows = jnp.where(
        lax.broadcasted_iota(jnp.int32, (depth * rows_x, wells), 0) == cells[None, :],
        rates[None, :],
        0.0,
    )
    pick_cols = (
        lax.broadcasted_iota(jnp.int32, (wells, rows_y), 1) == local_y[:, None]
    ).astype(jnp.float32)
    flow = jnp.dot(
        pick_rows, pick_cols, precision=lax.Precision.HIGHEST, preferred_element_type=jnp.float32
    ).reshape(depth, rows_x, rows_y)

    inside = jnp.stack(
        [wide_at > 0, wide_at < last_w, narrow_at > 0, narrow_at < last_n]
    ).astype(jnp.int32)
    edges = block_edges(pressure_start)
    flow, edges = lax.optimization_barrier((flow, edges))
    *lp_edges, log_perm = block_edges(log_perm, keep=True)
    perm_halos = halos(lp_edges)
    pressure = pressure_start
    for step in range(STEPS):
        pressure, edges = advance(inside, log_perm, perm_halos, pressure, halos(edges), flow)
    return (log_perm, pressure)


def solution(mesh):
    in_specs = (
        P("member", "wide", "narrow"),
        P(),
        P(),
        P(),
        P("member", "wide", "narrow"),
        P("member"),
        P("member"),
        P("member"),
        P("member"),
    )
    out_specs = (P("member", "wide", "narrow"), P("member", "wide", "narrow"))
    return jax.shard_map(body, mesh=mesh, in_specs=in_specs, out_specs=out_specs, check_vma=False)
```

```python
import functools

import jax
import jax.numpy as jnp
from jax import lax
from jax.experimental import pallas as pl
from jax.experimental.pallas import tpu as pltpu
from jax.sharding import PartitionSpec as P

STEPS = 2


STEP_SIZE = 0.03
CAP_LOG = 1.5
CHUNK_Z = 8
EDGE_Z = 32
DEPTH_X = 16


def permeability(values):
    return jnp.exp(CAP_LOG * jnp.tanh(values / CAP_LOG))


def harmonic(a, b):
    return 2.0 * a * b / (a + b)


def halos(edges):
    forward_w = [(i, i + 1) for i in range(lax.axis_size("wide") - 1)]
    backward_w = [(j, i) for i, j in forward_w]
    forward_n = [(i, i + 1) for i in range(lax.axis_size("narrow") - 1)]
    backward_n = [(j, i) for i, j in forward_n]
    first_x, last_x, first_y, last_y = edges
    x_lo = lax.ppermute(last_x, "wide", forward_w)
    x_hi = lax.ppermute(first_x, "wide", backward_w)
    y_lo = lax.ppermute(last_y, "narrow", forward_n)
    y_hi = lax.ppermute(first_y, "narrow", backward_n)
    return x_lo, x_hi, y_lo, y_hi


def to_columns(rows):
    tz, nx = rows.shape
    eye = jnp.where(
        lax.broadcasted_iota(jnp.int32, (nx, nx), 0) == lax.broadcasted_iota(jnp.int32, (nx, nx), 1),
        1.0, 0.0,
    )
    cols = lax.dot_general(
        eye, rows, (((1,), (1,)), ((), ())),
        precision=lax.Precision.HIGHEST, preferred_element_type=jnp.float32,
    )
    return jnp.concatenate([cols[:, k : k + 1][None] for k in range(tz)], axis=0)


def x_rows(ref):
    return jnp.concatenate([ref[k : k + 1, :][None] for k in range(ref.shape[0])], axis=0)


def store_x_rows(ref, rows):
    for k in range(ref.shape[0]):
        ref[k : k + 1, :] = rows[k]


def to_rows(block):
    tz, nx, ny = block.shape
    lane = lax.broadcasted_iota(jnp.int32, (nx, 128), 1)
    pick = jnp.where(
        lax.broadcasted_iota(jnp.int32, (tz, 128), 0) == lax.broadcasted_iota(jnp.int32, (tz, 128), 1),
        1.0, 0.0,
    )
    result = []
    for column in (0, ny - 1):
        gathered = jnp.zeros((nx, 128), jnp.float32)
        for k in range(tz):
            gathered = jnp.where(lane == k, block[k, :, column : column + 1], gathered)
        result.append(
            lax.dot_general(
                pick, gathered, (((1,), (1,)), ((), ())),
                precision=lax.Precision.HIGHEST, preferred_element_type=jnp.float32,
            )
        )
    return result[0], result[1]


def edge_kernel(block_ref, xl_ref, xh_ref, yl_ref, yh_ref, *copy_ref):
    block = block_ref[...]
    if copy_ref:
        copy_ref[0][...] = block
    block = block.astype(jnp.float32)
    store_x_rows(xl_ref, block[:, :1, :])
    store_x_rows(xh_ref, block[:, -1:, :])
    yl_ref[...], yh_ref[...] = to_rows(block)


def block_edges(block, keep=False):
    depth, nx, ny = block.shape
    tz = EDGE_Z
    f32 = jnp.float32
    whole = pl.BlockSpec((tz, nx, ny), lambda c: (c, 0, 0))
    row = pl.BlockSpec((tz, ny), lambda c: (c, 0))
    col = pl.BlockSpec((tz, nx), lambda c: (c, 0))
    out_shape = [
        jax.ShapeDtypeStruct((depth, ny), f32),
        jax.ShapeDtypeStruct((depth, ny), f32),
        jax.ShapeDtypeStruct((depth, nx), f32),
        jax.ShapeDtypeStruct((depth, nx), f32),
    ]
    out_specs = [row, row, col, col]
    if keep:
        out_shape.append(jax.ShapeDtypeStruct(block.shape, block.dtype))
        out_specs.append(whole)
    return pl.pallas_call(
        edge_kernel,
        out_shape=tuple(out_shape),
        grid=(depth // tz,),
        in_specs=[whole],
        out_specs=out_specs,
        compiler_params=pltpu.CompilerParams(dimension_semantics=("arbitrary",)),
    )(block)


def update(trans, pm_ref, pb_ref, pa_ref, qxl_ref, qxh_ref, qyl_ref, qyh_ref, f_ref, outs):
    o_ref, exl_ref, exh_ref, eyl_ref, eyh_ref = outs
    t_zp, t_zm, t_xp, t_xm, t_yp, t_ym = trans
    tz, nx, ny = pm_ref.shape
    f32 = jnp.float32
    xi = lax.broadcasted_iota(jnp.int32, (tz, nx, ny), 1)
    yi = lax.broadcasted_iota(jnp.int32, (tz, nx, ny), 2)
    p = pm_ref[...].astype(f32)
    pext = jnp.concatenate([pb_ref[...].astype(f32), p, pa_ref[...].astype(f32)], axis=0)
    n_xp = jnp.where(xi == nx - 1, x_rows(qxh_ref), pltpu.roll(p, nx - 1, 1))
    n_xm = jnp.where(xi == 0, x_rows(qxl_ref), pltpu.roll(p, 1, 1))
    n_yp = jnp.where(yi == ny - 1, to_columns(qyh_ref[...]), pltpu.roll(p, ny - 1, 2))
    n_ym = jnp.where(yi == 0, to_columns(qyl_ref[...]), pltpu.roll(p, 1, 2))

    flux = t_zp * (pext[2:] - p)
    flux = flux + t_zm * (pext[:-2] - p)
    flux = flux + t_xp * (n_xp - p)
    flux = flux + t_xm * (n_xm - p)
    flux = flux + t_yp * (n_yp - p)
    flux = flux + t_ym * (n_ym - p)
    new = p + STEP_SIZE * (flux + f_ref[...]) / (1.0 + 0.5 * p * p)
    o_ref[...] = new
    store_x_rows(exl_ref, new[:, :1, :])
    store_x_rows(exh_ref, new[:, nx - 1 :, :])
    eyl_ref[...], eyh_ref[...] = to_rows(new)


def first_step_kernel(
    inside_ref, lpm_ref, lpb_ref, lpa_ref, lxl_ref, lxh_ref, lyl_ref, lyh_ref,
    pm_ref, pb_ref, pa_ref, qxl_ref, qxh_ref, qyl_ref, qyh_ref, f_ref,
    o_ref, exl_ref, exh_ref, eyl_ref, eyh_ref, tzm_ref, txm_ref, tym_ref, txp_ref, typ_ref,
):
    c = pl.program_id(0)
    last = pl.num_programs(0) - 1
    tz, nx, ny = pm_ref.shape
    f32 = jnp.float32

    def side_perm(ref, k):
        return jnp.where(inside_ref[k] > 0, permeability(ref[...].astype(f32)), 0.0)

    kxl = jnp.where(inside_ref[0] > 0, permeability(x_rows(lxl_ref)), 0.0)
    kxh = jnp.where(inside_ref[1] > 0, permeability(x_rows(lxh_ref)), 0.0)
    kyl = to_columns(side_perm(lyl_ref, 2))
    kyh = to_columns(side_perm(lyh_ref, 3))

    below = jnp.where(c == 0, 0.0, permeability(lpb_ref[...].astype(f32)))
    above = jnp.where(c == last, 0.0, permeability(lpa_ref[...].astype(f32)))
    centre = permeability(lpm_ref[...].astype(f32))
    ext = jnp.concatenate([below, centre, above], axis=0)
    faces = harmonic(ext[:-1], ext[1:])
    t_zm = faces[:-1]
    t_zp = faces[1:]

    xi = lax.broadcasted_iota(jnp.int32, (tz, nx, ny), 1)
    yi = lax.broadcasted_iota(jnp.int32, (tz, nx, ny), 2)

    fx = harmonic(centre, pltpu.roll(centre, nx - 1, 1))
    t_xp = jnp.where(xi == nx - 1, harmonic(centre[:, nx - 1 :, :], kxh), fx)
    t_xm = jnp.where(xi == 0, harmonic(centre[:, :1, :], kxl), pltpu.roll(fx, 1, 1))
    fy = harmonic(centre, pltpu.roll(centre, ny - 1, 2))
    t_yp = jnp.where(yi == ny - 1, harmonic(centre[:, :, ny - 1 :], kyh), fy)
    t_ym = jnp.where(yi == 0, harmonic(centre[:, :, :1], kyl), pltpu.roll(fy, 1, 2))

    tzm_ref[...] = t_zm
    txm_ref[...] = t_xm
    tym_ref[...] = t_ym
    store_x_rows(txp_ref, t_xp[:, nx - 1 :, :])
    typ_ref[...] = to_rows(t_yp)[1]
    update(
        (t_zp, t_zm, t_xp, t_xm, t_yp, t_ym),
        pm_ref, pb_ref, pa_ref, qxl_ref, qxh_ref, qyl_ref, qyh_ref, f_ref,
        (o_ref, exl_ref, exh_ref, eyl_ref, eyh_ref),
    )


def later_step_kernel(
    tzm_ref, tza_ref, txm_ref, tym_ref, txp_ref, typ_ref,
    pm_ref, pb_ref, pa_ref, qxl_ref, qxh_ref, qyl_ref, qyh_ref, f_ref,
    o_ref, exl_ref, exh_ref, eyl_ref, eyh_ref,
):
    c = pl.program_id(0)
    last = pl.num_programs(0) - 1
    tz, nx, ny = pm_ref.shape
    xi = lax.broadcasted_iota(jnp.int32, (tz, nx, ny), 1)
    yi = lax.broadcasted_iota(jnp.int32, (tz, nx, ny), 2)
    t_zm = tzm_ref[...]
    t_zp = jnp.concatenate([t_zm[1:], jnp.where(c == last, 0.0, tza_ref[...])], axis=0)
    t_xm = txm_ref[...]
    t_xp = jnp.where(xi == nx - 1, x_rows(txp_ref), pltpu.roll(t_xm, nx - 1, 1))
    t_ym = tym_ref[...]
    t_yp = jnp.where(yi == ny - 1, to_columns(typ_ref[...]), pltpu.roll(t_ym, ny - 1, 2))
    update(
        (t_zp, t_zm, t_xp, t_xm, t_yp, t_ym),
        pm_ref, pb_ref, pa_ref, qxl_ref, qxh_ref, qyl_ref, qyh_ref, f_ref,
        (o_ref, exl_ref, exh_ref, eyl_ref, eyh_ref),
    )


def advance(stored, pressure, pressure_halos, flow, inside=None, log_perm=None, perm_halos=None):
    depth, nx, ny = pressure.shape
    tz = CHUNK_Z
    grid = (depth // tz,)
    main = pl.BlockSpec((tz, nx, ny), lambda c: (c, 0, 0))
    below = pl.BlockSpec((1, nx, ny), lambda c: (jnp.maximum(c * tz - 1, 0), 0, 0))
    above = pl.BlockSpec((1, nx, ny), lambda c: (jnp.minimum(c * tz + tz, depth - 1), 0, 0))
    row = pl.BlockSpec((tz, ny), lambda c: (c, 0))
    col = pl.BlockSpec((tz, nx), lambda c: (c, 0))
    side = [row, row, col, col]
    smem = pl.BlockSpec(memory_space=pltpu.SMEM)
    f32 = jnp.float32
    full = jax.ShapeDtypeStruct((depth, nx, ny), f32)
    rows = jax.ShapeDtypeStruct((depth, ny), f32)
    cols = jax.ShapeDtypeStruct((depth, nx), f32)
    out_shape = [full, rows, rows, cols, cols]
    out_specs = [main] + side
    pressure_args = [pressure, pressure, pressure, *pressure_halos, flow]
    pressure_specs = [main, below, above] + side + [main]
    params = pltpu.CompilerParams(dimension_semantics=("arbitrary",))
    if stored is None:
        outs = pl.pallas_call(
            first_step_kernel,
            out_shape=tuple(out_shape + [full, full, full, rows, cols]),
            grid=grid,
            in_specs=[smem, main, below, above] + side + pressure_specs,
            out_specs=out_specs + [main, main, main, row, col],
            compiler_params=params,
        )(inside, log_perm, log_perm, log_perm, *perm_halos, *pressure_args)
        return outs[0], outs[1:5], outs[5:]
    t_zm, t_xm, t_ym, t_xp, t_yp = stored
    outs = pl.pallas_call(
        later_step_kernel,
        out_shape=tuple(out_shape),
        grid=grid,
        in_specs=[main, above, main, main, row, col] + pressure_specs,
        out_specs=out_specs,
        compiler_params=params,
    )(t_zm, t_zm, t_xm, t_ym, t_xp, t_yp, *pressure_args)
    return outs[0], outs[1:5], stored


def depth_kernel(rz_ref, n_ref, o_ref):
    rz = rz_ref[...]
    for i in range(n_ref.shape[1]):
        o_ref[:, i, :] = jnp.dot(rz, n_ref[:, i, :], preferred_element_type=jnp.float32).astype(
            jnp.bfloat16
        )


def depth_transform(root_z, noise):
    depth, nx, ny = noise.shape
    bx = min(nx, DEPTH_X)
    block = pl.BlockSpec((depth, bx, ny), lambda i: (0, i, 0))
    return pl.pallas_call(
        depth_kernel,
        out_shape=jax.ShapeDtypeStruct(noise.shape, jnp.bfloat16),
        grid=(nx // bx,),
        in_specs=[pl.BlockSpec(root_z.shape, lambda i: (0, 0)), block],
        out_specs=block,
        compiler_params=pltpu.CompilerParams(dimension_semantics=("arbitrary",)),
    )(root_z, noise)


def line_kernel(g_ref, rx_ref, ry_ref, o_ref, *, count_w, count_n):
    f32 = jnp.float32
    nx = g_ref.shape[2]
    ny = g_ref.shape[3]
    rx = rx_ref[...]
    halves = []
    for n in range(count_n):
        lines = jnp.concatenate([g_ref[w * count_n + n, 0] for w in range(count_w)], axis=0)
        halves.append(jnp.dot(rx, lines, preferred_element_type=f32).astype(jnp.bfloat16))
    second = jnp.concatenate(halves, axis=1)
    third = lax.dot_general(
        second, ry_ref[...], (((1,), (1,)), ((), ())), preferred_element_type=f32
    ).astype(jnp.bfloat16)
    for w in range(count_w):
        for n in range(count_n):
            o_ref[w * count_n + n, 0] = third[w * nx : (w + 1) * nx, n * ny : (n + 1) * ny]


def line_transforms(gathered, root_x, root_y, count_w, count_n):
    groups, planes, nx, ny = gathered.shape
    block = pl.BlockSpec((groups, 1, nx, ny), lambda z: (0, z, 0, 0))
    whole_x = pl.BlockSpec(root_x.shape, lambda z: (0, 0))
    whole_y = pl.BlockSpec(root_y.shape, lambda z: (0, 0))
    return pl.pallas_call(
        functools.partial(line_kernel, count_w=count_w, count_n=count_n),
        out_shape=jax.ShapeDtypeStruct(gathered.shape, jnp.bfloat16),
        grid=(planes,),
        in_specs=[block, whole_x, whole_y],
        out_specs=block,
        compiler_params=pltpu.CompilerParams(dimension_semantics=("arbitrary",)),
    )(gathered, root_x, root_y)


def body(noise, root_z, root_x, root_y, pressure_start, well_x, well_y, well_z, well_rate):
    depth, rows_x, rows_y = noise.shape
    first = depth_transform(root_z, noise)
    count_w = lax.axis_size("wide")
    count_n = lax.axis_size("narrow")
    groups = count_w * count_n
    planes = depth // groups
    gathered = lax.all_to_all(
        first.reshape(groups, planes, rows_x, rows_y),
        ("wide", "narrow"), split_axis=0, concat_axis=0, tiled=True,
    )
    outgoing = line_transforms(gathered, root_x, root_y, count_w, count_n)
    log_perm = lax.all_to_all(
        outgoing, ("wide", "narrow"), split_axis=0, concat_axis=0, tiled=True,
    ).reshape(depth, rows_x, rows_y)

    wide_at = lax.axis_index("wide")
    narrow_at = lax.axis_index("narrow")
    last_w = lax.axis_size("wide") - 1
    last_n = lax.axis_size("narrow") - 1

    local_x = well_x - wide_at * rows_x
    local_y = well_y - narrow_at * rows_y
    valid = (local_x >= 0) & (local_x < rows_x) & (local_y >= 0) & (local_y < rows_y)
    rates = jnp.where(valid, well_rate, 0.0).astype(jnp.float32)
    wells = well_x.shape[0]
    cells = well_z * rows_x + local_x
    pick_rows = jnp.where(
        lax.broadcasted_iota(jnp.int32, (depth * rows_x, wells), 0) == cells[None, :],
        rates[None, :],
        0.0,
    )
    pick_cols = (
        lax.broadcasted_iota(jnp.int32, (wells, rows_y), 1) == local_y[:, None]
    ).astype(jnp.float32)
    flow = jnp.dot(
        pick_rows, pick_cols, precision=lax.Precision.HIGHEST, preferred_element_type=jnp.float32
    ).reshape(depth, rows_x, rows_y)

    inside = jnp.stack(
        [wide_at > 0, wide_at < last_w, narrow_at > 0, narrow_at < last_n]
    ).astype(jnp.int32)
    edges = block_edges(pressure_start)
    flow, edges = lax.optimization_barrier((flow, edges))
    *lp_edges, log_perm = block_edges(log_perm, keep=True)
    perm_halos = halos(lp_edges)
    pressure = pressure_start
    stored = None
    for step in range(STEPS):
        pressure, edges, stored = advance(
            stored, pressure, halos(edges), flow, inside, log_perm, perm_halos
        )
    return (log_perm, pressure)


def solution(mesh):
    in_specs = (
        P("member", "wide", "narrow"),
        P(),
        P(),
        P(),
        P("member", "wide", "narrow"),
        P("member"),
        P("member"),
        P("member"),
        P("member"),
    )
    out_specs = (P("member", "wide", "narrow"), P("member", "wide", "narrow"))
    return jax.shard_map(body, mesh=mesh, in_specs=in_specs, out_specs=out_specs, check_vma=False)
```

```python
import functools

import jax
import jax.numpy as jnp
from jax import lax
from jax.experimental import pallas as pl
from jax.experimental.pallas import tpu as pltpu
from jax.sharding import PartitionSpec as P

STEPS = 2


STEP_SIZE = 0.03
CAP_LOG = 1.5
CHUNK_Z = 16
EDGE_Z = 32
DEPTH_X = 32


def permeability(values):
    return jnp.exp(CAP_LOG * jnp.tanh(values / CAP_LOG))


def harmonic(a, b):
    return 2.0 * a * b / (a + b)


def halos(edges):
    forward_w = [(i, i + 1) for i in range(lax.axis_size("wide") - 1)]
    backward_w = [(j, i) for i, j in forward_w]
    forward_n = [(i, i + 1) for i in range(lax.axis_size("narrow") - 1)]
    backward_n = [(j, i) for i, j in forward_n]
    first_x, last_x, first_y, last_y = edges
    x_lo = lax.ppermute(last_x, "wide", forward_w)
    x_hi = lax.ppermute(first_x, "wide", backward_w)
    y_lo = lax.ppermute(last_y, "narrow", forward_n)
    y_hi = lax.ppermute(first_y, "narrow", backward_n)
    return x_lo, x_hi, y_lo, y_hi


def to_columns(rows):
    tz, nx = rows.shape
    eye = jnp.where(
        lax.broadcasted_iota(jnp.int32, (nx, nx), 0) == lax.broadcasted_iota(jnp.int32, (nx, nx), 1),
        1.0, 0.0,
    )
    cols = lax.dot_general(
        eye, rows, (((1,), (1,)), ((), ())),
        precision=lax.Precision.HIGHEST, preferred_element_type=jnp.float32,
    )
    return jnp.concatenate([cols[:, k : k + 1][None] for k in range(tz)], axis=0)


def x_rows(ref):
    return jnp.concatenate([ref[k : k + 1, :][None] for k in range(ref.shape[0])], axis=0)


def store_x_rows(ref, rows):
    for k in range(ref.shape[0]):
        ref[k : k + 1, :] = rows[k]


def to_rows(block):
    tz, nx, ny = block.shape
    lane = lax.broadcasted_iota(jnp.int32, (nx, 128), 1)
    pick = jnp.where(
        lax.broadcasted_iota(jnp.int32, (tz, 128), 0) == lax.broadcasted_iota(jnp.int32, (tz, 128), 1),
        1.0, 0.0,
    )
    result = []
    for column in (0, ny - 1):
        gathered = jnp.zeros((nx, 128), jnp.float32)
        for k in range(tz):
            gathered = jnp.where(lane == k, block[k, :, column : column + 1], gathered)
        result.append(
            lax.dot_general(
                pick, gathered, (((1,), (1,)), ((), ())),
                precision=lax.Precision.HIGHEST, preferred_element_type=jnp.float32,
            )
        )
    return result[0], result[1]


def edge_kernel(block_ref, xl_ref, xh_ref, yl_ref, yh_ref, *copy_ref):
    block = block_ref[...]
    if copy_ref:
        copy_ref[0][...] = block
    block = block.astype(jnp.float32)
    store_x_rows(xl_ref, block[:, :1, :])
    store_x_rows(xh_ref, block[:, -1:, :])
    yl_ref[...], yh_ref[...] = to_rows(block)


def block_edges(block, keep=False):
    depth, nx, ny = block.shape
    tz = EDGE_Z
    f32 = jnp.float32
    whole = pl.BlockSpec((tz, nx, ny), lambda c: (c, 0, 0))
    row = pl.BlockSpec((tz, ny), lambda c: (c, 0))
    col = pl.BlockSpec((tz, nx), lambda c: (c, 0))
    out_shape = [
        jax.ShapeDtypeStruct((depth, ny), f32),
        jax.ShapeDtypeStruct((depth, ny), f32),
        jax.ShapeDtypeStruct((depth, nx), f32),
        jax.ShapeDtypeStruct((depth, nx), f32),
    ]
    out_specs = [row, row, col, col]
    if keep:
        out_shape.append(jax.ShapeDtypeStruct(block.shape, block.dtype))
        out_specs.append(whole)
    return pl.pallas_call(
        edge_kernel,
        out_shape=tuple(out_shape),
        grid=(depth // tz,),
        in_specs=[whole],
        out_specs=out_specs,
        compiler_params=pltpu.CompilerParams(dimension_semantics=("arbitrary",)),
    )(block)


def update(trans, pm_ref, pb_ref, pa_ref, qxl_ref, qxh_ref, qyl_ref, qyh_ref, f_ref, outs):
    o_ref, exl_ref, exh_ref, eyl_ref, eyh_ref = outs
    t_zp, t_zm, t_xp, t_xm, t_yp, t_ym = trans
    tz, nx, ny = pm_ref.shape
    f32 = jnp.float32
    xi = lax.broadcasted_iota(jnp.int32, (tz, nx, ny), 1)
    yi = lax.broadcasted_iota(jnp.int32, (tz, nx, ny), 2)
    p = pm_ref[...].astype(f32)
    pext = jnp.concatenate([pb_ref[...].astype(f32), p, pa_ref[...].astype(f32)], axis=0)
    n_xp = jnp.where(xi == nx - 1, x_rows(qxh_ref), pltpu.roll(p, nx - 1, 1))
    n_xm = jnp.where(xi == 0, x_rows(qxl_ref), pltpu.roll(p, 1, 1))
    n_yp = jnp.where(yi == ny - 1, to_columns(qyh_ref[...]), pltpu.roll(p, ny - 1, 2))
    n_ym = jnp.where(yi == 0, to_columns(qyl_ref[...]), pltpu.roll(p, 1, 2))

    flux = t_zp * (pext[2:] - p)
    flux = flux + t_zm * (pext[:-2] - p)
    flux = flux + t_xp * (n_xp - p)
    flux = flux + t_xm * (n_xm - p)
    flux = flux + t_yp * (n_yp - p)
    flux = flux + t_ym * (n_ym - p)
    new = p + STEP_SIZE * (flux + f_ref[...]) / (1.0 + 0.5 * p * p)
    o_ref[...] = new
    store_x_rows(exl_ref, new[:, :1, :])
    store_x_rows(exh_ref, new[:, nx - 1 :, :])
    eyl_ref[...], eyh_ref[...] = to_rows(new)


def first_step_kernel(
    inside_ref, lpm_ref, lpb_ref, lpa_ref, lxl_ref, lxh_ref, lyl_ref, lyh_ref,
    pm_ref, pb_ref, pa_ref, qxl_ref, qxh_ref, qyl_ref, qyh_ref, f_ref,
    o_ref, exl_ref, exh_ref, eyl_ref, eyh_ref, tzm_ref, txm_ref, tym_ref, txp_ref, typ_ref,
):
    c = pl.program_id(0)
    last = pl.num_programs(0) - 1
    tz, nx, ny = pm_ref.shape
    f32 = jnp.float32

    def side_perm(ref, k):
        return jnp.where(inside_ref[k] > 0, permeability(ref[...].astype(f32)), 0.0)

    kxl = jnp.where(inside_ref[0] > 0, permeability(x_rows(lxl_ref)), 0.0)
    kxh = jnp.where(inside_ref[1] > 0, permeability(x_rows(lxh_ref)), 0.0)
    kyl = to_columns(side_perm(lyl_ref, 2))
    kyh = to_columns(side_perm(lyh_ref, 3))

    below = jnp.where(c == 0, 0.0, permeability(lpb_ref[...].astype(f32)))
    above = jnp.where(c == last, 0.0, permeability(lpa_ref[...].astype(f32)))
    centre = permeability(lpm_ref[...].astype(f32))
    ext = jnp.concatenate([below, centre, above], axis=0)
    faces = harmonic(ext[:-1], ext[1:])
    t_zm = faces[:-1]
    t_zp = faces[1:]

    xi = lax.broadcasted_iota(jnp.int32, (tz, nx, ny), 1)
    yi = lax.broadcasted_iota(jnp.int32, (tz, nx, ny), 2)

    fx = harmonic(centre, pltpu.roll(centre, nx - 1, 1))
    t_xp = jnp.where(xi == nx - 1, harmonic(centre[:, nx - 1 :, :], kxh), fx)
    t_xm = jnp.where(xi == 0, harmonic(centre[:, :1, :], kxl), pltpu.roll(fx, 1, 1))
    fy = harmonic(centre, pltpu.roll(centre, ny - 1, 2))
    t_yp = jnp.where(yi == ny - 1, harmonic(centre[:, :, ny - 1 :], kyh), fy)
    t_ym = jnp.where(yi == 0, harmonic(centre[:, :, :1], kyl), pltpu.roll(fy, 1, 2))

    tzm_ref[...] = t_zm
    txm_ref[...] = t_xm
    tym_ref[...] = t_ym
    store_x_rows(txp_ref, t_xp[:, nx - 1 :, :])
    typ_ref[...] = to_rows(t_yp)[1]
    update(
        (t_zp, t_zm, t_xp, t_xm, t_yp, t_ym),
        pm_ref, pb_ref, pa_ref, qxl_ref, qxh_ref, qyl_ref, qyh_ref, f_ref,
        (o_ref, exl_ref, exh_ref, eyl_ref, eyh_ref),
    )


def later_step_kernel(
    tzm_ref, tza_ref, txm_ref, tym_ref, txp_ref, typ_ref,
    pm_ref, pb_ref, pa_ref, qxl_ref, qxh_ref, qyl_ref, qyh_ref, f_ref,
    o_ref, exl_ref, exh_ref, eyl_ref, eyh_ref,
):
    c = pl.program_id(0)
    last = pl.num_programs(0) - 1
    tz, nx, ny = pm_ref.shape
    xi = lax.broadcasted_iota(jnp.int32, (tz, nx, ny), 1)
    yi = lax.broadcasted_iota(jnp.int32, (tz, nx, ny), 2)
    t_zm = tzm_ref[...]
    t_zp = jnp.concatenate([t_zm[1:], jnp.where(c == last, 0.0, tza_ref[...])], axis=0)
    t_xm = txm_ref[...]
    t_xp = jnp.where(xi == nx - 1, x_rows(txp_ref), pltpu.roll(t_xm, nx - 1, 1))
    t_ym = tym_ref[...]
    t_yp = jnp.where(yi == ny - 1, to_columns(typ_ref[...]), pltpu.roll(t_ym, ny - 1, 2))
    update(
        (t_zp, t_zm, t_xp, t_xm, t_yp, t_ym),
        pm_ref, pb_ref, pa_ref, qxl_ref, qxh_ref, qyl_ref, qyh_ref, f_ref,
        (o_ref, exl_ref, exh_ref, eyl_ref, eyh_ref),
    )


def advance(stored, pressure, pressure_halos, flow, inside=None, log_perm=None, perm_halos=None):
    depth, nx, ny = pressure.shape
    tz = CHUNK_Z
    grid = (depth // tz,)
    main = pl.BlockSpec((tz, nx, ny), lambda c: (c, 0, 0))
    below = pl.BlockSpec((1, nx, ny), lambda c: (jnp.maximum(c * tz - 1, 0), 0, 0))
    above = pl.BlockSpec((1, nx, ny), lambda c: (jnp.minimum(c * tz + tz, depth - 1), 0, 0))
    row = pl.BlockSpec((tz, ny), lambda c: (c, 0))
    col = pl.BlockSpec((tz, nx), lambda c: (c, 0))
    side = [row, row, col, col]
    smem = pl.BlockSpec(memory_space=pltpu.SMEM)
    f32 = jnp.float32
    full = jax.ShapeDtypeStruct((depth, nx, ny), f32)
    rows = jax.ShapeDtypeStruct((depth, ny), f32)
    cols = jax.ShapeDtypeStruct((depth, nx), f32)
    out_shape = [full, rows, rows, cols, cols]
    out_specs = [main] + side
    pressure_args = [pressure, pressure, pressure, *pressure_halos, flow]
    pressure_specs = [main, below, above] + side + [main]
    params = pltpu.CompilerParams(dimension_semantics=("arbitrary",))
    if stored is None:
        outs = pl.pallas_call(
            first_step_kernel,
            out_shape=tuple(out_shape + [full, full, full, rows, cols]),
            grid=grid,
            in_specs=[smem, main, below, above] + side + pressure_specs,
            out_specs=out_specs + [main, main, main, row, col],
            compiler_params=params,
        )(inside, log_perm, log_perm, log_perm, *perm_halos, *pressure_args)
        return outs[0], outs[1:5], outs[5:]
    t_zm, t_xm, t_ym, t_xp, t_yp = stored
    outs = pl.pallas_call(
        later_step_kernel,
        out_shape=tuple(out_shape),
        grid=grid,
        in_specs=[main, above, main, main, row, col] + pressure_specs,
        out_specs=out_specs,
        compiler_params=params,
    )(t_zm, t_zm, t_xm, t_ym, t_xp, t_yp, *pressure_args)
    return outs[0], outs[1:5], stored


def depth_kernel(rz_ref, n_ref, o_ref):
    rz = rz_ref[...]
    for i in range(n_ref.shape[1]):
        o_ref[:, i, :] = jnp.dot(rz, n_ref[:, i, :], preferred_element_type=jnp.float32).astype(
            jnp.bfloat16
        )


def depth_transform(root_z, noise):
    depth, nx, ny = noise.shape
    bx = min(nx, DEPTH_X)
    block = pl.BlockSpec((depth, bx, ny), lambda i: (0, i, 0))
    return pl.pallas_call(
        depth_kernel,
        out_shape=jax.ShapeDtypeStruct(noise.shape, jnp.bfloat16),
        grid=(nx // bx,),
        in_specs=[pl.BlockSpec(root_z.shape, lambda i: (0, 0)), block],
        out_specs=block,
        compiler_params=pltpu.CompilerParams(dimension_semantics=("arbitrary",)),
    )(root_z, noise)


def line_kernel(g_ref, rx_ref, ry_ref, o_ref, *, count_w, count_n):
    f32 = jnp.float32
    nx = g_ref.shape[2]
    ny = g_ref.shape[3]
    rx = rx_ref[...]
    halves = []
    for n in range(count_n):
        lines = jnp.concatenate([g_ref[w * count_n + n, 0] for w in range(count_w)], axis=0)
        halves.append(jnp.dot(rx, lines, preferred_element_type=f32).astype(jnp.bfloat16))
    second = jnp.concatenate(halves, axis=1)
    third = lax.dot_general(
        second, ry_ref[...], (((1,), (1,)), ((), ())), preferred_element_type=f32
    ).astype(jnp.bfloat16)
    for w in range(count_w):
        for n in range(count_n):
            o_ref[w * count_n + n, 0] = third[w * nx : (w + 1) * nx, n * ny : (n + 1) * ny]


def line_transforms(gathered, root_x, root_y, count_w, count_n):
    groups, planes, nx, ny = gathered.shape
    block = pl.BlockSpec((groups, 1, nx, ny), lambda z: (0, z, 0, 0))
    whole_x = pl.BlockSpec(root_x.shape, lambda z: (0, 0))
    whole_y = pl.BlockSpec(root_y.shape, lambda z: (0, 0))
    return pl.pallas_call(
        functools.partial(line_kernel, count_w=count_w, count_n=count_n),
        out_shape=jax.ShapeDtypeStruct(gathered.shape, jnp.bfloat16),
        grid=(planes,),
        in_specs=[block, whole_x, whole_y],
        out_specs=block,
        compiler_params=pltpu.CompilerParams(dimension_semantics=("arbitrary",)),
    )(gathered, root_x, root_y)


def body(noise, root_z, root_x, root_y, pressure_start, well_x, well_y, well_z, well_rate):
    depth, rows_x, rows_y = noise.shape
    first = depth_transform(root_z, noise)
    count_w = lax.axis_size("wide")
    count_n = lax.axis_size("narrow")
    groups = count_w * count_n
    planes = depth // groups
    gathered = lax.all_to_all(
        first.reshape(groups, planes, rows_x, rows_y),
        ("wide", "narrow"), split_axis=0, concat_axis=0, tiled=True,
    )
    outgoing = line_transforms(gathered, root_x, root_y, count_w, count_n)
    log_perm = lax.all_to_all(
        outgoing, ("wide", "narrow"), split_axis=0, concat_axis=0, tiled=True,
    ).reshape(depth, rows_x, rows_y)

    wide_at = lax.axis_index("wide")
    narrow_at = lax.axis_index("narrow")
    last_w = lax.axis_size("wide") - 1
    last_n = lax.axis_size("narrow") - 1

    local_x = well_x - wide_at * rows_x
    local_y = well_y - narrow_at * rows_y
    valid = (local_x >= 0) & (local_x < rows_x) & (local_y >= 0) & (local_y < rows_y)
    rates = jnp.where(valid, well_rate, 0.0).astype(jnp.float32)
    wells = well_x.shape[0]
    cells = well_z * rows_x + local_x
    pick_rows = jnp.where(
        lax.broadcasted_iota(jnp.int32, (depth * rows_x, wells), 0) == cells[None, :],
        rates[None, :],
        0.0,
    )
    pick_cols = (
        lax.broadcasted_iota(jnp.int32, (wells, rows_y), 1) == local_y[:, None]
    ).astype(jnp.float32)
    flow = jnp.dot(
        pick_rows, pick_cols, precision=lax.Precision.HIGHEST, preferred_element_type=jnp.float32
    ).reshape(depth, rows_x, rows_y)

    inside = jnp.stack(
        [wide_at > 0, wide_at < last_w, narrow_at > 0, narrow_at < last_n]
    ).astype(jnp.int32)
    edges = block_edges(pressure_start)
    flow, edges = lax.optimization_barrier((flow, edges))
    *lp_edges, log_perm = block_edges(log_perm, keep=True)
    perm_halos = halos(lp_edges)
    pressure = pressure_start
    stored = None
    for step in range(STEPS):
        pressure, edges, stored = advance(
            stored, pressure, halos(edges), flow, inside, log_perm, perm_halos
        )
    return (log_perm, pressure)


def solution(mesh):
    in_specs = (
        P("member", "wide", "narrow"),
        P(),
        P(),
        P(),
        P("member", "wide", "narrow"),
        P("member"),
        P("member"),
        P("member"),
        P("member"),
    )
    out_specs = (P("member", "wide", "narrow"), P("member", "wide", "narrow"))
    return jax.shard_map(body, mesh=mesh, in_specs=in_specs, out_specs=out_specs, check_vma=False)
```

```python
import functools

import jax
import jax.numpy as jnp
from jax import lax
from jax.experimental import pallas as pl
from jax.experimental.pallas import tpu as pltpu
from jax.sharding import PartitionSpec as P

STEPS = 2


STEP_SIZE = 0.03
CAP_LOG = 1.5
CHUNK_Z = 16
EDGE_Z = 32
DEPTH_X = 16


def permeability(values):
    return jnp.exp(CAP_LOG * jnp.tanh(values / CAP_LOG))


def harmonic(a, b):
    return 2.0 * a * b / (a + b)


def halos(edges):
    forward_w = [(i, i + 1) for i in range(lax.axis_size("wide") - 1)]
    backward_w = [(j, i) for i, j in forward_w]
    forward_n = [(i, i + 1) for i in range(lax.axis_size("narrow") - 1)]
    backward_n = [(j, i) for i, j in forward_n]
    first_x, last_x, first_y, last_y = edges
    x_lo = lax.ppermute(last_x, "wide", forward_w)
    x_hi = lax.ppermute(first_x, "wide", backward_w)
    y_lo = lax.ppermute(last_y, "narrow", forward_n)
    y_hi = lax.ppermute(first_y, "narrow", backward_n)
    return x_lo, x_hi, y_lo, y_hi


def to_columns(rows):
    tz, nx = rows.shape
    eye = jnp.where(
        lax.broadcasted_iota(jnp.int32, (nx, nx), 0) == lax.broadcasted_iota(jnp.int32, (nx, nx), 1),
        1.0, 0.0,
    )
    cols = lax.dot_general(
        eye, rows, (((1,), (1,)), ((), ())),
        precision=lax.Precision.HIGHEST, preferred_element_type=jnp.float32,
    )
    return jnp.concatenate([cols[:, k : k + 1][None] for k in range(tz)], axis=0)


def x_rows(ref):
    return jnp.concatenate([ref[k : k + 1, :][None] for k in range(ref.shape[0])], axis=0)


def store_x_rows(ref, rows):
    for k in range(ref.shape[0]):
        ref[k : k + 1, :] = rows[k]


def to_rows(block):
    tz, nx, ny = block.shape
    lane = lax.broadcasted_iota(jnp.int32, (nx, 128), 1)
    pick = jnp.where(
        lax.broadcasted_iota(jnp.int32, (tz, 128), 0) == lax.broadcasted_iota(jnp.int32, (tz, 128), 1),
        1.0, 0.0,
    )
    result = []
    for column in (0, ny - 1):
        gathered = jnp.zeros((nx, 128), jnp.float32)
        for k in range(tz):
            gathered = jnp.where(lane == k, block[k, :, column : column + 1], gathered)
        result.append(
            lax.dot_general(
                pick, gathered, (((1,), (1,)), ((), ())),
                precision=lax.Precision.HIGHEST, preferred_element_type=jnp.float32,
            )
        )
    return result[0], result[1]


def edge_kernel(block_ref, xl_ref, xh_ref, yl_ref, yh_ref, *copy_ref):
    block = block_ref[...]
    if copy_ref:
        copy_ref[0][...] = block
    block = block.astype(jnp.float32)
    store_x_rows(xl_ref, block[:, :1, :])
    store_x_rows(xh_ref, block[:, -1:, :])
    yl_ref[...], yh_ref[...] = to_rows(block)


def block_edges(block, keep=False):
    depth, nx, ny = block.shape
    tz = EDGE_Z
    f32 = jnp.float32
    whole = pl.BlockSpec((tz, nx, ny), lambda c: (c, 0, 0))
    row = pl.BlockSpec((tz, ny), lambda c: (c, 0))
    col = pl.BlockSpec((tz, nx), lambda c: (c, 0))
    out_shape = [
        jax.ShapeDtypeStruct((depth, ny), f32),
        jax.ShapeDtypeStruct((depth, ny), f32),
        jax.ShapeDtypeStruct((depth, nx), f32),
        jax.ShapeDtypeStruct((depth, nx), f32),
    ]
    out_specs = [row, row, col, col]
    if keep:
        out_shape.append(jax.ShapeDtypeStruct(block.shape, block.dtype))
        out_specs.append(whole)
    return pl.pallas_call(
        edge_kernel,
        out_shape=tuple(out_shape),
        grid=(depth // tz,),
        in_specs=[whole],
        out_specs=out_specs,
        compiler_params=pltpu.CompilerParams(dimension_semantics=("arbitrary",)),
    )(block)


def update(trans, pm_ref, pb_ref, pa_ref, qxl_ref, qxh_ref, qyl_ref, qyh_ref, f_ref, outs):
    o_ref, exl_ref, exh_ref, eyl_ref, eyh_ref = outs
    t_zp, t_zm, t_xp, t_xm, t_yp, t_ym = trans
    tz, nx, ny = pm_ref.shape
    f32 = jnp.float32
    xi = lax.broadcasted_iota(jnp.int32, (tz, nx, ny), 1)
    yi = lax.broadcasted_iota(jnp.int32, (tz, nx, ny), 2)
    p = pm_ref[...].astype(f32)
    pext = jnp.concatenate([pb_ref[...].astype(f32), p, pa_ref[...].astype(f32)], axis=0)
    n_xp = jnp.where(xi == nx - 1, x_rows(qxh_ref), pltpu.roll(p, nx - 1, 1))
    n_xm = jnp.where(xi == 0, x_rows(qxl_ref), pltpu.roll(p, 1, 1))
    n_yp = jnp.where(yi == ny - 1, to_columns(qyh_ref[...]), pltpu.roll(p, ny - 1, 2))
    n_ym = jnp.where(yi == 0, to_columns(qyl_ref[...]), pltpu.roll(p, 1, 2))

    flux = t_zp * (pext[2:] - p)
    flux = flux + t_zm * (pext[:-2] - p)
    flux = flux + t_xp * (n_xp - p)
    flux = flux + t_xm * (n_xm - p)
    flux = flux + t_yp * (n_yp - p)
    flux = flux + t_ym * (n_ym - p)
    new = p + STEP_SIZE * (flux + f_ref[...]) / (1.0 + 0.5 * p * p)
    o_ref[...] = new
    store_x_rows(exl_ref, new[:, :1, :])
    store_x_rows(exh_ref, new[:, nx - 1 :, :])
    eyl_ref[...], eyh_ref[...] = to_rows(new)


def first_step_kernel(
    inside_ref, lpm_ref, lpb_ref, lpa_ref, rim_ref,
    pm_ref, pb_ref, pa_ref, qxl_ref, qxh_ref, qyl_ref, qyh_ref, f_ref,
    o_ref, exl_ref, exh_ref, eyl_ref, eyh_ref, tzm_ref, txm_ref, tym_ref, txp_ref, typ_ref,
):
    c = pl.program_id(0)
    last = pl.num_programs(0) - 1
    tz, nx, ny = pm_ref.shape
    f32 = jnp.float32

    def side_perm(values, k):
        return jnp.where(inside_ref[k] > 0, permeability(values), 0.0)

    kxl = side_perm(rim_ref[:, 0:1, :], 0)
    kxh = side_perm(rim_ref[:, 1:2, :], 1)
    kyl = to_columns(side_perm(rim_ref[:, 2, 0:nx], 2))
    kyh = to_columns(side_perm(rim_ref[:, 3, 0:nx], 3))

    below = jnp.where(c == 0, 0.0, permeability(lpb_ref[...].astype(f32)))
    above = jnp.where(c == last, 0.0, permeability(lpa_ref[...].astype(f32)))
    centre = permeability(lpm_ref[...].astype(f32))
    ext = jnp.concatenate([below, centre, above], axis=0)
    faces = harmonic(ext[:-1], ext[1:])
    t_zm = faces[:-1]
    t_zp = faces[1:]

    xi = lax.broadcasted_iota(jnp.int32, (tz, nx, ny), 1)
    yi = lax.broadcasted_iota(jnp.int32, (tz, nx, ny), 2)

    fx = harmonic(centre, pltpu.roll(centre, nx - 1, 1))
    t_xp = jnp.where(xi == nx - 1, harmonic(centre[:, nx - 1 :, :], kxh), fx)
    t_xm = jnp.where(xi == 0, harmonic(centre[:, :1, :], kxl), pltpu.roll(fx, 1, 1))
    fy = harmonic(centre, pltpu.roll(centre, ny - 1, 2))
    t_yp = jnp.where(yi == ny - 1, harmonic(centre[:, :, ny - 1 :], kyh), fy)
    t_ym = jnp.where(yi == 0, harmonic(centre[:, :, :1], kyl), pltpu.roll(fy, 1, 2))

    tzm_ref[...] = t_zm
    txm_ref[...] = t_xm
    tym_ref[...] = t_ym
    store_x_rows(txp_ref, t_xp[:, nx - 1 :, :])
    typ_ref[...] = to_rows(t_yp)[1]
    update(
        (t_zp, t_zm, t_xp, t_xm, t_yp, t_ym),
        pm_ref, pb_ref, pa_ref, qxl_ref, qxh_ref, qyl_ref, qyh_ref, f_ref,
        (o_ref, exl_ref, exh_ref, eyl_ref, eyh_ref),
    )


def later_step_kernel(
    tzm_ref, tza_ref, txm_ref, tym_ref, txp_ref, typ_ref,
    pm_ref, pb_ref, pa_ref, qxl_ref, qxh_ref, qyl_ref, qyh_ref, f_ref,
    o_ref, exl_ref, exh_ref, eyl_ref, eyh_ref,
):
    c = pl.program_id(0)
    last = pl.num_programs(0) - 1
    tz, nx, ny = pm_ref.shape
    xi = lax.broadcasted_iota(jnp.int32, (tz, nx, ny), 1)
    yi = lax.broadcasted_iota(jnp.int32, (tz, nx, ny), 2)
    t_zm = tzm_ref[...]
    t_zp = jnp.concatenate([t_zm[1:], jnp.where(c == last, 0.0, tza_ref[...])], axis=0)
    t_xm = txm_ref[...]
    t_xp = jnp.where(xi == nx - 1, x_rows(txp_ref), pltpu.roll(t_xm, nx - 1, 1))
    t_ym = tym_ref[...]
    t_yp = jnp.where(yi == ny - 1, to_columns(typ_ref[...]), pltpu.roll(t_ym, ny - 1, 2))
    update(
        (t_zp, t_zm, t_xp, t_xm, t_yp, t_ym),
        pm_ref, pb_ref, pa_ref, qxl_ref, qxh_ref, qyl_ref, qyh_ref, f_ref,
        (o_ref, exl_ref, exh_ref, eyl_ref, eyh_ref),
    )


def advance(stored, pressure, pressure_halos, flow, inside=None, log_perm=None, rims=None):
    depth, nx, ny = pressure.shape
    tz = CHUNK_Z
    grid = (depth // tz,)
    main = pl.BlockSpec((tz, nx, ny), lambda c: (c, 0, 0))
    below = pl.BlockSpec((1, nx, ny), lambda c: (jnp.maximum(c * tz - 1, 0), 0, 0))
    above = pl.BlockSpec((1, nx, ny), lambda c: (jnp.minimum(c * tz + tz, depth - 1), 0, 0))
    row = pl.BlockSpec((tz, ny), lambda c: (c, 0))
    col = pl.BlockSpec((tz, nx), lambda c: (c, 0))
    side = [row, row, col, col]
    smem = pl.BlockSpec(memory_space=pltpu.SMEM)
    f32 = jnp.float32
    full = jax.ShapeDtypeStruct((depth, nx, ny), f32)
    rows = jax.ShapeDtypeStruct((depth, ny), f32)
    cols = jax.ShapeDtypeStruct((depth, nx), f32)
    out_shape = [full, rows, rows, cols, cols]
    out_specs = [main] + side
    pressure_args = [pressure, pressure, pressure, *pressure_halos, flow]
    pressure_specs = [main, below, above] + side + [main]
    params = pltpu.CompilerParams(dimension_semantics=("arbitrary",))
    if stored is None:
        outs = pl.pallas_call(
            first_step_kernel,
            out_shape=tuple(out_shape + [full, full, full, rows, cols]),
            grid=grid,
            in_specs=[smem, main, below, above, pl.BlockSpec((tz, 4, ny), lambda c: (c, 0, 0))]
            + pressure_specs,
            out_specs=out_specs + [main, main, main, row, col],
            compiler_params=params,
        )(inside, log_perm, log_perm, log_perm, rims, *pressure_args)
        return outs[0], outs[1:5], outs[5:]
    t_zm, t_xm, t_ym, t_xp, t_yp = stored
    outs = pl.pallas_call(
        later_step_kernel,
        out_shape=tuple(out_shape),
        grid=grid,
        in_specs=[main, above, main, main, row, col] + pressure_specs,
        out_specs=out_specs,
        compiler_params=params,
    )(t_zm, t_zm, t_xm, t_ym, t_xp, t_yp, *pressure_args)
    return outs[0], outs[1:5], stored


def depth_kernel(rz_ref, n_ref, o_ref):
    rz = rz_ref[...]
    for i in range(n_ref.shape[1]):
        o_ref[:, i, :] = jnp.dot(rz, n_ref[:, i, :], preferred_element_type=jnp.float32).astype(
            jnp.bfloat16
        )


def depth_transform(root_z, noise):
    depth, nx, ny = noise.shape
    bx = min(nx, DEPTH_X)
    block = pl.BlockSpec((depth, bx, ny), lambda i: (0, i, 0))
    return pl.pallas_call(
        depth_kernel,
        out_shape=jax.ShapeDtypeStruct(noise.shape, jnp.bfloat16),
        grid=(nx // bx,),
        in_specs=[pl.BlockSpec(root_z.shape, lambda i: (0, 0)), block],
        out_specs=block,
        compiler_params=pltpu.CompilerParams(dimension_semantics=("arbitrary",)),
    )(root_z, noise)


def line_kernel(g_ref, rx_ref, ry_ref, o_ref, h_ref, *, count_w, count_n):
    f32 = jnp.float32
    nx = g_ref.shape[2]
    ny = g_ref.shape[3]
    rx = rx_ref[...]
    halves = []
    for n in range(count_n):
        lines = jnp.concatenate([g_ref[w * count_n + n, 0] for w in range(count_w)], axis=0)
        halves.append(jnp.dot(rx, lines, preferred_element_type=f32).astype(jnp.bfloat16))
    second = jnp.concatenate(halves, axis=1)
    third = lax.dot_general(
        second, ry_ref[...], (((1,), (1,)), ((), ())), preferred_element_type=f32
    ).astype(jnp.bfloat16)
    for w in range(count_w):
        for n in range(count_n):
            o_ref[w * count_n + n, 0] = third[w * nx : (w + 1) * nx, n * ny : (n + 1) * ny]

    total_y = count_n * ny
    wanted = [n * ny - 1 if n > 0 else 0 for n in range(count_n)]
    wanted += [(n + 1) * ny if n < count_n - 1 else 0 for n in range(count_n)]
    picks = max(8, len(wanted))
    row = lax.broadcasted_iota(jnp.int32, (picks, total_y), 0)
    lane = lax.broadcasted_iota(jnp.int32, (picks, total_y), 1)
    sel = jnp.zeros((picks, total_y), jnp.bool_)
    for r, y in enumerate(wanted):
        sel = sel | ((row == r) & (lane == y))
    columns = lax.dot_general(
        jnp.where(sel, 1.0, 0.0).astype(jnp.bfloat16), third, (((1,), (1,)), ((), ())),
        preferred_element_type=f32,
    )
    h_ref[...] = jnp.zeros(h_ref.shape, f32)
    for w in range(count_w):
        for n in range(count_n):
            d = w * count_n + n
            ys = slice(n * ny, (n + 1) * ny)
            if w > 0:
                h_ref[d, 0, 0:1, :] = third[w * nx - 1 : w * nx, ys].astype(f32)
            if w < count_w - 1:
                h_ref[d, 0, 1:2, :] = third[(w + 1) * nx : (w + 1) * nx + 1, ys].astype(f32)
            if n > 0:
                h_ref[d, 0, 2:3, 0:nx] = columns[n : n + 1, w * nx : (w + 1) * nx]
            if n < count_n - 1:
                h_ref[d, 0, 3:4, 0:nx] = columns[count_n + n : count_n + n + 1, w * nx : (w + 1) * nx]


def line_transforms(gathered, root_x, root_y, count_w, count_n):
    groups, planes, nx, ny = gathered.shape
    block = pl.BlockSpec((groups, 1, nx, ny), lambda z: (0, z, 0, 0))
    whole_x = pl.BlockSpec(root_x.shape, lambda z: (0, 0))
    whole_y = pl.BlockSpec(root_y.shape, lambda z: (0, 0))
    rims = pl.BlockSpec((groups, 1, 4, ny), lambda z: (0, z, 0, 0))
    return pl.pallas_call(
        functools.partial(line_kernel, count_w=count_w, count_n=count_n),
        out_shape=(
            jax.ShapeDtypeStruct(gathered.shape, jnp.bfloat16),
            jax.ShapeDtypeStruct((groups, planes, 4, ny), jnp.float32),
        ),
        grid=(planes,),
        in_specs=[block, whole_x, whole_y],
        out_specs=(block, rims),
        compiler_params=pltpu.CompilerParams(dimension_semantics=("arbitrary",)),
    )(gathered, root_x, root_y)


def body(noise, root_z, root_x, root_y, pressure_start, well_x, well_y, well_z, well_rate):
    depth, rows_x, rows_y = noise.shape
    first = depth_transform(root_z, noise)
    count_w = lax.axis_size("wide")
    count_n = lax.axis_size("narrow")
    groups = count_w * count_n
    planes = depth // groups
    gathered = lax.all_to_all(
        first.reshape(groups, planes, rows_x, rows_y),
        ("wide", "narrow"), split_axis=0, concat_axis=0, tiled=True,
    )
    outgoing, rims = line_transforms(gathered, root_x, root_y, count_w, count_n)
    log_perm = lax.all_to_all(
        outgoing, ("wide", "narrow"), split_axis=0, concat_axis=0, tiled=True,
    ).reshape(depth, rows_x, rows_y)

    wide_at = lax.axis_index("wide")
    narrow_at = lax.axis_index("narrow")
    last_w = lax.axis_size("wide") - 1
    last_n = lax.axis_size("narrow") - 1

    local_x = well_x - wide_at * rows_x
    local_y = well_y - narrow_at * rows_y
    valid = (local_x >= 0) & (local_x < rows_x) & (local_y >= 0) & (local_y < rows_y)
    rates = jnp.where(valid, well_rate, 0.0).astype(jnp.float32)
    wells = well_x.shape[0]
    cells = well_z * rows_x + local_x
    pick_rows = jnp.where(
        lax.broadcasted_iota(jnp.int32, (depth * rows_x, wells), 0) == cells[None, :],
        rates[None, :],
        0.0,
    )
    pick_cols = (
        lax.broadcasted_iota(jnp.int32, (wells, rows_y), 1) == local_y[:, None]
    ).astype(jnp.float32)
    flow = jnp.dot(
        pick_rows, pick_cols, precision=lax.Precision.HIGHEST, preferred_element_type=jnp.float32
    ).reshape(depth, rows_x, rows_y)

    inside = jnp.stack(
        [wide_at > 0, wide_at < last_w, narrow_at > 0, narrow_at < last_n]
    ).astype(jnp.int32)
    edges = block_edges(pressure_start)
    flow, edges = lax.optimization_barrier((flow, edges))
    rims = lax.all_to_all(
        rims, ("wide", "narrow"), split_axis=0, concat_axis=0, tiled=True,
    ).reshape(depth, 4, rows_y)
    pressure = pressure_start
    stored = None
    for step in range(STEPS):
        pressure, edges, stored = advance(
            stored, pressure, halos(edges), flow, inside, log_perm, rims
        )
    return (log_perm, pressure)


def solution(mesh):
    in_specs = (
        P("member", "wide", "narrow"),
        P(),
        P(),
        P(),
        P("member", "wide", "narrow"),
        P("member"),
        P("member"),
        P("member"),
        P("member"),
    )
    out_specs = (P("member", "wide", "narrow"), P("member", "wide", "narrow"))
    return jax.shard_map(body, mesh=mesh, in_specs=in_specs, out_specs=out_specs, check_vma=False)
```

```python
import functools

import jax
import jax.numpy as jnp
from jax import lax
from jax.experimental import pallas as pl
from jax.experimental.pallas import tpu as pltpu
from jax.sharding import PartitionSpec as P

STEPS = 2


STEP_SIZE = 0.03
CAP_LOG = 1.5
CHUNK_Z = 16
EDGE_Z = 32
DEPTH_X = 16


def permeability(values):
    return jnp.exp(CAP_LOG * jnp.tanh(values / CAP_LOG))


def harmonic(a, b):
    return 2.0 * a * b / (a + b)


def halos(edges):
    forward_w = [(i, i + 1) for i in range(lax.axis_size("wide") - 1)]
    backward_w = [(j, i) for i, j in forward_w]
    forward_n = [(i, i + 1) for i in range(lax.axis_size("narrow") - 1)]
    backward_n = [(j, i) for i, j in forward_n]
    first_x, last_x, first_y, last_y = edges
    x_lo = lax.ppermute(last_x, "wide", forward_w)
    x_hi = lax.ppermute(first_x, "wide", backward_w)
    y_lo = lax.ppermute(last_y, "narrow", forward_n)
    y_hi = lax.ppermute(first_y, "narrow", backward_n)
    return x_lo, x_hi, y_lo, y_hi


def to_columns(rows):
    tz, nx = rows.shape
    eye = jnp.where(
        lax.broadcasted_iota(jnp.int32, (nx, nx), 0) == lax.broadcasted_iota(jnp.int32, (nx, nx), 1),
        1.0, 0.0,
    )
    cols = lax.dot_general(
        eye, rows, (((1,), (1,)), ((), ())),
        precision=lax.Precision.HIGHEST, preferred_element_type=jnp.float32,
    )
    return jnp.concatenate([cols[:, k : k + 1][None] for k in range(tz)], axis=0)


def x_rows(ref):
    return jnp.concatenate([ref[k : k + 1, :][None] for k in range(ref.shape[0])], axis=0)


def store_x_rows(ref, rows):
    for k in range(ref.shape[0]):
        ref[k : k + 1, :] = rows[k]


def to_rows(block):
    tz, nx, ny = block.shape
    lane = lax.broadcasted_iota(jnp.int32, (nx, 128), 1)
    pick = jnp.where(
        lax.broadcasted_iota(jnp.int32, (tz, 128), 0) == lax.broadcasted_iota(jnp.int32, (tz, 128), 1),
        1.0, 0.0,
    )
    result = []
    for column in (0, ny - 1):
        gathered = jnp.zeros((nx, 128), jnp.float32)
        for k in range(tz):
            gathered = jnp.where(lane == k, block[k, :, column : column + 1], gathered)
        result.append(
            lax.dot_general(
                pick, gathered, (((1,), (1,)), ((), ())),
                precision=lax.Precision.HIGHEST, preferred_element_type=jnp.float32,
            )
        )
    return result[0], result[1]


def edge_kernel(block_ref, xl_ref, xh_ref, yl_ref, yh_ref, *copy_ref):
    block = block_ref[...]
    if copy_ref:
        copy_ref[0][...] = block
    block = block.astype(jnp.float32)
    store_x_rows(xl_ref, block[:, :1, :])
    store_x_rows(xh_ref, block[:, -1:, :])
    yl_ref[...], yh_ref[...] = to_rows(block)


def block_edges(block, keep=False):
    depth, nx, ny = block.shape
    tz = EDGE_Z
    f32 = jnp.float32
    whole = pl.BlockSpec((tz, nx, ny), lambda c: (c, 0, 0))
    row = pl.BlockSpec((tz, ny), lambda c: (c, 0))
    col = pl.BlockSpec((tz, nx), lambda c: (c, 0))
    out_shape = [
        jax.ShapeDtypeStruct((depth, ny), f32),
        jax.ShapeDtypeStruct((depth, ny), f32),
        jax.ShapeDtypeStruct((depth, nx), f32),
        jax.ShapeDtypeStruct((depth, nx), f32),
    ]
    out_specs = [row, row, col, col]
    if keep:
        out_shape.append(jax.ShapeDtypeStruct(block.shape, block.dtype))
        out_specs.append(whole)
    return pl.pallas_call(
        edge_kernel,
        out_shape=tuple(out_shape),
        grid=(depth // tz,),
        in_specs=[whole],
        out_specs=out_specs,
        compiler_params=pltpu.CompilerParams(dimension_semantics=("arbitrary",)),
    )(block)


def update(trans, pm_ref, pb_ref, pa_ref, qxl_ref, qxh_ref, qyl_ref, qyh_ref, f_ref, outs):
    o_ref, exl_ref, exh_ref, eyl_ref, eyh_ref = outs
    t_zp, t_zm, t_xp, t_xm, t_yp, t_ym = trans
    tz, nx, ny = pm_ref.shape
    f32 = jnp.float32
    xi = lax.broadcasted_iota(jnp.int32, (tz, nx, ny), 1)
    yi = lax.broadcasted_iota(jnp.int32, (tz, nx, ny), 2)
    p = pm_ref[...].astype(f32)
    pext = jnp.concatenate([pb_ref[...].astype(f32), p, pa_ref[...].astype(f32)], axis=0)
    n_xp = jnp.where(xi == nx - 1, x_rows(qxh_ref), pltpu.roll(p, nx - 1, 1))
    n_xm = jnp.where(xi == 0, x_rows(qxl_ref), pltpu.roll(p, 1, 1))
    n_yp = jnp.where(yi == ny - 1, to_columns(qyh_ref[...]), pltpu.roll(p, ny - 1, 2))
    n_ym = jnp.where(yi == 0, to_columns(qyl_ref[...]), pltpu.roll(p, 1, 2))

    flux = t_zp * (pext[2:] - p)
    flux = flux + t_zm * (pext[:-2] - p)
    flux = flux + t_xp * (n_xp - p)
    flux = flux + t_xm * (n_xm - p)
    flux = flux + t_yp * (n_yp - p)
    flux = flux + t_ym * (n_ym - p)
    new = p + STEP_SIZE * (flux + f_ref[...]) / (1.0 + 0.5 * p * p)
    o_ref[...] = new
    store_x_rows(exl_ref, new[:, :1, :])
    store_x_rows(exh_ref, new[:, nx - 1 :, :])
    eyl_ref[...], eyh_ref[...] = to_rows(new)


def first_step_kernel(
    inside_ref, lpm_ref, lpb_ref, lpa_ref, rim_ref,
    pm_ref, pb_ref, pa_ref, qxl_ref, qxh_ref, qyl_ref, qyh_ref, f_ref,
    o_ref, exl_ref, exh_ref, eyl_ref, eyh_ref, tzm_ref, txm_ref, tym_ref, txp_ref, typ_ref,
):
    c = pl.program_id(0)
    last = pl.num_programs(0) - 1
    tz, nx, ny = pm_ref.shape
    f32 = jnp.float32

    def side_perm(values, k):
        return jnp.where(inside_ref[k] > 0, permeability(values), 0.0)

    kxl = side_perm(rim_ref[:, 0:1, :].astype(f32), 0)
    kxh = side_perm(rim_ref[:, 1:2, :].astype(f32), 1)
    kyl = to_columns(side_perm(rim_ref[:, 2, 0:nx].astype(f32), 2))
    kyh = to_columns(side_perm(rim_ref[:, 3, 0:nx].astype(f32), 3))

    below = jnp.where(c == 0, 0.0, permeability(lpb_ref[...].astype(f32)))
    above = jnp.where(c == last, 0.0, permeability(lpa_ref[...].astype(f32)))
    centre = permeability(lpm_ref[...].astype(f32))
    ext = jnp.concatenate([below, centre, above], axis=0)
    faces = harmonic(ext[:-1], ext[1:])
    t_zm = faces[:-1]
    t_zp = faces[1:]

    xi = lax.broadcasted_iota(jnp.int32, (tz, nx, ny), 1)
    yi = lax.broadcasted_iota(jnp.int32, (tz, nx, ny), 2)

    fx = harmonic(centre, pltpu.roll(centre, nx - 1, 1))
    t_xp = jnp.where(xi == nx - 1, harmonic(centre[:, nx - 1 :, :], kxh), fx)
    t_xm = jnp.where(xi == 0, harmonic(centre[:, :1, :], kxl), pltpu.roll(fx, 1, 1))
    fy = harmonic(centre, pltpu.roll(centre, ny - 1, 2))
    t_yp = jnp.where(yi == ny - 1, harmonic(centre[:, :, ny - 1 :], kyh), fy)
    t_ym = jnp.where(yi == 0, harmonic(centre[:, :, :1], kyl), pltpu.roll(fy, 1, 2))

    tzm_ref[...] = t_zm
    txm_ref[...] = t_xm
    tym_ref[...] = t_ym
    store_x_rows(txp_ref, t_xp[:, nx - 1 :, :])
    typ_ref[...] = to_rows(t_yp)[1]
    update(
        (t_zp, t_zm, t_xp, t_xm, t_yp, t_ym),
        pm_ref, pb_ref, pa_ref, qxl_ref, qxh_ref, qyl_ref, qyh_ref, f_ref,
        (o_ref, exl_ref, exh_ref, eyl_ref, eyh_ref),
    )


def later_step_kernel(
    tzm_ref, tza_ref, txm_ref, tym_ref, txp_ref, typ_ref,
    pm_ref, pb_ref, pa_ref, qxl_ref, qxh_ref, qyl_ref, qyh_ref, f_ref,
    o_ref, exl_ref, exh_ref, eyl_ref, eyh_ref,
):
    c = pl.program_id(0)
    last = pl.num_programs(0) - 1
    tz, nx, ny = pm_ref.shape
    xi = lax.broadcasted_iota(jnp.int32, (tz, nx, ny), 1)
    yi = lax.broadcasted_iota(jnp.int32, (tz, nx, ny), 2)
    t_zm = tzm_ref[...]
    t_zp = jnp.concatenate([t_zm[1:], jnp.where(c == last, 0.0, tza_ref[...])], axis=0)
    t_xm = txm_ref[...]
    t_xp = jnp.where(xi == nx - 1, x_rows(txp_ref), pltpu.roll(t_xm, nx - 1, 1))
    t_ym = tym_ref[...]
    t_yp = jnp.where(yi == ny - 1, to_columns(typ_ref[...]), pltpu.roll(t_ym, ny - 1, 2))
    update(
        (t_zp, t_zm, t_xp, t_xm, t_yp, t_ym),
        pm_ref, pb_ref, pa_ref, qxl_ref, qxh_ref, qyl_ref, qyh_ref, f_ref,
        (o_ref, exl_ref, exh_ref, eyl_ref, eyh_ref),
    )


def advance(stored, pressure, pressure_halos, flow, inside=None, log_perm=None, rims=None):
    depth, nx, ny = pressure.shape
    tz = CHUNK_Z
    grid = (depth // tz,)
    main = pl.BlockSpec((tz, nx, ny), lambda c: (c, 0, 0))
    below = pl.BlockSpec((1, nx, ny), lambda c: (jnp.maximum(c * tz - 1, 0), 0, 0))
    above = pl.BlockSpec((1, nx, ny), lambda c: (jnp.minimum(c * tz + tz, depth - 1), 0, 0))
    row = pl.BlockSpec((tz, ny), lambda c: (c, 0))
    col = pl.BlockSpec((tz, nx), lambda c: (c, 0))
    side = [row, row, col, col]
    smem = pl.BlockSpec(memory_space=pltpu.SMEM)
    f32 = jnp.float32
    full = jax.ShapeDtypeStruct((depth, nx, ny), f32)
    rows = jax.ShapeDtypeStruct((depth, ny), f32)
    cols = jax.ShapeDtypeStruct((depth, nx), f32)
    out_shape = [full, rows, rows, cols, cols]
    out_specs = [main] + side
    pressure_args = [pressure, pressure, pressure, *pressure_halos, flow]
    pressure_specs = [main, below, above] + side + [main]
    params = pltpu.CompilerParams(dimension_semantics=("arbitrary",))
    if stored is None:
        outs = pl.pallas_call(
            first_step_kernel,
            out_shape=tuple(out_shape + [full, full, full, rows, cols]),
            grid=grid,
            in_specs=[smem, main, below, above, pl.BlockSpec((tz, 4, ny), lambda c: (c, 0, 0))]
            + pressure_specs,
            out_specs=out_specs + [main, main, main, row, col],
            compiler_params=params,
        )(inside, log_perm, log_perm, log_perm, rims, *pressure_args)
        return outs[0], outs[1:5], outs[5:]
    t_zm, t_xm, t_ym, t_xp, t_yp = stored
    outs = pl.pallas_call(
        later_step_kernel,
        out_shape=tuple(out_shape),
        grid=grid,
        in_specs=[main, above, main, main, row, col] + pressure_specs,
        out_specs=out_specs,
        compiler_params=params,
    )(t_zm, t_zm, t_xm, t_ym, t_xp, t_yp, *pressure_args)
    return outs[0], outs[1:5], stored


def depth_kernel(rz_ref, n_ref, o_ref):
    rz = rz_ref[...]
    for i in range(n_ref.shape[1]):
        o_ref[:, i, :] = jnp.dot(rz, n_ref[:, i, :], preferred_element_type=jnp.float32).astype(
            jnp.bfloat16
        )


def depth_transform(root_z, noise):
    depth, nx, ny = noise.shape
    bx = min(nx, DEPTH_X)
    block = pl.BlockSpec((depth, bx, ny), lambda i: (0, i, 0))
    return pl.pallas_call(
        depth_kernel,
        out_shape=jax.ShapeDtypeStruct(noise.shape, jnp.bfloat16),
        grid=(nx // bx,),
        in_specs=[pl.BlockSpec(root_z.shape, lambda i: (0, 0)), block],
        out_specs=block,
        compiler_params=pltpu.CompilerParams(dimension_semantics=("arbitrary",)),
    )(root_z, noise)


def line_kernel(g_ref, rx_ref, ry_ref, o_ref, h_ref, *, count_w, count_n):
    f32 = jnp.float32
    nx = g_ref.shape[2]
    ny = g_ref.shape[3]
    rx = rx_ref[...]
    halves = []
    for n in range(count_n):
        lines = jnp.concatenate([g_ref[w * count_n + n, 0] for w in range(count_w)], axis=0)
        halves.append(jnp.dot(rx, lines, preferred_element_type=f32).astype(jnp.bfloat16))
    second = jnp.concatenate(halves, axis=1)
    third = lax.dot_general(
        second, ry_ref[...], (((1,), (1,)), ((), ())), preferred_element_type=f32
    ).astype(jnp.bfloat16)
    for w in range(count_w):
        for n in range(count_n):
            o_ref[w * count_n + n, 0] = third[w * nx : (w + 1) * nx, n * ny : (n + 1) * ny]

    total_y = count_n * ny
    wanted = [n * ny - 1 if n > 0 else 0 for n in range(count_n)]
    wanted += [(n + 1) * ny if n < count_n - 1 else 0 for n in range(count_n)]
    picks = max(8, len(wanted))
    row = lax.broadcasted_iota(jnp.int32, (picks, total_y), 0)
    lane = lax.broadcasted_iota(jnp.int32, (picks, total_y), 1)
    sel = jnp.zeros((picks, total_y), jnp.bool_)
    for r, y in enumerate(wanted):
        sel = sel | ((row == r) & (lane == y))
    columns = lax.dot_general(
        jnp.where(sel, 1.0, 0.0).astype(jnp.bfloat16), third, (((1,), (1,)), ((), ())),
        preferred_element_type=f32,
    )
    h_ref[...] = jnp.zeros(h_ref.shape, f32)
    for w in range(count_w):
        for n in range(count_n):
            d = w * count_n + n
            ys = slice(n * ny, (n + 1) * ny)
            if w > 0:
                h_ref[d, 0, 0:1, :] = third[w * nx - 1 : w * nx, ys].astype(f32)
            if w < count_w - 1:
                h_ref[d, 0, 1:2, :] = third[(w + 1) * nx : (w + 1) * nx + 1, ys].astype(f32)
            if n > 0:
                h_ref[d, 0, 2:3, 0:nx] = columns[n : n + 1, w * nx : (w + 1) * nx]
            if n < count_n - 1:
                h_ref[d, 0, 3:4, 0:nx] = columns[count_n + n : count_n + n + 1, w * nx : (w + 1) * nx]


def line_transforms(gathered, root_x, root_y, count_w, count_n):
    groups, planes, nx, ny = gathered.shape
    block = pl.BlockSpec((groups, 1, nx, ny), lambda z: (0, z, 0, 0))
    whole_x = pl.BlockSpec(root_x.shape, lambda z: (0, 0))
    whole_y = pl.BlockSpec(root_y.shape, lambda z: (0, 0))
    rims = pl.BlockSpec((groups, 1, 4, ny), lambda z: (0, z, 0, 0))
    return pl.pallas_call(
        functools.partial(line_kernel, count_w=count_w, count_n=count_n),
        out_shape=(
            jax.ShapeDtypeStruct(gathered.shape, jnp.bfloat16),
            jax.ShapeDtypeStruct((groups, planes, 4, ny), jnp.float32),
        ),
        grid=(planes,),
        in_specs=[block, whole_x, whole_y],
        out_specs=(block, rims),
        compiler_params=pltpu.CompilerParams(dimension_semantics=("arbitrary",)),
    )(gathered, root_x, root_y)


def body(noise, root_z, root_x, root_y, pressure_start, well_x, well_y, well_z, well_rate):
    depth, rows_x, rows_y = noise.shape
    first = depth_transform(root_z, noise)
    count_w = lax.axis_size("wide")
    count_n = lax.axis_size("narrow")
    groups = count_w * count_n
    planes = depth // groups
    gathered = lax.all_to_all(
        first.reshape(groups, planes, rows_x, rows_y),
        ("wide", "narrow"), split_axis=0, concat_axis=0, tiled=True,
    )
    outgoing, rims = line_transforms(gathered, root_x, root_y, count_w, count_n)
    log_perm = lax.all_to_all(
        outgoing, ("wide", "narrow"), split_axis=0, concat_axis=0, tiled=True,
    ).reshape(depth, rows_x, rows_y)

    wide_at = lax.axis_index("wide")
    narrow_at = lax.axis_index("narrow")
    last_w = lax.axis_size("wide") - 1
    last_n = lax.axis_size("narrow") - 1

    local_x = well_x - wide_at * rows_x
    local_y = well_y - narrow_at * rows_y
    valid = (local_x >= 0) & (local_x < rows_x) & (local_y >= 0) & (local_y < rows_y)
    rates = jnp.where(valid, well_rate, 0.0).astype(jnp.float32)
    wells = well_x.shape[0]
    cells = well_z * rows_x + local_x
    pick_rows = jnp.where(
        lax.broadcasted_iota(jnp.int32, (depth * rows_x, wells), 0) == cells[None, :],
        rates[None, :],
        0.0,
    )
    pick_cols = (
        lax.broadcasted_iota(jnp.int32, (wells, rows_y), 1) == local_y[:, None]
    ).astype(jnp.float32)
    flow = jnp.dot(
        pick_rows, pick_cols, precision=lax.Precision.HIGHEST, preferred_element_type=jnp.float32
    ).reshape(depth, rows_x, rows_y)

    inside = jnp.stack(
        [wide_at > 0, wide_at < last_w, narrow_at > 0, narrow_at < last_n]
    ).astype(jnp.int32)
    edges = block_edges(pressure_start)
    flow, edges = lax.optimization_barrier((flow, edges))
    rims, flow = lax.optimization_barrier((rims, flow))
    rims = lax.all_to_all(
        rims.astype(jnp.bfloat16), ("wide", "narrow"), split_axis=0, concat_axis=0, tiled=True,
    ).reshape(depth, 4, rows_y)
    pressure = pressure_start
    stored = None
    for step in range(STEPS):
        pressure, edges, stored = advance(
            stored, pressure, halos(edges), flow, inside, log_perm, rims
        )
    return (log_perm, pressure)


def solution(mesh):
    in_specs = (
        P("member", "wide", "narrow"),
        P(),
        P(),
        P(),
        P("member", "wide", "narrow"),
        P("member"),
        P("member"),
        P("member"),
        P("member"),
    )
    out_specs = (P("member", "wide", "narrow"), P("member", "wide", "narrow"))
    return jax.shard_map(body, mesh=mesh, in_specs=in_specs, out_specs=out_specs, check_vma=False)
```

```python
import functools

import jax
import jax.numpy as jnp
from jax import lax
from jax.experimental import pallas as pl
from jax.experimental.pallas import tpu as pltpu
from jax.sharding import PartitionSpec as P

STEPS = 2


STEP_SIZE = 0.03
CAP_LOG = 1.5
CHUNK_Z = 16
EDGE_Z = 32
DEPTH_X = 16


def permeability(values):
    return jnp.exp(CAP_LOG * jnp.tanh(values / CAP_LOG))


def harmonic(a, b):
    return 2.0 * a * b / (a + b)


def halos(edges):
    forward_w = [(i, i + 1) for i in range(lax.axis_size("wide") - 1)]
    backward_w = [(j, i) for i, j in forward_w]
    forward_n = [(i, i + 1) for i in range(lax.axis_size("narrow") - 1)]
    backward_n = [(j, i) for i, j in forward_n]
    first_x, last_x, first_y, last_y = edges
    x_lo = lax.ppermute(last_x, "wide", forward_w)
    x_hi = lax.ppermute(first_x, "wide", backward_w)
    y_lo = lax.ppermute(last_y, "narrow", forward_n)
    y_hi = lax.ppermute(first_y, "narrow", backward_n)
    return x_lo, x_hi, y_lo, y_hi


def to_columns(rows):
    tz, nx = rows.shape
    eye = jnp.where(
        lax.broadcasted_iota(jnp.int32, (nx, nx), 0) == lax.broadcasted_iota(jnp.int32, (nx, nx), 1),
        1.0, 0.0,
    )
    cols = lax.dot_general(
        eye, rows, (((1,), (1,)), ((), ())),
        precision=lax.Precision.HIGHEST, preferred_element_type=jnp.float32,
    )
    return jnp.concatenate([cols[:, k : k + 1][None] for k in range(tz)], axis=0)


def x_rows(ref):
    return jnp.concatenate([ref[k : k + 1, :][None] for k in range(ref.shape[0])], axis=0)


def store_x_rows(ref, rows):
    for k in range(ref.shape[0]):
        ref[k : k + 1, :] = rows[k]


def to_rows(block):
    tz, nx, ny = block.shape
    lane = lax.broadcasted_iota(jnp.int32, (nx, 128), 1)
    pick = jnp.where(
        lax.broadcasted_iota(jnp.int32, (tz, 128), 0) == lax.broadcasted_iota(jnp.int32, (tz, 128), 1),
        1.0, 0.0,
    )
    result = []
    for column in (0, ny - 1):
        gathered = jnp.zeros((nx, 128), jnp.float32)
        for k in range(tz):
            gathered = jnp.where(lane == k, block[k, :, column : column + 1], gathered)
        result.append(
            lax.dot_general(
                pick, gathered, (((1,), (1,)), ((), ())),
                precision=lax.Precision.HIGHEST, preferred_element_type=jnp.float32,
            )
        )
    return result[0], result[1]


def edge_kernel(block_ref, xl_ref, xh_ref, yl_ref, yh_ref, *copy_ref):
    block = block_ref[...]
    if copy_ref:
        copy_ref[0][...] = block
    block = block.astype(jnp.float32)
    store_x_rows(xl_ref, block[:, :1, :])
    store_x_rows(xh_ref, block[:, -1:, :])
    yl_ref[...], yh_ref[...] = to_rows(block)


def block_edges(block, keep=False):
    depth, nx, ny = block.shape
    tz = EDGE_Z
    f32 = jnp.float32
    whole = pl.BlockSpec((tz, nx, ny), lambda c: (c, 0, 0))
    row = pl.BlockSpec((tz, ny), lambda c: (c, 0))
    col = pl.BlockSpec((tz, nx), lambda c: (c, 0))
    out_shape = [
        jax.ShapeDtypeStruct((depth, ny), f32),
        jax.ShapeDtypeStruct((depth, ny), f32),
        jax.ShapeDtypeStruct((depth, nx), f32),
        jax.ShapeDtypeStruct((depth, nx), f32),
    ]
    out_specs = [row, row, col, col]
    if keep:
        out_shape.append(jax.ShapeDtypeStruct(block.shape, block.dtype))
        out_specs.append(whole)
    return pl.pallas_call(
        edge_kernel,
        out_shape=tuple(out_shape),
        grid=(depth // tz,),
        in_specs=[whole],
        out_specs=out_specs,
        compiler_params=pltpu.CompilerParams(dimension_semantics=("arbitrary",)),
    )(block)


def update(trans, pm_ref, pb_ref, pa_ref, qxl_ref, qxh_ref, qyl_ref, qyh_ref, f_ref, outs):
    o_ref, exl_ref, exh_ref, eyl_ref, eyh_ref = outs
    t_zp, t_zm, t_xp, t_xm, t_yp, t_ym = trans
    tz, nx, ny = pm_ref.shape
    f32 = jnp.float32
    xi = lax.broadcasted_iota(jnp.int32, (tz, nx, ny), 1)
    yi = lax.broadcasted_iota(jnp.int32, (tz, nx, ny), 2)
    p = pm_ref[...].astype(f32)
    pext = jnp.concatenate([pb_ref[...].astype(f32), p, pa_ref[...].astype(f32)], axis=0)
    n_xp = jnp.where(xi == nx - 1, x_rows(qxh_ref), pltpu.roll(p, nx - 1, 1))
    n_xm = jnp.where(xi == 0, x_rows(qxl_ref), pltpu.roll(p, 1, 1))
    n_yp = jnp.where(yi == ny - 1, to_columns(qyh_ref[...]), pltpu.roll(p, ny - 1, 2))
    n_ym = jnp.where(yi == 0, to_columns(qyl_ref[...]), pltpu.roll(p, 1, 2))

    flux = t_zp * (pext[2:] - p)
    flux = flux + t_zm * (pext[:-2] - p)
    flux = flux + t_xp * (n_xp - p)
    flux = flux + t_xm * (n_xm - p)
    flux = flux + t_yp * (n_yp - p)
    flux = flux + t_ym * (n_ym - p)
    new = p + STEP_SIZE * (flux + f_ref[...]) / (1.0 + 0.5 * p * p)
    o_ref[...] = new
    store_x_rows(exl_ref, new[:, :1, :])
    store_x_rows(exh_ref, new[:, nx - 1 :, :])
    eyl_ref[...], eyh_ref[...] = to_rows(new)


def first_step_kernel(
    inside_ref, lpm_ref, lpb_ref, lpa_ref, lxl_ref, lxh_ref, lyl_ref, lyh_ref,
    pm_ref, pb_ref, pa_ref, qxl_ref, qxh_ref, qyl_ref, qyh_ref, f_ref,
    o_ref, exl_ref, exh_ref, eyl_ref, eyh_ref, tzm_ref, txm_ref, tym_ref, txp_ref, typ_ref,
):
    c = pl.program_id(0)
    last = pl.num_programs(0) - 1
    tz, nx, ny = pm_ref.shape
    f32 = jnp.float32

    def side_perm(ref, k):
        return jnp.where(inside_ref[k] > 0, permeability(ref[...].astype(f32)), 0.0)

    kxl = jnp.where(inside_ref[0] > 0, permeability(x_rows(lxl_ref)), 0.0)
    kxh = jnp.where(inside_ref[1] > 0, permeability(x_rows(lxh_ref)), 0.0)
    kyl = to_columns(side_perm(lyl_ref, 2))
    kyh = to_columns(side_perm(lyh_ref, 3))

    below = jnp.where(c == 0, 0.0, permeability(lpb_ref[...].astype(f32)))
    above = jnp.where(c == last, 0.0, permeability(lpa_ref[...].astype(f32)))
    centre = permeability(lpm_ref[...].astype(f32))
    ext = jnp.concatenate([below, centre, above], axis=0)
    faces = harmonic(ext[:-1], ext[1:])
    t_zm = faces[:-1]
    t_zp = faces[1:]

    xi = lax.broadcasted_iota(jnp.int32, (tz, nx, ny), 1)
    yi = lax.broadcasted_iota(jnp.int32, (tz, nx, ny), 2)

    fx = harmonic(centre, pltpu.roll(centre, nx - 1, 1))
    t_xp = jnp.where(xi == nx - 1, harmonic(centre[:, nx - 1 :, :], kxh), fx)
    t_xm = jnp.where(xi == 0, harmonic(centre[:, :1, :], kxl), pltpu.roll(fx, 1, 1))
    fy = harmonic(centre, pltpu.roll(centre, ny - 1, 2))
    t_yp = jnp.where(yi == ny - 1, harmonic(centre[:, :, ny - 1 :], kyh), fy)
    t_ym = jnp.where(yi == 0, harmonic(centre[:, :, :1], kyl), pltpu.roll(fy, 1, 2))

    tzm_ref[...] = t_zm
    txm_ref[...] = t_xm
    tym_ref[...] = t_ym
    store_x_rows(txp_ref, t_xp[:, nx - 1 :, :])
    typ_ref[...] = to_rows(t_yp)[1]
    update(
        (t_zp, t_zm, t_xp, t_xm, t_yp, t_ym),
        pm_ref, pb_ref, pa_ref, qxl_ref, qxh_ref, qyl_ref, qyh_ref, f_ref,
        (o_ref, exl_ref, exh_ref, eyl_ref, eyh_ref),
    )


def later_step_kernel(
    tzm_ref, tza_ref, txm_ref, tym_ref, txp_ref, typ_ref,
    pm_ref, pb_ref, pa_ref, qxl_ref, qxh_ref, qyl_ref, qyh_ref, f_ref,
    o_ref, exl_ref, exh_ref, eyl_ref, eyh_ref,
):
    c = pl.program_id(0)
    last = pl.num_programs(0) - 1
    tz, nx, ny = pm_ref.shape
    xi = lax.broadcasted_iota(jnp.int32, (tz, nx, ny), 1)
    yi = lax.broadcasted_iota(jnp.int32, (tz, nx, ny), 2)
    t_zm = tzm_ref[...]
    t_zp = jnp.concatenate([t_zm[1:], jnp.where(c == last, 0.0, tza_ref[...])], axis=0)
    t_xm = txm_ref[...]
    t_xp = jnp.where(xi == nx - 1, x_rows(txp_ref), pltpu.roll(t_xm, nx - 1, 1))
    t_ym = tym_ref[...]
    t_yp = jnp.where(yi == ny - 1, to_columns(typ_ref[...]), pltpu.roll(t_ym, ny - 1, 2))
    update(
        (t_zp, t_zm, t_xp, t_xm, t_yp, t_ym),
        pm_ref, pb_ref, pa_ref, qxl_ref, qxh_ref, qyl_ref, qyh_ref, f_ref,
        (o_ref, exl_ref, exh_ref, eyl_ref, eyh_ref),
    )


def advance(stored, pressure, pressure_halos, flow, inside=None, log_perm=None, perm_halos=None):
    depth, nx, ny = pressure.shape
    tz = CHUNK_Z
    grid = (depth // tz,)
    main = pl.BlockSpec((tz, nx, ny), lambda c: (c, 0, 0))
    below = pl.BlockSpec((1, nx, ny), lambda c: (jnp.maximum(c * tz - 1, 0), 0, 0))
    above = pl.BlockSpec((1, nx, ny), lambda c: (jnp.minimum(c * tz + tz, depth - 1), 0, 0))
    row = pl.BlockSpec((tz, ny), lambda c: (c, 0))
    col = pl.BlockSpec((tz, nx), lambda c: (c, 0))
    side = [row, row, col, col]
    smem = pl.BlockSpec(memory_space=pltpu.SMEM)
    f32 = jnp.float32
    full = jax.ShapeDtypeStruct((depth, nx, ny), f32)
    rows = jax.ShapeDtypeStruct((depth, ny), f32)
    cols = jax.ShapeDtypeStruct((depth, nx), f32)
    out_shape = [full, rows, rows, cols, cols]
    out_specs = [main] + side
    pressure_args = [pressure, pressure, pressure, *pressure_halos, flow]
    pressure_specs = [main, below, above] + side + [main]
    params = pltpu.CompilerParams(dimension_semantics=("arbitrary",))
    if stored is None:
        outs = pl.pallas_call(
            first_step_kernel,
            out_shape=tuple(out_shape + [full, full, full, rows, cols]),
            grid=grid,
            in_specs=[smem, main, below, above] + side + pressure_specs,
            out_specs=out_specs + [main, main, main, row, col],
            compiler_params=params,
        )(inside, log_perm, log_perm, log_perm, *perm_halos, *pressure_args)
        return outs[0], outs[1:5], outs[5:]
    t_zm, t_xm, t_ym, t_xp, t_yp = stored
    outs = pl.pallas_call(
        later_step_kernel,
        out_shape=tuple(out_shape),
        grid=grid,
        in_specs=[main, above, main, main, row, col] + pressure_specs,
        out_specs=out_specs,
        compiler_params=params,
    )(t_zm, t_zm, t_xm, t_ym, t_xp, t_yp, *pressure_args)
    return outs[0], outs[1:5], stored


def depth_kernel(rz_ref, n_ref, o_ref):
    rz = rz_ref[...]
    for i in range(n_ref.shape[1]):
        o_ref[:, i, :] = jnp.dot(rz, n_ref[:, i, :], preferred_element_type=jnp.float32).astype(
            jnp.bfloat16
        )


def depth_transform(root_z, noise):
    depth, nx, ny = noise.shape
    bx = min(nx, DEPTH_X)
    block = pl.BlockSpec((depth, bx, ny), lambda i: (0, i, 0))
    return pl.pallas_call(
        depth_kernel,
        out_shape=jax.ShapeDtypeStruct(noise.shape, jnp.bfloat16),
        grid=(nx // bx,),
        in_specs=[pl.BlockSpec(root_z.shape, lambda i: (0, 0)), block],
        out_specs=block,
        compiler_params=pltpu.CompilerParams(dimension_semantics=("arbitrary",)),
    )(root_z, noise)


def line_kernel(g_ref, rx_ref, ry_ref, o_ref, *, count_w, count_n):
    f32 = jnp.float32
    nx = g_ref.shape[2]
    ny = g_ref.shape[3]
    rx = rx_ref[...]
    halves = []
    for n in range(count_n):
        lines = jnp.concatenate([g_ref[w * count_n + n, 0] for w in range(count_w)], axis=0)
        halves.append(jnp.dot(rx, lines, preferred_element_type=f32).astype(jnp.bfloat16))
    second = jnp.concatenate(halves, axis=1)
    third = lax.dot_general(
        second, ry_ref[...], (((1,), (1,)), ((), ())), preferred_element_type=f32
    ).astype(jnp.bfloat16)
    for w in range(count_w):
        for n in range(count_n):
            o_ref[w * count_n + n, 0] = third[w * nx : (w + 1) * nx, n * ny : (n + 1) * ny]


def line_transforms(gathered, root_x, root_y, count_w, count_n):
    groups, planes, nx, ny = gathered.shape
    block = pl.BlockSpec((groups, 1, nx, ny), lambda z: (0, z, 0, 0))
    whole_x = pl.BlockSpec(root_x.shape, lambda z: (0, 0))
    whole_y = pl.BlockSpec(root_y.shape, lambda z: (0, 0))
    return pl.pallas_call(
        functools.partial(line_kernel, count_w=count_w, count_n=count_n),
        out_shape=jax.ShapeDtypeStruct(gathered.shape, jnp.bfloat16),
        grid=(planes,),
        in_specs=[block, whole_x, whole_y],
        out_specs=block,
        compiler_params=pltpu.CompilerParams(dimension_semantics=("arbitrary",)),
    )(gathered, root_x, root_y)


def body(noise, root_z, root_x, root_y, pressure_start, well_x, well_y, well_z, well_rate):
    depth, rows_x, rows_y = noise.shape
    first = depth_transform(root_z, noise)
    count_w = lax.axis_size("wide")
    count_n = lax.axis_size("narrow")
    groups = count_w * count_n
    planes = depth // groups
    gathered = lax.all_to_all(
        first.reshape(groups, planes, rows_x, rows_y),
        ("wide", "narrow"), split_axis=0, concat_axis=0, tiled=True,
    )
    wide_at = lax.axis_index("wide")
    narrow_at = lax.axis_index("narrow")
    last_w = lax.axis_size("wide") - 1
    last_n = lax.axis_size("narrow") - 1

    local_x = well_x - wide_at * rows_x
    local_y = well_y - narrow_at * rows_y
    valid = (local_x >= 0) & (local_x < rows_x) & (local_y >= 0) & (local_y < rows_y)
    rates = jnp.where(valid, well_rate, 0.0).astype(jnp.float32)
    wells = well_x.shape[0]
    cells = well_z * rows_x + local_x
    pick_rows = jnp.where(
        lax.broadcasted_iota(jnp.int32, (depth * rows_x, wells), 0) == cells[None, :],
        rates[None, :],
        0.0,
    )
    pick_cols = (
        lax.broadcasted_iota(jnp.int32, (wells, rows_y), 1) == local_y[:, None]
    ).astype(jnp.float32)
    flow = jnp.dot(
        pick_rows, pick_cols, precision=lax.Precision.HIGHEST, preferred_element_type=jnp.float32
    ).reshape(depth, rows_x, rows_y)

    inside = jnp.stack(
        [wide_at > 0, wide_at < last_w, narrow_at > 0, narrow_at < last_n]
    ).astype(jnp.int32)
    edges = block_edges(pressure_start)
    gathered, flow, edges = lax.optimization_barrier((gathered, flow, edges))
    outgoing = line_transforms(gathered, root_x, root_y, count_w, count_n)
    log_perm = lax.all_to_all(
        outgoing, ("wide", "narrow"), split_axis=0, concat_axis=0, tiled=True,
    ).reshape(depth, rows_x, rows_y)

    *lp_edges, log_perm = block_edges(log_perm, keep=True)
    perm_halos = halos(lp_edges)
    pressure = pressure_start
    stored = None
    for step in range(STEPS):
        pressure, edges, stored = advance(
            stored, pressure, halos(edges), flow, inside, log_perm, perm_halos
        )
    return (log_perm, pressure)


def solution(mesh):
    in_specs = (
        P("member", "wide", "narrow"),
        P(),
        P(),
        P(),
        P("member", "wide", "narrow"),
        P("member"),
        P("member"),
        P("member"),
        P("member"),
    )
    out_specs = (P("member", "wide", "narrow"), P("member", "wide", "narrow"))
    return jax.shard_map(body, mesh=mesh, in_specs=in_specs, out_specs=out_specs, check_vma=False)
```

```python
import functools

import jax
import jax.numpy as jnp
from jax import lax
from jax.experimental import pallas as pl
from jax.experimental.pallas import tpu as pltpu
from jax.sharding import PartitionSpec as P

STEPS = 2


STEP_SIZE = 0.03
CAP_LOG = 1.5
CHUNK_Z = 32
EDGE_Z = 32
DEPTH_X = 16


def permeability(values):
    return jnp.exp(CAP_LOG * jnp.tanh(values / CAP_LOG))


def harmonic(a, b):
    return 2.0 * a * b / (a + b)


def halos(edges):
    forward_w = [(i, i + 1) for i in range(lax.axis_size("wide") - 1)]
    backward_w = [(j, i) for i, j in forward_w]
    forward_n = [(i, i + 1) for i in range(lax.axis_size("narrow") - 1)]
    backward_n = [(j, i) for i, j in forward_n]
    first_x, last_x, first_y, last_y = edges
    x_lo = lax.ppermute(last_x, "wide", forward_w)
    x_hi = lax.ppermute(first_x, "wide", backward_w)
    y_lo = lax.ppermute(last_y, "narrow", forward_n)
    y_hi = lax.ppermute(first_y, "narrow", backward_n)
    return x_lo, x_hi, y_lo, y_hi


def to_columns(rows):
    tz, nx = rows.shape
    eye = jnp.where(
        lax.broadcasted_iota(jnp.int32, (nx, nx), 0) == lax.broadcasted_iota(jnp.int32, (nx, nx), 1),
        1.0, 0.0,
    )
    cols = lax.dot_general(
        eye, rows, (((1,), (1,)), ((), ())),
        precision=lax.Precision.HIGHEST, preferred_element_type=jnp.float32,
    )
    return jnp.concatenate([cols[:, k : k + 1][None] for k in range(tz)], axis=0)


def x_rows(ref):
    return jnp.concatenate([ref[k : k + 1, :][None] for k in range(ref.shape[0])], axis=0)


def store_x_rows(ref, rows):
    for k in range(ref.shape[0]):
        ref[k : k + 1, :] = rows[k]


def to_rows(block):
    tz, nx, ny = block.shape
    lane = lax.broadcasted_iota(jnp.int32, (nx, 128), 1)
    pick = jnp.where(
        lax.broadcasted_iota(jnp.int32, (tz, 128), 0) == lax.broadcasted_iota(jnp.int32, (tz, 128), 1),
        1.0, 0.0,
    )
    result = []
    for column in (0, ny - 1):
        gathered = jnp.zeros((nx, 128), jnp.float32)
        for k in range(tz):
            gathered = jnp.where(lane == k, block[k, :, column : column + 1], gathered)
        result.append(
            lax.dot_general(
                pick, gathered, (((1,), (1,)), ((), ())),
                precision=lax.Precision.HIGHEST, preferred_element_type=jnp.float32,
            )
        )
    return result[0], result[1]


def edge_kernel(block_ref, xl_ref, xh_ref, yl_ref, yh_ref, *copy_ref):
    block = block_ref[...]
    if copy_ref:
        copy_ref[0][...] = block
    block = block.astype(jnp.float32)
    store_x_rows(xl_ref, block[:, :1, :])
    store_x_rows(xh_ref, block[:, -1:, :])
    yl_ref[...], yh_ref[...] = to_rows(block)


def block_edges(block, keep=False):
    depth, nx, ny = block.shape
    tz = EDGE_Z
    f32 = jnp.float32
    whole = pl.BlockSpec((tz, nx, ny), lambda c: (c, 0, 0))
    row = pl.BlockSpec((tz, ny), lambda c: (c, 0))
    col = pl.BlockSpec((tz, nx), lambda c: (c, 0))
    out_shape = [
        jax.ShapeDtypeStruct((depth, ny), f32),
        jax.ShapeDtypeStruct((depth, ny), f32),
        jax.ShapeDtypeStruct((depth, nx), f32),
        jax.ShapeDtypeStruct((depth, nx), f32),
    ]
    out_specs = [row, row, col, col]
    if keep:
        out_shape.append(jax.ShapeDtypeStruct(block.shape, block.dtype))
        out_specs.append(whole)
    return pl.pallas_call(
        edge_kernel,
        out_shape=tuple(out_shape),
        grid=(depth // tz,),
        in_specs=[whole],
        out_specs=out_specs,
        compiler_params=pltpu.CompilerParams(dimension_semantics=("arbitrary",)),
    )(block)


def update(trans, pm_ref, pb_ref, pa_ref, qxl_ref, qxh_ref, qyl_ref, qyh_ref, f_ref, outs):
    o_ref, exl_ref, exh_ref, eyl_ref, eyh_ref = outs
    t_zp, t_zm, t_xp, t_xm, t_yp, t_ym = trans
    tz, nx, ny = pm_ref.shape
    f32 = jnp.float32
    xi = lax.broadcasted_iota(jnp.int32, (tz, nx, ny), 1)
    yi = lax.broadcasted_iota(jnp.int32, (tz, nx, ny), 2)
    p = pm_ref[...].astype(f32)
    pext = jnp.concatenate([pb_ref[...].astype(f32), p, pa_ref[...].astype(f32)], axis=0)
    n_xp = jnp.where(xi == nx - 1, x_rows(qxh_ref), pltpu.roll(p, nx - 1, 1))
    n_xm = jnp.where(xi == 0, x_rows(qxl_ref), pltpu.roll(p, 1, 1))
    n_yp = jnp.where(yi == ny - 1, to_columns(qyh_ref[...]), pltpu.roll(p, ny - 1, 2))
    n_ym = jnp.where(yi == 0, to_columns(qyl_ref[...]), pltpu.roll(p, 1, 2))

    flux = t_zp * (pext[2:] - p)
    flux = flux + t_zm * (pext[:-2] - p)
    flux = flux + t_xp * (n_xp - p)
    flux = flux + t_xm * (n_xm - p)
    flux = flux + t_yp * (n_yp - p)
    flux = flux + t_ym * (n_ym - p)
    new = p + STEP_SIZE * (flux + f_ref[...]) / (1.0 + 0.5 * p * p)
    o_ref[...] = new
    store_x_rows(exl_ref, new[:, :1, :])
    store_x_rows(exh_ref, new[:, nx - 1 :, :])
    eyl_ref[...], eyh_ref[...] = to_rows(new)


def first_step_kernel(
    inside_ref, lpm_ref, lpb_ref, lpa_ref, lxl_ref, lxh_ref, lyl_ref, lyh_ref,
    pm_ref, pb_ref, pa_ref, qxl_ref, qxh_ref, qyl_ref, qyh_ref, f_ref,
    o_ref, exl_ref, exh_ref, eyl_ref, eyh_ref, tzm_ref, txm_ref, tym_ref, txp_ref, typ_ref,
):
    c = pl.program_id(0)
    last = pl.num_programs(0) - 1
    tz, nx, ny = pm_ref.shape
    f32 = jnp.float32

    def side_perm(ref, k):
        return jnp.where(inside_ref[k] > 0, permeability(ref[...].astype(f32)), 0.0)

    kxl = jnp.where(inside_ref[0] > 0, permeability(x_rows(lxl_ref)), 0.0)
    kxh = jnp.where(inside_ref[1] > 0, permeability(x_rows(lxh_ref)), 0.0)
    kyl = to_columns(side_perm(lyl_ref, 2))
    kyh = to_columns(side_perm(lyh_ref, 3))

    below = jnp.where(c == 0, 0.0, permeability(lpb_ref[...].astype(f32)))
    above = jnp.where(c == last, 0.0, permeability(lpa_ref[...].astype(f32)))
    centre = permeability(lpm_ref[...].astype(f32))
    ext = jnp.concatenate([below, centre, above], axis=0)
    faces = harmonic(ext[:-1], ext[1:])
    t_zm = faces[:-1]
    t_zp = faces[1:]

    xi = lax.broadcasted_iota(jnp.int32, (tz, nx, ny), 1)
    yi = lax.broadcasted_iota(jnp.int32, (tz, nx, ny), 2)

    fx = harmonic(centre, pltpu.roll(centre, nx - 1, 1))
    t_xp = jnp.where(xi == nx - 1, harmonic(centre[:, nx - 1 :, :], kxh), fx)
    t_xm = jnp.where(xi == 0, harmonic(centre[:, :1, :], kxl), pltpu.roll(fx, 1, 1))
    fy = harmonic(centre, pltpu.roll(centre, ny - 1, 2))
    t_yp = jnp.where(yi == ny - 1, harmonic(centre[:, :, ny - 1 :], kyh), fy)
    t_ym = jnp.where(yi == 0, harmonic(centre[:, :, :1], kyl), pltpu.roll(fy, 1, 2))

    tzm_ref[...] = t_zm
    txm_ref[...] = t_xm
    tym_ref[...] = t_ym
    store_x_rows(txp_ref, t_xp[:, nx - 1 :, :])
    typ_ref[...] = to_rows(t_yp)[1]
    update(
        (t_zp, t_zm, t_xp, t_xm, t_yp, t_ym),
        pm_ref, pb_ref, pa_ref, qxl_ref, qxh_ref, qyl_ref, qyh_ref, f_ref,
        (o_ref, exl_ref, exh_ref, eyl_ref, eyh_ref),
    )


def later_step_kernel(
    tzm_ref, tza_ref, txm_ref, tym_ref, txp_ref, typ_ref,
    pm_ref, pb_ref, pa_ref, qxl_ref, qxh_ref, qyl_ref, qyh_ref, f_ref,
    o_ref, exl_ref, exh_ref, eyl_ref, eyh_ref,
):
    c = pl.program_id(0)
    last = pl.num_programs(0) - 1
    tz, nx, ny = pm_ref.shape
    xi = lax.broadcasted_iota(jnp.int32, (tz, nx, ny), 1)
    yi = lax.broadcasted_iota(jnp.int32, (tz, nx, ny), 2)
    t_zm = tzm_ref[...]
    t_zp = jnp.concatenate([t_zm[1:], jnp.where(c == last, 0.0, tza_ref[...])], axis=0)
    t_xm = txm_ref[...]
    t_xp = jnp.where(xi == nx - 1, x_rows(txp_ref), pltpu.roll(t_xm, nx - 1, 1))
    t_ym = tym_ref[...]
    t_yp = jnp.where(yi == ny - 1, to_columns(typ_ref[...]), pltpu.roll(t_ym, ny - 1, 2))
    update(
        (t_zp, t_zm, t_xp, t_xm, t_yp, t_ym),
        pm_ref, pb_ref, pa_ref, qxl_ref, qxh_ref, qyl_ref, qyh_ref, f_ref,
        (o_ref, exl_ref, exh_ref, eyl_ref, eyh_ref),
    )


def advance(stored, pressure, pressure_halos, flow, inside=None, log_perm=None, perm_halos=None):
    depth, nx, ny = pressure.shape
    tz = CHUNK_Z
    grid = (depth // tz,)
    main = pl.BlockSpec((tz, nx, ny), lambda c: (c, 0, 0))
    below = pl.BlockSpec((1, nx, ny), lambda c: (jnp.maximum(c * tz - 1, 0), 0, 0))
    above = pl.BlockSpec((1, nx, ny), lambda c: (jnp.minimum(c * tz + tz, depth - 1), 0, 0))
    row = pl.BlockSpec((tz, ny), lambda c: (c, 0))
    col = pl.BlockSpec((tz, nx), lambda c: (c, 0))
    side = [row, row, col, col]
    smem = pl.BlockSpec(memory_space=pltpu.SMEM)
    f32 = jnp.float32
    full = jax.ShapeDtypeStruct((depth, nx, ny), f32)
    rows = jax.ShapeDtypeStruct((depth, ny), f32)
    cols = jax.ShapeDtypeStruct((depth, nx), f32)
    out_shape = [full, rows, rows, cols, cols]
    out_specs = [main] + side
    pressure_args = [pressure, pressure, pressure, *pressure_halos, flow]
    pressure_specs = [main, below, above] + side + [main]
    params = pltpu.CompilerParams(dimension_semantics=("arbitrary",))
    if stored is None:
        outs = pl.pallas_call(
            first_step_kernel,
            out_shape=tuple(out_shape + [full, full, full, rows, cols]),
            grid=grid,
            in_specs=[smem, main, below, above] + side + pressure_specs,
            out_specs=out_specs + [main, main, main, row, col],
            compiler_params=params,
        )(inside, log_perm, log_perm, log_perm, *perm_halos, *pressure_args)
        return outs[0], outs[1:5], outs[5:]
    t_zm, t_xm, t_ym, t_xp, t_yp = stored
    outs = pl.pallas_call(
        later_step_kernel,
        out_shape=tuple(out_shape),
        grid=grid,
        in_specs=[main, above, main, main, row, col] + pressure_specs,
        out_specs=out_specs,
        compiler_params=params,
    )(t_zm, t_zm, t_xm, t_ym, t_xp, t_yp, *pressure_args)
    return outs[0], outs[1:5], stored


def depth_kernel(rz_ref, n_ref, o_ref):
    rz = rz_ref[...]
    for i in range(n_ref.shape[1]):
        o_ref[:, i, :] = jnp.dot(rz, n_ref[:, i, :], preferred_element_type=jnp.float32).astype(
            jnp.bfloat16
        )


def depth_transform(root_z, noise):
    depth, nx, ny = noise.shape
    bx = min(nx, DEPTH_X)
    block = pl.BlockSpec((depth, bx, ny), lambda i: (0, i, 0))
    return pl.pallas_call(
        depth_kernel,
        out_shape=jax.ShapeDtypeStruct(noise.shape, jnp.bfloat16),
        grid=(nx // bx,),
        in_specs=[pl.BlockSpec(root_z.shape, lambda i: (0, 0)), block],
        out_specs=block,
        compiler_params=pltpu.CompilerParams(dimension_semantics=("arbitrary",)),
    )(root_z, noise)


def line_kernel(g_ref, rx_ref, ry_ref, o_ref, *, count_w, count_n):
    f32 = jnp.float32
    nx = g_ref.shape[2]
    ny = g_ref.shape[3]
    rx = rx_ref[...]
    halves = []
    for n in range(count_n):
        lines = jnp.concatenate([g_ref[w * count_n + n, 0] for w in range(count_w)], axis=0)
        halves.append(jnp.dot(rx, lines, preferred_element_type=f32).astype(jnp.bfloat16))
    second = jnp.concatenate(halves, axis=1)
    third = lax.dot_general(
        second, ry_ref[...], (((1,), (1,)), ((), ())), preferred_element_type=f32
    ).astype(jnp.bfloat16)
    for w in range(count_w):
        for n in range(count_n):
            o_ref[w * count_n + n, 0] = third[w * nx : (w + 1) * nx, n * ny : (n + 1) * ny]


def line_transforms(gathered, root_x, root_y, count_w, count_n):
    groups, planes, nx, ny = gathered.shape
    block = pl.BlockSpec((groups, 1, nx, ny), lambda z: (0, z, 0, 0))
    whole_x = pl.BlockSpec(root_x.shape, lambda z: (0, 0))
    whole_y = pl.BlockSpec(root_y.shape, lambda z: (0, 0))
    return pl.pallas_call(
        functools.partial(line_kernel, count_w=count_w, count_n=count_n),
        out_shape=jax.ShapeDtypeStruct(gathered.shape, jnp.bfloat16),
        grid=(planes,),
        in_specs=[block, whole_x, whole_y],
        out_specs=block,
        compiler_params=pltpu.CompilerParams(dimension_semantics=("arbitrary",)),
    )(gathered, root_x, root_y)


def body(noise, root_z, root_x, root_y, pressure_start, well_x, well_y, well_z, well_rate):
    depth, rows_x, rows_y = noise.shape
    first = depth_transform(root_z, noise)
    count_w = lax.axis_size("wide")
    count_n = lax.axis_size("narrow")
    groups = count_w * count_n
    planes = depth // groups
    gathered = lax.all_to_all(
        first.reshape(groups, planes, rows_x, rows_y),
        ("wide", "narrow"), split_axis=0, concat_axis=0, tiled=True,
    )
    wide_at = lax.axis_index("wide")
    narrow_at = lax.axis_index("narrow")
    last_w = lax.axis_size("wide") - 1
    last_n = lax.axis_size("narrow") - 1

    local_x = well_x - wide_at * rows_x
    local_y = well_y - narrow_at * rows_y
    valid = (local_x >= 0) & (local_x < rows_x) & (local_y >= 0) & (local_y < rows_y)
    rates = jnp.where(valid, well_rate, 0.0).astype(jnp.float32)
    wells = well_x.shape[0]
    cells = well_z * rows_x + local_x
    pick_rows = jnp.where(
        lax.broadcasted_iota(jnp.int32, (depth * rows_x, wells), 0) == cells[None, :],
        rates[None, :],
        0.0,
    )
    pick_cols = (
        lax.broadcasted_iota(jnp.int32, (wells, rows_y), 1) == local_y[:, None]
    ).astype(jnp.float32)
    flow = jnp.dot(
        pick_rows, pick_cols, precision=lax.Precision.HIGHEST, preferred_element_type=jnp.float32
    ).reshape(depth, rows_x, rows_y)

    inside = jnp.stack(
        [wide_at > 0, wide_at < last_w, narrow_at > 0, narrow_at < last_n]
    ).astype(jnp.int32)
    edges = block_edges(pressure_start)
    gathered, flow, edges = lax.optimization_barrier((gathered, flow, edges))
    outgoing = line_transforms(gathered, root_x, root_y, count_w, count_n)
    log_perm = lax.all_to_all(
        outgoing, ("wide", "narrow"), split_axis=0, concat_axis=0, tiled=True,
    ).reshape(depth, rows_x, rows_y)

    *lp_edges, log_perm = block_edges(log_perm, keep=True)
    perm_halos = halos(lp_edges)
    pressure = pressure_start
    stored = None
    for step in range(STEPS):
        pressure, edges, stored = advance(
            stored, pressure, halos(edges), flow, inside, log_perm, perm_halos
        )
    return (log_perm, pressure)


def solution(mesh):
    in_specs = (
        P("member", "wide", "narrow"),
        P(),
        P(),
        P(),
        P("member", "wide", "narrow"),
        P("member"),
        P("member"),
        P("member"),
        P("member"),
    )
    out_specs = (P("member", "wide", "narrow"), P("member", "wide", "narrow"))
    return jax.shard_map(body, mesh=mesh, in_specs=in_specs, out_specs=out_specs, check_vma=False)
```

```python
import functools

import jax
import jax.numpy as jnp
from jax import lax
from jax.experimental import pallas as pl
from jax.experimental.pallas import tpu as pltpu
from jax.sharding import PartitionSpec as P

STEPS = 2


STEP_SIZE = 0.03
CAP_LOG = 1.5
CHUNK_Z = 16
EDGE_Z = 64
DEPTH_X = 16


def permeability(values):
    return jnp.exp(CAP_LOG * jnp.tanh(values / CAP_LOG))


def harmonic(a, b):
    return 2.0 * a * b / (a + b)


def halos(edges):
    forward_w = [(i, i + 1) for i in range(lax.axis_size("wide") - 1)]
    backward_w = [(j, i) for i, j in forward_w]
    forward_n = [(i, i + 1) for i in range(lax.axis_size("narrow") - 1)]
    backward_n = [(j, i) for i, j in forward_n]
    first_x, last_x, first_y, last_y = edges
    x_lo = lax.ppermute(last_x, "wide", forward_w)
    x_hi = lax.ppermute(first_x, "wide", backward_w)
    y_lo = lax.ppermute(last_y, "narrow", forward_n)
    y_hi = lax.ppermute(first_y, "narrow", backward_n)
    return x_lo, x_hi, y_lo, y_hi


def to_columns(rows):
    tz, nx = rows.shape
    eye = jnp.where(
        lax.broadcasted_iota(jnp.int32, (nx, nx), 0) == lax.broadcasted_iota(jnp.int32, (nx, nx), 1),
        1.0, 0.0,
    )
    cols = lax.dot_general(
        eye, rows, (((1,), (1,)), ((), ())),
        precision=lax.Precision.HIGHEST, preferred_element_type=jnp.float32,
    )
    return jnp.concatenate([cols[:, k : k + 1][None] for k in range(tz)], axis=0)


def x_rows(ref):
    return jnp.concatenate([ref[k : k + 1, :][None] for k in range(ref.shape[0])], axis=0)


def store_x_rows(ref, rows):
    for k in range(ref.shape[0]):
        ref[k : k + 1, :] = rows[k]


def to_rows(block):
    tz, nx, ny = block.shape
    lane = lax.broadcasted_iota(jnp.int32, (nx, 128), 1)
    pick = jnp.where(
        lax.broadcasted_iota(jnp.int32, (tz, 128), 0) == lax.broadcasted_iota(jnp.int32, (tz, 128), 1),
        1.0, 0.0,
    )
    result = []
    for column in (0, ny - 1):
        gathered = jnp.zeros((nx, 128), jnp.float32)
        for k in range(tz):
            gathered = jnp.where(lane == k, block[k, :, column : column + 1], gathered)
        result.append(
            lax.dot_general(
                pick, gathered, (((1,), (1,)), ((), ())),
                precision=lax.Precision.HIGHEST, preferred_element_type=jnp.float32,
            )
        )
    return result[0], result[1]


def edge_kernel(block_ref, xl_ref, xh_ref, yl_ref, yh_ref, *copy_ref):
    block = block_ref[...]
    if copy_ref:
        copy_ref[0][...] = block
    block = block.astype(jnp.float32)
    store_x_rows(xl_ref, block[:, :1, :])
    store_x_rows(xh_ref, block[:, -1:, :])
    yl_ref[...], yh_ref[...] = to_rows(block)


def block_edges(block, keep=False):
    depth, nx, ny = block.shape
    tz = EDGE_Z
    f32 = jnp.float32
    whole = pl.BlockSpec((tz, nx, ny), lambda c: (c, 0, 0))
    row = pl.BlockSpec((tz, ny), lambda c: (c, 0))
    col = pl.BlockSpec((tz, nx), lambda c: (c, 0))
    out_shape = [
        jax.ShapeDtypeStruct((depth, ny), f32),
        jax.ShapeDtypeStruct((depth, ny), f32),
        jax.ShapeDtypeStruct((depth, nx), f32),
        jax.ShapeDtypeStruct((depth, nx), f32),
    ]
    out_specs = [row, row, col, col]
    if keep:
        out_shape.append(jax.ShapeDtypeStruct(block.shape, block.dtype))
        out_specs.append(whole)
    return pl.pallas_call(
        edge_kernel,
        out_shape=tuple(out_shape),
        grid=(depth // tz,),
        in_specs=[whole],
        out_specs=out_specs,
        compiler_params=pltpu.CompilerParams(dimension_semantics=("arbitrary",)),
    )(block)


def update(trans, pm_ref, pb_ref, pa_ref, qxl_ref, qxh_ref, qyl_ref, qyh_ref, f_ref, outs):
    o_ref, exl_ref, exh_ref, eyl_ref, eyh_ref = outs
    t_zp, t_zm, t_xp, t_xm, t_yp, t_ym = trans
    tz, nx, ny = pm_ref.shape
    f32 = jnp.float32
    xi = lax.broadcasted_iota(jnp.int32, (tz, nx, ny), 1)
    yi = lax.broadcasted_iota(jnp.int32, (tz, nx, ny), 2)
    p = pm_ref[...].astype(f32)
    pext = jnp.concatenate([pb_ref[...].astype(f32), p, pa_ref[...].astype(f32)], axis=0)
    n_xp = jnp.where(xi == nx - 1, x_rows(qxh_ref), pltpu.roll(p, nx - 1, 1))
    n_xm = jnp.where(xi == 0, x_rows(qxl_ref), pltpu.roll(p, 1, 1))
    n_yp = jnp.where(yi == ny - 1, to_columns(qyh_ref[...]), pltpu.roll(p, ny - 1, 2))
    n_ym = jnp.where(yi == 0, to_columns(qyl_ref[...]), pltpu.roll(p, 1, 2))

    flux = t_zp * (pext[2:] - p)
    flux = flux + t_zm * (pext[:-2] - p)
    flux = flux + t_xp * (n_xp - p)
    flux = flux + t_xm * (n_xm - p)
    flux = flux + t_yp * (n_yp - p)
    flux = flux + t_ym * (n_ym - p)
    new = p + STEP_SIZE * (flux + f_ref[...]) / (1.0 + 0.5 * p * p)
    o_ref[...] = new
    store_x_rows(exl_ref, new[:, :1, :])
    store_x_rows(exh_ref, new[:, nx - 1 :, :])
    eyl_ref[...], eyh_ref[...] = to_rows(new)


def first_step_kernel(
    inside_ref, lpm_ref, lpb_ref, lpa_ref, lxl_ref, lxh_ref, lyl_ref, lyh_ref,
    pm_ref, pb_ref, pa_ref, qxl_ref, qxh_ref, qyl_ref, qyh_ref, f_ref,
    o_ref, exl_ref, exh_ref, eyl_ref, eyh_ref, tzm_ref, txm_ref, tym_ref, txp_ref, typ_ref,
):
    c = pl.program_id(0)
    last = pl.num_programs(0) - 1
    tz, nx, ny = pm_ref.shape
    f32 = jnp.float32

    def side_perm(ref, k):
        return jnp.where(inside_ref[k] > 0, permeability(ref[...].astype(f32)), 0.0)

    kxl = jnp.where(inside_ref[0] > 0, permeability(x_rows(lxl_ref)), 0.0)
    kxh = jnp.where(inside_ref[1] > 0, permeability(x_rows(lxh_ref)), 0.0)
    kyl = to_columns(side_perm(lyl_ref, 2))
    kyh = to_columns(side_perm(lyh_ref, 3))

    below = jnp.where(c == 0, 0.0, permeability(lpb_ref[...].astype(f32)))
    above = jnp.where(c == last, 0.0, permeability(lpa_ref[...].astype(f32)))
    centre = permeability(lpm_ref[...].astype(f32))
    ext = jnp.concatenate([below, centre, above], axis=0)
    faces = harmonic(ext[:-1], ext[1:])
    t_zm = faces[:-1]
    t_zp = faces[1:]

    xi = lax.broadcasted_iota(jnp.int32, (tz, nx, ny), 1)
    yi = lax.broadcasted_iota(jnp.int32, (tz, nx, ny), 2)

    fx = harmonic(centre, pltpu.roll(centre, nx - 1, 1))
    t_xp = jnp.where(xi == nx - 1, harmonic(centre[:, nx - 1 :, :], kxh), fx)
    t_xm = jnp.where(xi == 0, harmonic(centre[:, :1, :], kxl), pltpu.roll(fx, 1, 1))
    fy = harmonic(centre, pltpu.roll(centre, ny - 1, 2))
    t_yp = jnp.where(yi == ny - 1, harmonic(centre[:, :, ny - 1 :], kyh), fy)
    t_ym = jnp.where(yi == 0, harmonic(centre[:, :, :1], kyl), pltpu.roll(fy, 1, 2))

    tzm_ref[...] = t_zm
    txm_ref[...] = t_xm
    tym_ref[...] = t_ym
    store_x_rows(txp_ref, t_xp[:, nx - 1 :, :])
    typ_ref[...] = to_rows(t_yp)[1]
    update(
        (t_zp, t_zm, t_xp, t_xm, t_yp, t_ym),
        pm_ref, pb_ref, pa_ref, qxl_ref, qxh_ref, qyl_ref, qyh_ref, f_ref,
        (o_ref, exl_ref, exh_ref, eyl_ref, eyh_ref),
    )


def later_step_kernel(
    tzm_ref, tza_ref, txm_ref, tym_ref, txp_ref, typ_ref,
    pm_ref, pb_ref, pa_ref, qxl_ref, qxh_ref, qyl_ref, qyh_ref, f_ref,
    o_ref, exl_ref, exh_ref, eyl_ref, eyh_ref,
):
    c = pl.program_id(0)
    last = pl.num_programs(0) - 1
    tz, nx, ny = pm_ref.shape
    xi = lax.broadcasted_iota(jnp.int32, (tz, nx, ny), 1)
    yi = lax.broadcasted_iota(jnp.int32, (tz, nx, ny), 2)
    t_zm = tzm_ref[...]
    t_zp = jnp.concatenate([t_zm[1:], jnp.where(c == last, 0.0, tza_ref[...])], axis=0)
    t_xm = txm_ref[...]
    t_xp = jnp.where(xi == nx - 1, x_rows(txp_ref), pltpu.roll(t_xm, nx - 1, 1))
    t_ym = tym_ref[...]
    t_yp = jnp.where(yi == ny - 1, to_columns(typ_ref[...]), pltpu.roll(t_ym, ny - 1, 2))
    update(
        (t_zp, t_zm, t_xp, t_xm, t_yp, t_ym),
        pm_ref, pb_ref, pa_ref, qxl_ref, qxh_ref, qyl_ref, qyh_ref, f_ref,
        (o_ref, exl_ref, exh_ref, eyl_ref, eyh_ref),
    )


def advance(stored, pressure, pressure_halos, flow, inside=None, log_perm=None, perm_halos=None):
    depth, nx, ny = pressure.shape
    tz = CHUNK_Z
    grid = (depth // tz,)
    main = pl.BlockSpec((tz, nx, ny), lambda c: (c, 0, 0))
    below = pl.BlockSpec((1, nx, ny), lambda c: (jnp.maximum(c * tz - 1, 0), 0, 0))
    above = pl.BlockSpec((1, nx, ny), lambda c: (jnp.minimum(c * tz + tz, depth - 1), 0, 0))
    row = pl.BlockSpec((tz, ny), lambda c: (c, 0))
    col = pl.BlockSpec((tz, nx), lambda c: (c, 0))
    side = [row, row, col, col]
    smem = pl.BlockSpec(memory_space=pltpu.SMEM)
    f32 = jnp.float32
    full = jax.ShapeDtypeStruct((depth, nx, ny), f32)
    rows = jax.ShapeDtypeStruct((depth, ny), f32)
    cols = jax.ShapeDtypeStruct((depth, nx), f32)
    out_shape = [full, rows, rows, cols, cols]
    out_specs = [main] + side
    pressure_args = [pressure, pressure, pressure, *pressure_halos, flow]
    pressure_specs = [main, below, above] + side + [main]
    params = pltpu.CompilerParams(dimension_semantics=("arbitrary",))
    if stored is None:
        outs = pl.pallas_call(
            first_step_kernel,
            out_shape=tuple(out_shape + [full, full, full, rows, cols]),
            grid=grid,
            in_specs=[smem, main, below, above] + side + pressure_specs,
            out_specs=out_specs + [main, main, main, row, col],
            compiler_params=params,
        )(inside, log_perm, log_perm, log_perm, *perm_halos, *pressure_args)
        return outs[0], outs[1:5], outs[5:]
    t_zm, t_xm, t_ym, t_xp, t_yp = stored
    outs = pl.pallas_call(
        later_step_kernel,
        out_shape=tuple(out_shape),
        grid=grid,
        in_specs=[main, above, main, main, row, col] + pressure_specs,
        out_specs=out_specs,
        compiler_params=params,
    )(t_zm, t_zm, t_xm, t_ym, t_xp, t_yp, *pressure_args)
    return outs[0], outs[1:5], stored


def depth_kernel(rz_ref, n_ref, o_ref):
    rz = rz_ref[...]
    for i in range(n_ref.shape[1]):
        o_ref[:, i, :] = jnp.dot(rz, n_ref[:, i, :], preferred_element_type=jnp.float32).astype(
            jnp.bfloat16
        )


def depth_transform(root_z, noise):
    depth, nx, ny = noise.shape
    bx = min(nx, DEPTH_X)
    block = pl.BlockSpec((depth, bx, ny), lambda i: (0, i, 0))
    return pl.pallas_call(
        depth_kernel,
        out_shape=jax.ShapeDtypeStruct(noise.shape, jnp.bfloat16),
        grid=(nx // bx,),
        in_specs=[pl.BlockSpec(root_z.shape, lambda i: (0, 0)), block],
        out_specs=block,
        compiler_params=pltpu.CompilerParams(dimension_semantics=("arbitrary",)),
    )(root_z, noise)


def line_kernel(g_ref, rx_ref, ry_ref, o_ref, *, count_w, count_n):
    f32 = jnp.float32
    nx = g_ref.shape[2]
    ny = g_ref.shape[3]
    rx = rx_ref[...]
    halves = []
    for n in range(count_n):
        lines = jnp.concatenate([g_ref[w * count_n + n, 0] for w in range(count_w)], axis=0)
        halves.append(jnp.dot(rx, lines, preferred_element_type=f32).astype(jnp.bfloat16))
    second = jnp.concatenate(halves, axis=1)
    third = lax.dot_general(
        second, ry_ref[...], (((1,), (1,)), ((), ())), preferred_element_type=f32
    ).astype(jnp.bfloat16)
    for w in range(count_w):
        for n in range(count_n):
            o_ref[w * count_n + n, 0] = third[w * nx : (w + 1) * nx, n * ny : (n + 1) * ny]


def line_transforms(gathered, root_x, root_y, count_w, count_n):
    groups, planes, nx, ny = gathered.shape
    block = pl.BlockSpec((groups, 1, nx, ny), lambda z: (0, z, 0, 0))
    whole_x = pl.BlockSpec(root_x.shape, lambda z: (0, 0))
    whole_y = pl.BlockSpec(root_y.shape, lambda z: (0, 0))
    return pl.pallas_call(
        functools.partial(line_kernel, count_w=count_w, count_n=count_n),
        out_shape=jax.ShapeDtypeStruct(gathered.shape, jnp.bfloat16),
        grid=(planes,),
        in_specs=[block, whole_x, whole_y],
        out_specs=block,
        compiler_params=pltpu.CompilerParams(dimension_semantics=("arbitrary",)),
    )(gathered, root_x, root_y)


def body(noise, root_z, root_x, root_y, pressure_start, well_x, well_y, well_z, well_rate):
    depth, rows_x, rows_y = noise.shape
    first = depth_transform(root_z, noise)
    count_w = lax.axis_size("wide")
    count_n = lax.axis_size("narrow")
    groups = count_w * count_n
    planes = depth // groups
    gathered = lax.all_to_all(
        first.reshape(groups, planes, rows_x, rows_y),
        ("wide", "narrow"), split_axis=0, concat_axis=0, tiled=True,
    )
    wide_at = lax.axis_index("wide")
    narrow_at = lax.axis_index("narrow")
    last_w = lax.axis_size("wide") - 1
    last_n = lax.axis_size("narrow") - 1

    local_x = well_x - wide_at * rows_x
    local_y = well_y - narrow_at * rows_y
    valid = (local_x >= 0) & (local_x < rows_x) & (local_y >= 0) & (local_y < rows_y)
    rates = jnp.where(valid, well_rate, 0.0).astype(jnp.float32)
    wells = well_x.shape[0]
    cells = well_z * rows_x + local_x
    pick_rows = jnp.where(
        lax.broadcasted_iota(jnp.int32, (depth * rows_x, wells), 0) == cells[None, :],
        rates[None, :],
        0.0,
    )
    pick_cols = (
        lax.broadcasted_iota(jnp.int32, (wells, rows_y), 1) == local_y[:, None]
    ).astype(jnp.float32)
    flow = jnp.dot(
        pick_rows, pick_cols, precision=lax.Precision.HIGHEST, preferred_element_type=jnp.float32
    ).reshape(depth, rows_x, rows_y)

    inside = jnp.stack(
        [wide_at > 0, wide_at < last_w, narrow_at > 0, narrow_at < last_n]
    ).astype(jnp.int32)
    edges = block_edges(pressure_start)
    gathered, flow, edges = lax.optimization_barrier((gathered, flow, edges))
    outgoing = line_transforms(gathered, root_x, root_y, count_w, count_n)
    log_perm = lax.all_to_all(
        outgoing, ("wide", "narrow"), split_axis=0, concat_axis=0, tiled=True,
    ).reshape(depth, rows_x, rows_y)

    *lp_edges, log_perm = block_edges(log_perm, keep=True)
    perm_halos = halos(lp_edges)
    pressure = pressure_start
    stored = None
    for step in range(STEPS):
        pressure, edges, stored = advance(
            stored, pressure, halos(edges), flow, inside, log_perm, perm_halos
        )
    return (log_perm, pressure)


def solution(mesh):
    in_specs = (
        P("member", "wide", "narrow"),
        P(),
        P(),
        P(),
        P("member", "wide", "narrow"),
        P("member"),
        P("member"),
        P("member"),
        P("member"),
    )
    out_specs = (P("member", "wide", "narrow"), P("member", "wide", "narrow"))
    return jax.shard_map(body, mesh=mesh, in_specs=in_specs, out_specs=out_specs, check_vma=False)
```

```python
import functools

import jax
import jax.numpy as jnp
from jax import lax
from jax.experimental import pallas as pl
from jax.experimental.pallas import tpu as pltpu
from jax.sharding import PartitionSpec as P

STEPS = 2


STEP_SIZE = 0.03
CAP_LOG = 1.5
CHUNK_Z = 16
EDGE_Z = 128
DEPTH_X = 16


def permeability(values):
    return jnp.exp(CAP_LOG * jnp.tanh(values / CAP_LOG))


def harmonic(a, b):
    return 2.0 * a * b / (a + b)


def halos(edges):
    forward_w = [(i, i + 1) for i in range(lax.axis_size("wide") - 1)]
    backward_w = [(j, i) for i, j in forward_w]
    forward_n = [(i, i + 1) for i in range(lax.axis_size("narrow") - 1)]
    backward_n = [(j, i) for i, j in forward_n]
    first_x, last_x, first_y, last_y = edges
    x_lo = lax.ppermute(last_x, "wide", forward_w)
    x_hi = lax.ppermute(first_x, "wide", backward_w)
    y_lo = lax.ppermute(last_y, "narrow", forward_n)
    y_hi = lax.ppermute(first_y, "narrow", backward_n)
    return x_lo, x_hi, y_lo, y_hi


def to_columns(rows):
    tz, nx = rows.shape
    eye = jnp.where(
        lax.broadcasted_iota(jnp.int32, (nx, nx), 0) == lax.broadcasted_iota(jnp.int32, (nx, nx), 1),
        1.0, 0.0,
    )
    cols = lax.dot_general(
        eye, rows, (((1,), (1,)), ((), ())),
        precision=lax.Precision.HIGHEST, preferred_element_type=jnp.float32,
    )
    return jnp.concatenate([cols[:, k : k + 1][None] for k in range(tz)], axis=0)


def x_rows(ref):
    return jnp.concatenate([ref[k : k + 1, :][None] for k in range(ref.shape[0])], axis=0)


def store_x_rows(ref, rows):
    for k in range(ref.shape[0]):
        ref[k : k + 1, :] = rows[k]


def to_rows(block):
    tz, nx, ny = block.shape
    lane = lax.broadcasted_iota(jnp.int32, (nx, 128), 1)
    pick = jnp.where(
        lax.broadcasted_iota(jnp.int32, (tz, 128), 0) == lax.broadcasted_iota(jnp.int32, (tz, 128), 1),
        1.0, 0.0,
    )
    result = []
    for column in (0, ny - 1):
        gathered = jnp.zeros((nx, 128), jnp.float32)
        for k in range(tz):
            gathered = jnp.where(lane == k, block[k, :, column : column + 1], gathered)
        result.append(
            lax.dot_general(
                pick, gathered, (((1,), (1,)), ((), ())),
                precision=lax.Precision.HIGHEST, preferred_element_type=jnp.float32,
            )
        )
    return result[0], result[1]


def edge_kernel(block_ref, xl_ref, xh_ref, yl_ref, yh_ref, *copy_ref):
    block = block_ref[...]
    if copy_ref:
        copy_ref[0][...] = block
    block = block.astype(jnp.float32)
    store_x_rows(xl_ref, block[:, :1, :])
    store_x_rows(xh_ref, block[:, -1:, :])
    yl_ref[...], yh_ref[...] = to_rows(block)


def block_edges(block, keep=False):
    depth, nx, ny = block.shape
    tz = EDGE_Z
    f32 = jnp.float32
    whole = pl.BlockSpec((tz, nx, ny), lambda c: (c, 0, 0))
    row = pl.BlockSpec((tz, ny), lambda c: (c, 0))
    col = pl.BlockSpec((tz, nx), lambda c: (c, 0))
    out_shape = [
        jax.ShapeDtypeStruct((depth, ny), f32),
        jax.ShapeDtypeStruct((depth, ny), f32),
        jax.ShapeDtypeStruct((depth, nx), f32),
        jax.ShapeDtypeStruct((depth, nx), f32),
    ]
    out_specs = [row, row, col, col]
    if keep:
        out_shape.append(jax.ShapeDtypeStruct(block.shape, block.dtype))
        out_specs.append(whole)
    return pl.pallas_call(
        edge_kernel,
        out_shape=tuple(out_shape),
        grid=(depth // tz,),
        in_specs=[whole],
        out_specs=out_specs,
        compiler_params=pltpu.CompilerParams(dimension_semantics=("arbitrary",)),
    )(block)


def update(trans, pm_ref, pb_ref, pa_ref, qxl_ref, qxh_ref, qyl_ref, qyh_ref, f_ref, outs):
    o_ref, exl_ref, exh_ref, eyl_ref, eyh_ref = outs
    t_zp, t_zm, t_xp, t_xm, t_yp, t_ym = trans
    tz, nx, ny = pm_ref.shape
    f32 = jnp.float32
    xi = lax.broadcasted_iota(jnp.int32, (tz, nx, ny), 1)
    yi = lax.broadcasted_iota(jnp.int32, (tz, nx, ny), 2)
    p = pm_ref[...].astype(f32)
    pext = jnp.concatenate([pb_ref[...].astype(f32), p, pa_ref[...].astype(f32)], axis=0)
    n_xp = jnp.where(xi == nx - 1, x_rows(qxh_ref), pltpu.roll(p, nx - 1, 1))
    n_xm = jnp.where(xi == 0, x_rows(qxl_ref), pltpu.roll(p, 1, 1))
    n_yp = jnp.where(yi == ny - 1, to_columns(qyh_ref[...]), pltpu.roll(p, ny - 1, 2))
    n_ym = jnp.where(yi == 0, to_columns(qyl_ref[...]), pltpu.roll(p, 1, 2))

    flux = t_zp * (pext[2:] - p)
    flux = flux + t_zm * (pext[:-2] - p)
    flux = flux + t_xp * (n_xp - p)
    flux = flux + t_xm * (n_xm - p)
    flux = flux + t_yp * (n_yp - p)
    flux = flux + t_ym * (n_ym - p)
    new = p + STEP_SIZE * (flux + f_ref[...]) / (1.0 + 0.5 * p * p)
    o_ref[...] = new
    store_x_rows(exl_ref, new[:, :1, :])
    store_x_rows(exh_ref, new[:, nx - 1 :, :])
    eyl_ref[...], eyh_ref[...] = to_rows(new)


def first_step_kernel(
    inside_ref, lpm_ref, lpb_ref, lpa_ref, lxl_ref, lxh_ref, lyl_ref, lyh_ref,
    pm_ref, pb_ref, pa_ref, qxl_ref, qxh_ref, qyl_ref, qyh_ref, f_ref,
    o_ref, exl_ref, exh_ref, eyl_ref, eyh_ref, tzm_ref, txm_ref, tym_ref, txp_ref, typ_ref,
):
    c = pl.program_id(0)
    last = pl.num_programs(0) - 1
    tz, nx, ny = pm_ref.shape
    f32 = jnp.float32

    def side_perm(ref, k):
        return jnp.where(inside_ref[k] > 0, permeability(ref[...].astype(f32)), 0.0)

    kxl = jnp.where(inside_ref[0] > 0, permeability(x_rows(lxl_ref)), 0.0)
    kxh = jnp.where(inside_ref[1] > 0, permeability(x_rows(lxh_ref)), 0.0)
    kyl = to_columns(side_perm(lyl_ref, 2))
    kyh = to_columns(side_perm(lyh_ref, 3))

    below = jnp.where(c == 0, 0.0, permeability(lpb_ref[...].astype(f32)))
    above = jnp.where(c == last, 0.0, permeability(lpa_ref[...].astype(f32)))
    centre = permeability(lpm_ref[...].astype(f32))
    ext = jnp.concatenate([below, centre, above], axis=0)
    faces = harmonic(ext[:-1], ext[1:])
    t_zm = faces[:-1]
    t_zp = faces[1:]

    xi = lax.broadcasted_iota(jnp.int32, (tz, nx, ny), 1)
    yi = lax.broadcasted_iota(jnp.int32, (tz, nx, ny), 2)

    fx = harmonic(centre, pltpu.roll(centre, nx - 1, 1))
    t_xp = jnp.where(xi == nx - 1, harmonic(centre[:, nx - 1 :, :], kxh), fx)
    t_xm = jnp.where(xi == 0, harmonic(centre[:, :1, :], kxl), pltpu.roll(fx, 1, 1))
    fy = harmonic(centre, pltpu.roll(centre, ny - 1, 2))
    t_yp = jnp.where(yi == ny - 1, harmonic(centre[:, :, ny - 1 :], kyh), fy)
    t_ym = jnp.where(yi == 0, harmonic(centre[:, :, :1], kyl), pltpu.roll(fy, 1, 2))

    tzm_ref[...] = t_zm
    txm_ref[...] = t_xm
    tym_ref[...] = t_ym
    store_x_rows(txp_ref, t_xp[:, nx - 1 :, :])
    typ_ref[...] = to_rows(t_yp)[1]
    update(
        (t_zp, t_zm, t_xp, t_xm, t_yp, t_ym),
        pm_ref, pb_ref, pa_ref, qxl_ref, qxh_ref, qyl_ref, qyh_ref, f_ref,
        (o_ref, exl_ref, exh_ref, eyl_ref, eyh_ref),
    )


def later_step_kernel(
    tzm_ref, tza_ref, txm_ref, tym_ref, txp_ref, typ_ref,
    pm_ref, pb_ref, pa_ref, qxl_ref, qxh_ref, qyl_ref, qyh_ref, f_ref,
    o_ref, exl_ref, exh_ref, eyl_ref, eyh_ref,
):
    c = pl.program_id(0)
    last = pl.num_programs(0) - 1
    tz, nx, ny = pm_ref.shape
    xi = lax.broadcasted_iota(jnp.int32, (tz, nx, ny), 1)
    yi = lax.broadcasted_iota(jnp.int32, (tz, nx, ny), 2)
    t_zm = tzm_ref[...]
    t_zp = jnp.concatenate([t_zm[1:], jnp.where(c == last, 0.0, tza_ref[...])], axis=0)
    t_xm = txm_ref[...]
    t_xp = jnp.where(xi == nx - 1, x_rows(txp_ref), pltpu.roll(t_xm, nx - 1, 1))
    t_ym = tym_ref[...]
    t_yp = jnp.where(yi == ny - 1, to_columns(typ_ref[...]), pltpu.roll(t_ym, ny - 1, 2))
    update(
        (t_zp, t_zm, t_xp, t_xm, t_yp, t_ym),
        pm_ref, pb_ref, pa_ref, qxl_ref, qxh_ref, qyl_ref, qyh_ref, f_ref,
        (o_ref, exl_ref, exh_ref, eyl_ref, eyh_ref),
    )


def advance(stored, pressure, pressure_halos, flow, inside=None, log_perm=None, perm_halos=None):
    depth, nx, ny = pressure.shape
    tz = CHUNK_Z
    grid = (depth // tz,)
    main = pl.BlockSpec((tz, nx, ny), lambda c: (c, 0, 0))
    below = pl.BlockSpec((1, nx, ny), lambda c: (jnp.maximum(c * tz - 1, 0), 0, 0))
    above = pl.BlockSpec((1, nx, ny), lambda c: (jnp.minimum(c * tz + tz, depth - 1), 0, 0))
    row = pl.BlockSpec((tz, ny), lambda c: (c, 0))
    col = pl.BlockSpec((tz, nx), lambda c: (c, 0))
    side = [row, row, col, col]
    smem = pl.BlockSpec(memory_space=pltpu.SMEM)
    f32 = jnp.float32
    full = jax.ShapeDtypeStruct((depth, nx, ny), f32)
    rows = jax.ShapeDtypeStruct((depth, ny), f32)
    cols = jax.ShapeDtypeStruct((depth, nx), f32)
    out_shape = [full, rows, rows, cols, cols]
    out_specs = [main] + side
    pressure_args = [pressure, pressure, pressure, *pressure_halos, flow]
    pressure_specs = [main, below, above] + side + [main]
    params = pltpu.CompilerParams(dimension_semantics=("arbitrary",))
    if stored is None:
        outs = pl.pallas_call(
            first_step_kernel,
            out_shape=tuple(out_shape + [full, full, full, rows, cols]),
            grid=grid,
            in_specs=[smem, main, below, above] + side + pressure_specs,
            out_specs=out_specs + [main, main, main, row, col],
            compiler_params=params,
        )(inside, log_perm, log_perm, log_perm, *perm_halos, *pressure_args)
        return outs[0], outs[1:5], outs[5:]
    t_zm, t_xm, t_ym, t_xp, t_yp = stored
    outs = pl.pallas_call(
        later_step_kernel,
        out_shape=tuple(out_shape),
        grid=grid,
        in_specs=[main, above, main, main, row, col] + pressure_specs,
        out_specs=out_specs,
        compiler_params=params,
    )(t_zm, t_zm, t_xm, t_ym, t_xp, t_yp, *pressure_args)
    return outs[0], outs[1:5], stored


def depth_kernel(rz_ref, n_ref, o_ref):
    rz = rz_ref[...]
    for i in range(n_ref.shape[1]):
        o_ref[:, i, :] = jnp.dot(rz, n_ref[:, i, :], preferred_element_type=jnp.float32).astype(
            jnp.bfloat16
        )


def depth_transform(root_z, noise):
    depth, nx, ny = noise.shape
    bx = min(nx, DEPTH_X)
    block = pl.BlockSpec((depth, bx, ny), lambda i: (0, i, 0))
    return pl.pallas_call(
        depth_kernel,
        out_shape=jax.ShapeDtypeStruct(noise.shape, jnp.bfloat16),
        grid=(nx // bx,),
        in_specs=[pl.BlockSpec(root_z.shape, lambda i: (0, 0)), block],
        out_specs=block,
        compiler_params=pltpu.CompilerParams(dimension_semantics=("arbitrary",)),
    )(root_z, noise)


def line_kernel(g_ref, rx_ref, ry_ref, o_ref, *, count_w, count_n):
    f32 = jnp.float32
    nx = g_ref.shape[2]
    ny = g_ref.shape[3]
    rx = rx_ref[...]
    halves = []
    for n in range(count_n):
        lines = jnp.concatenate([g_ref[w * count_n + n, 0] for w in range(count_w)], axis=0)
        halves.append(jnp.dot(rx, lines, preferred_element_type=f32).astype(jnp.bfloat16))
    second = jnp.concatenate(halves, axis=1)
    third = lax.dot_general(
        second, ry_ref[...], (((1,), (1,)), ((), ())), preferred_element_type=f32
    ).astype(jnp.bfloat16)
    for w in range(count_w):
        for n in range(count_n):
            o_ref[w * count_n + n, 0] = third[w * nx : (w + 1) * nx, n * ny : (n + 1) * ny]


def line_transforms(gathered, root_x, root_y, count_w, count_n):
    groups, planes, nx, ny = gathered.shape
    block = pl.BlockSpec((groups, 1, nx, ny), lambda z: (0, z, 0, 0))
    whole_x = pl.BlockSpec(root_x.shape, lambda z: (0, 0))
    whole_y = pl.BlockSpec(root_y.shape, lambda z: (0, 0))
    return pl.pallas_call(
        functools.partial(line_kernel, count_w=count_w, count_n=count_n),
        out_shape=jax.ShapeDtypeStruct(gathered.shape, jnp.bfloat16),
        grid=(planes,),
        in_specs=[block, whole_x, whole_y],
        out_specs=block,
        compiler_params=pltpu.CompilerParams(dimension_semantics=("arbitrary",)),
    )(gathered, root_x, root_y)


def body(noise, root_z, root_x, root_y, pressure_start, well_x, well_y, well_z, well_rate):
    depth, rows_x, rows_y = noise.shape
    first = depth_transform(root_z, noise)
    count_w = lax.axis_size("wide")
    count_n = lax.axis_size("narrow")
    groups = count_w * count_n
    planes = depth // groups
    gathered = lax.all_to_all(
        first.reshape(groups, planes, rows_x, rows_y),
        ("wide", "narrow"), split_axis=0, concat_axis=0, tiled=True,
    )
    wide_at = lax.axis_index("wide")
    narrow_at = lax.axis_index("narrow")
    last_w = lax.axis_size("wide") - 1
    last_n = lax.axis_size("narrow") - 1

    local_x = well_x - wide_at * rows_x
    local_y = well_y - narrow_at * rows_y
    valid = (local_x >= 0) & (local_x < rows_x) & (local_y >= 0) & (local_y < rows_y)
    rates = jnp.where(valid, well_rate, 0.0).astype(jnp.float32)
    wells = well_x.shape[0]
    cells = well_z * rows_x + local_x
    pick_rows = jnp.where(
        lax.broadcasted_iota(jnp.int32, (depth * rows_x, wells), 0) == cells[None, :],
        rates[None, :],
        0.0,
    )
    pick_cols = (
        lax.broadcasted_iota(jnp.int32, (wells, rows_y), 1) == local_y[:, None]
    ).astype(jnp.float32)
    flow = jnp.dot(
        pick_rows, pick_cols, precision=lax.Precision.HIGHEST, preferred_element_type=jnp.float32
    ).reshape(depth, rows_x, rows_y)

    inside = jnp.stack(
        [wide_at > 0, wide_at < last_w, narrow_at > 0, narrow_at < last_n]
    ).astype(jnp.int32)
    edges = block_edges(pressure_start)
    gathered, flow, edges = lax.optimization_barrier((gathered, flow, edges))
    outgoing = line_transforms(gathered, root_x, root_y, count_w, count_n)
    log_perm = lax.all_to_all(
        outgoing, ("wide", "narrow"), split_axis=0, concat_axis=0, tiled=True,
    ).reshape(depth, rows_x, rows_y)

    *lp_edges, log_perm = block_edges(log_perm, keep=True)
    perm_halos = halos(lp_edges)
    pressure = pressure_start
    stored = None
    for step in range(STEPS):
        pressure, edges, stored = advance(
            stored, pressure, halos(edges), flow, inside, log_perm, perm_halos
        )
    return (log_perm, pressure)


def solution(mesh):
    in_specs = (
        P("member", "wide", "narrow"),
        P(),
        P(),
        P(),
        P("member", "wide", "narrow"),
        P("member"),
        P("member"),
        P("member"),
        P("member"),
    )
    out_specs = (P("member", "wide", "narrow"), P("member", "wide", "narrow"))
    return jax.shard_map(body, mesh=mesh, in_specs=in_specs, out_specs=out_specs, check_vma=False)
```

```python
import functools

import jax
import jax.numpy as jnp
from jax import lax
from jax.experimental import pallas as pl
from jax.experimental.pallas import tpu as pltpu
from jax.sharding import PartitionSpec as P

STEPS = 2


STEP_SIZE = 0.03
CAP_LOG = 1.5
CHUNK_Z = 16
EDGE_Z = 64
DEPTH_X = 8


def permeability(values):
    return jnp.exp(CAP_LOG * jnp.tanh(values / CAP_LOG))


def harmonic(a, b):
    return 2.0 * a * b / (a + b)


def halos(edges):
    forward_w = [(i, i + 1) for i in range(lax.axis_size("wide") - 1)]
    backward_w = [(j, i) for i, j in forward_w]
    forward_n = [(i, i + 1) for i in range(lax.axis_size("narrow") - 1)]
    backward_n = [(j, i) for i, j in forward_n]
    first_x, last_x, first_y, last_y = edges
    x_lo = lax.ppermute(last_x, "wide", forward_w)
    x_hi = lax.ppermute(first_x, "wide", backward_w)
    y_lo = lax.ppermute(last_y, "narrow", forward_n)
    y_hi = lax.ppermute(first_y, "narrow", backward_n)
    return x_lo, x_hi, y_lo, y_hi


def to_columns(rows):
    tz, nx = rows.shape
    eye = jnp.where(
        lax.broadcasted_iota(jnp.int32, (nx, nx), 0) == lax.broadcasted_iota(jnp.int32, (nx, nx), 1),
        1.0, 0.0,
    )
    cols = lax.dot_general(
        eye, rows, (((1,), (1,)), ((), ())),
        precision=lax.Precision.HIGHEST, preferred_element_type=jnp.float32,
    )
    return jnp.concatenate([cols[:, k : k + 1][None] for k in range(tz)], axis=0)


def x_rows(ref):
    return jnp.concatenate([ref[k : k + 1, :][None] for k in range(ref.shape[0])], axis=0)


def store_x_rows(ref, rows):
    for k in range(ref.shape[0]):
        ref[k : k + 1, :] = rows[k]


def to_rows(block):
    tz, nx, ny = block.shape
    lane = lax.broadcasted_iota(jnp.int32, (nx, 128), 1)
    pick = jnp.where(
        lax.broadcasted_iota(jnp.int32, (tz, 128), 0) == lax.broadcasted_iota(jnp.int32, (tz, 128), 1),
        1.0, 0.0,
    )
    result = []
    for column in (0, ny - 1):
        gathered = jnp.zeros((nx, 128), jnp.float32)
        for k in range(tz):
            gathered = jnp.where(lane == k, block[k, :, column : column + 1], gathered)
        result.append(
            lax.dot_general(
                pick, gathered, (((1,), (1,)), ((), ())),
                precision=lax.Precision.HIGHEST, preferred_element_type=jnp.float32,
            )
        )
    return result[0], result[1]


def edge_kernel(block_ref, xl_ref, xh_ref, yl_ref, yh_ref, *copy_ref):
    block = block_ref[...]
    if copy_ref:
        copy_ref[0][...] = block
    block = block.astype(jnp.float32)
    store_x_rows(xl_ref, block[:, :1, :])
    store_x_rows(xh_ref, block[:, -1:, :])
    yl_ref[...], yh_ref[...] = to_rows(block)


def block_edges(block, keep=False):
    depth, nx, ny = block.shape
    tz = EDGE_Z
    f32 = jnp.float32
    whole = pl.BlockSpec((tz, nx, ny), lambda c: (c, 0, 0))
    row = pl.BlockSpec((tz, ny), lambda c: (c, 0))
    col = pl.BlockSpec((tz, nx), lambda c: (c, 0))
    out_shape = [
        jax.ShapeDtypeStruct((depth, ny), f32),
        jax.ShapeDtypeStruct((depth, ny), f32),
        jax.ShapeDtypeStruct((depth, nx), f32),
        jax.ShapeDtypeStruct((depth, nx), f32),
    ]
    out_specs = [row, row, col, col]
    if keep:
        out_shape.append(jax.ShapeDtypeStruct(block.shape, block.dtype))
        out_specs.append(whole)
    return pl.pallas_call(
        edge_kernel,
        out_shape=tuple(out_shape),
        grid=(depth // tz,),
        in_specs=[whole],
        out_specs=out_specs,
        compiler_params=pltpu.CompilerParams(dimension_semantics=("arbitrary",)),
    )(block)


def update(trans, pm_ref, pb_ref, pa_ref, qxl_ref, qxh_ref, qyl_ref, qyh_ref, f_ref, outs):
    o_ref, exl_ref, exh_ref, eyl_ref, eyh_ref = outs
    t_zp, t_zm, t_xp, t_xm, t_yp, t_ym = trans
    tz, nx, ny = pm_ref.shape
    f32 = jnp.float32
    xi = lax.broadcasted_iota(jnp.int32, (tz, nx, ny), 1)
    yi = lax.broadcasted_iota(jnp.int32, (tz, nx, ny), 2)
    p = pm_ref[...].astype(f32)
    pext = jnp.concatenate([pb_ref[...].astype(f32), p, pa_ref[...].astype(f32)], axis=0)
    n_xp = jnp.where(xi == nx - 1, x_rows(qxh_ref), pltpu.roll(p, nx - 1, 1))
    n_xm = jnp.where(xi == 0, x_rows(qxl_ref), pltpu.roll(p, 1, 1))
    n_yp = jnp.where(yi == ny - 1, to_columns(qyh_ref[...]), pltpu.roll(p, ny - 1, 2))
    n_ym = jnp.where(yi == 0, to_columns(qyl_ref[...]), pltpu.roll(p, 1, 2))

    flux = t_zp * (pext[2:] - p)
    flux = flux + t_zm * (pext[:-2] - p)
    flux = flux + t_xp * (n_xp - p)
    flux = flux + t_xm * (n_xm - p)
    flux = flux + t_yp * (n_yp - p)
    flux = flux + t_ym * (n_ym - p)
    new = p + STEP_SIZE * (flux + f_ref[...]) / (1.0 + 0.5 * p * p)
    o_ref[...] = new
    store_x_rows(exl_ref, new[:, :1, :])
    store_x_rows(exh_ref, new[:, nx - 1 :, :])
    eyl_ref[...], eyh_ref[...] = to_rows(new)


def first_step_kernel(
    inside_ref, lpm_ref, lpb_ref, lpa_ref, lxl_ref, lxh_ref, lyl_ref, lyh_ref,
    pm_ref, pb_ref, pa_ref, qxl_ref, qxh_ref, qyl_ref, qyh_ref, f_ref,
    o_ref, exl_ref, exh_ref, eyl_ref, eyh_ref, tzm_ref, txm_ref, tym_ref, txp_ref, typ_ref,
):
    c = pl.program_id(0)
    last = pl.num_programs(0) - 1
    tz, nx, ny = pm_ref.shape
    f32 = jnp.float32

    def side_perm(ref, k):
        return jnp.where(inside_ref[k] > 0, permeability(ref[...].astype(f32)), 0.0)

    kxl = jnp.where(inside_ref[0] > 0, permeability(x_rows(lxl_ref)), 0.0)
    kxh = jnp.where(inside_ref[1] > 0, permeability(x_rows(lxh_ref)), 0.0)
    kyl = to_columns(side_perm(lyl_ref, 2))
    kyh = to_columns(side_perm(lyh_ref, 3))

    below = jnp.where(c == 0, 0.0, permeability(lpb_ref[...].astype(f32)))
    above = jnp.where(c == last, 0.0, permeability(lpa_ref[...].astype(f32)))
    centre = permeability(lpm_ref[...].astype(f32))
    ext = jnp.concatenate([below, centre, above], axis=0)
    faces = harmonic(ext[:-1], ext[1:])
    t_zm = faces[:-1]
    t_zp = faces[1:]

    xi = lax.broadcasted_iota(jnp.int32, (tz, nx, ny), 1)
    yi = lax.broadcasted_iota(jnp.int32, (tz, nx, ny), 2)

    fx = harmonic(centre, pltpu.roll(centre, nx - 1, 1))
    t_xp = jnp.where(xi == nx - 1, harmonic(centre[:, nx - 1 :, :], kxh), fx)
    t_xm = jnp.where(xi == 0, harmonic(centre[:, :1, :], kxl), pltpu.roll(fx, 1, 1))
    fy = harmonic(centre, pltpu.roll(centre, ny - 1, 2))
    t_yp = jnp.where(yi == ny - 1, harmonic(centre[:, :, ny - 1 :], kyh), fy)
    t_ym = jnp.where(yi == 0, harmonic(centre[:, :, :1], kyl), pltpu.roll(fy, 1, 2))

    tzm_ref[...] = t_zm
    txm_ref[...] = t_xm
    tym_ref[...] = t_ym
    store_x_rows(txp_ref, t_xp[:, nx - 1 :, :])
    typ_ref[...] = to_rows(t_yp)[1]
    update(
        (t_zp, t_zm, t_xp, t_xm, t_yp, t_ym),
        pm_ref, pb_ref, pa_ref, qxl_ref, qxh_ref, qyl_ref, qyh_ref, f_ref,
        (o_ref, exl_ref, exh_ref, eyl_ref, eyh_ref),
    )


def later_step_kernel(
    tzm_ref, tza_ref, txm_ref, tym_ref, txp_ref, typ_ref,
    pm_ref, pb_ref, pa_ref, qxl_ref, qxh_ref, qyl_ref, qyh_ref, f_ref,
    o_ref, exl_ref, exh_ref, eyl_ref, eyh_ref,
):
    c = pl.program_id(0)
    last = pl.num_programs(0) - 1
    tz, nx, ny = pm_ref.shape
    xi = lax.broadcasted_iota(jnp.int32, (tz, nx, ny), 1)
    yi = lax.broadcasted_iota(jnp.int32, (tz, nx, ny), 2)
    t_zm = tzm_ref[...]
    t_zp = jnp.concatenate([t_zm[1:], jnp.where(c == last, 0.0, tza_ref[...])], axis=0)
    t_xm = txm_ref[...]
    t_xp = jnp.where(xi == nx - 1, x_rows(txp_ref), pltpu.roll(t_xm, nx - 1, 1))
    t_ym = tym_ref[...]
    t_yp = jnp.where(yi == ny - 1, to_columns(typ_ref[...]), pltpu.roll(t_ym, ny - 1, 2))
    update(
        (t_zp, t_zm, t_xp, t_xm, t_yp, t_ym),
        pm_ref, pb_ref, pa_ref, qxl_ref, qxh_ref, qyl_ref, qyh_ref, f_ref,
        (o_ref, exl_ref, exh_ref, eyl_ref, eyh_ref),
    )


def advance(stored, pressure, pressure_halos, flow, inside=None, log_perm=None, perm_halos=None):
    depth, nx, ny = pressure.shape
    tz = CHUNK_Z
    grid = (depth // tz,)
    main = pl.BlockSpec((tz, nx, ny), lambda c: (c, 0, 0))
    below = pl.BlockSpec((1, nx, ny), lambda c: (jnp.maximum(c * tz - 1, 0), 0, 0))
    above = pl.BlockSpec((1, nx, ny), lambda c: (jnp.minimum(c * tz + tz, depth - 1), 0, 0))
    row = pl.BlockSpec((tz, ny), lambda c: (c, 0))
    col = pl.BlockSpec((tz, nx), lambda c: (c, 0))
    side = [row, row, col, col]
    smem = pl.BlockSpec(memory_space=pltpu.SMEM)
    f32 = jnp.float32
    full = jax.ShapeDtypeStruct((depth, nx, ny), f32)
    rows = jax.ShapeDtypeStruct((depth, ny), f32)
    cols = jax.ShapeDtypeStruct((depth, nx), f32)
    out_shape = [full, rows, rows, cols, cols]
    out_specs = [main] + side
    pressure_args = [pressure, pressure, pressure, *pressure_halos, flow]
    pressure_specs = [main, below, above] + side + [main]
    params = pltpu.CompilerParams(dimension_semantics=("arbitrary",))
    if stored is None:
        outs = pl.pallas_call(
            first_step_kernel,
            out_shape=tuple(out_shape + [full, full, full, rows, cols]),
            grid=grid,
            in_specs=[smem, main, below, above] + side + pressure_specs,
            out_specs=out_specs + [main, main, main, row, col],
            compiler_params=params,
        )(inside, log_perm, log_perm, log_perm, *perm_halos, *pressure_args)
        return outs[0], outs[1:5], outs[5:]
    t_zm, t_xm, t_ym, t_xp, t_yp = stored
    outs = pl.pallas_call(
        later_step_kernel,
        out_shape=tuple(out_shape),
        grid=grid,
        in_specs=[main, above, main, main, row, col] + pressure_specs,
        out_specs=out_specs,
        compiler_params=params,
    )(t_zm, t_zm, t_xm, t_ym, t_xp, t_yp, *pressure_args)
    return outs[0], outs[1:5], stored


def depth_kernel(rz_ref, n_ref, o_ref):
    rz = rz_ref[...]
    for i in range(n_ref.shape[1]):
        o_ref[:, i, :] = jnp.dot(rz, n_ref[:, i, :], preferred_element_type=jnp.float32).astype(
            jnp.bfloat16
        )


def depth_transform(root_z, noise):
    depth, nx, ny = noise.shape
    bx = min(nx, DEPTH_X)
    block = pl.BlockSpec((depth, bx, ny), lambda i: (0, i, 0))
    return pl.pallas_call(
        depth_kernel,
        out_shape=jax.ShapeDtypeStruct(noise.shape, jnp.bfloat16),
        grid=(nx // bx,),
        in_specs=[pl.BlockSpec(root_z.shape, lambda i: (0, 0)), block],
        out_specs=block,
        compiler_params=pltpu.CompilerParams(dimension_semantics=("arbitrary",)),
    )(root_z, noise)


def line_kernel(g_ref, rx_ref, ry_ref, o_ref, *, count_w, count_n):
    f32 = jnp.float32
    nx = g_ref.shape[2]
    ny = g_ref.shape[3]
    rx = rx_ref[...]
    halves = []
    for n in range(count_n):
        lines = jnp.concatenate([g_ref[w * count_n + n, 0] for w in range(count_w)], axis=0)
        halves.append(jnp.dot(rx, lines, preferred_element_type=f32).astype(jnp.bfloat16))
    second = jnp.concatenate(halves, axis=1)
    third = lax.dot_general(
        second, ry_ref[...], (((1,), (1,)), ((), ())), preferred_element_type=f32
    ).astype(jnp.bfloat16)
    for w in range(count_w):
        for n in range(count_n):
            o_ref[w * count_n + n, 0] = third[w * nx : (w + 1) * nx, n * ny : (n + 1) * ny]


def line_transforms(gathered, root_x, root_y, count_w, count_n):
    groups, planes, nx, ny = gathered.shape
    block = pl.BlockSpec((groups, 1, nx, ny), lambda z: (0, z, 0, 0))
    whole_x = pl.BlockSpec(root_x.shape, lambda z: (0, 0))
    whole_y = pl.BlockSpec(root_y.shape, lambda z: (0, 0))
    return pl.pallas_call(
        functools.partial(line_kernel, count_w=count_w, count_n=count_n),
        out_shape=jax.ShapeDtypeStruct(gathered.shape, jnp.bfloat16),
        grid=(planes,),
        in_specs=[block, whole_x, whole_y],
        out_specs=block,
        compiler_params=pltpu.CompilerParams(dimension_semantics=("arbitrary",)),
    )(gathered, root_x, root_y)


def body(noise, root_z, root_x, root_y, pressure_start, well_x, well_y, well_z, well_rate):
    depth, rows_x, rows_y = noise.shape
    first = depth_transform(root_z, noise)
    count_w = lax.axis_size("wide")
    count_n = lax.axis_size("narrow")
    groups = count_w * count_n
    planes = depth // groups
    gathered = lax.all_to_all(
        first.reshape(groups, planes, rows_x, rows_y),
        ("wide", "narrow"), split_axis=0, concat_axis=0, tiled=True,
    )
    wide_at = lax.axis_index("wide")
    narrow_at = lax.axis_index("narrow")
    last_w = lax.axis_size("wide") - 1
    last_n = lax.axis_size("narrow") - 1

    local_x = well_x - wide_at * rows_x
    local_y = well_y - narrow_at * rows_y
    valid = (local_x >= 0) & (local_x < rows_x) & (local_y >= 0) & (local_y < rows_y)
    rates = jnp.where(valid, well_rate, 0.0).astype(jnp.float32)
    wells = well_x.shape[0]
    cells = well_z * rows_x + local_x
    pick_rows = jnp.where(
        lax.broadcasted_iota(jnp.int32, (depth * rows_x, wells), 0) == cells[None, :],
        rates[None, :],
        0.0,
    )
    pick_cols = (
        lax.broadcasted_iota(jnp.int32, (wells, rows_y), 1) == local_y[:, None]
    ).astype(jnp.float32)
    flow = jnp.dot(
        pick_rows, pick_cols, precision=lax.Precision.HIGHEST, preferred_element_type=jnp.float32
    ).reshape(depth, rows_x, rows_y)

    inside = jnp.stack(
        [wide_at > 0, wide_at < last_w, narrow_at > 0, narrow_at < last_n]
    ).astype(jnp.int32)
    edges = block_edges(pressure_start)
    gathered, flow, edges = lax.optimization_barrier((gathered, flow, edges))
    outgoing = line_transforms(gathered, root_x, root_y, count_w, count_n)
    log_perm = lax.all_to_all(
        outgoing, ("wide", "narrow"), split_axis=0, concat_axis=0, tiled=True,
    ).reshape(depth, rows_x, rows_y)

    *lp_edges, log_perm = block_edges(log_perm, keep=True)
    perm_halos = halos(lp_edges)
    pressure = pressure_start
    stored = None
    for step in range(STEPS):
        pressure, edges, stored = advance(
            stored, pressure, halos(edges), flow, inside, log_perm, perm_halos
        )
    return (log_perm, pressure)


def solution(mesh):
    in_specs = (
        P("member", "wide", "narrow"),
        P(),
        P(),
        P(),
        P("member", "wide", "narrow"),
        P("member"),
        P("member"),
        P("member"),
        P("member"),
    )
    out_specs = (P("member", "wide", "narrow"), P("member", "wide", "narrow"))
    return jax.shard_map(body, mesh=mesh, in_specs=in_specs, out_specs=out_specs, check_vma=False)
```

```python
import functools

import jax
import jax.numpy as jnp
from jax import lax
from jax.experimental import pallas as pl
from jax.experimental.pallas import tpu as pltpu
from jax.sharding import PartitionSpec as P

STEPS = 2


STEP_SIZE = 0.03
CAP_LOG = 1.5
CHUNK_Z = 16
EDGE_Z = 64
DEPTH_X = 16


def permeability(values):
    return jnp.exp(CAP_LOG * jnp.tanh(values / CAP_LOG))


def harmonic(a, b):
    return 2.0 * a * b / (a + b)


def halos(edges):
    forward_w = [(i, i + 1) for i in range(lax.axis_size("wide") - 1)]
    backward_w = [(j, i) for i, j in forward_w]
    forward_n = [(i, i + 1) for i in range(lax.axis_size("narrow") - 1)]
    backward_n = [(j, i) for i, j in forward_n]
    first_x, last_x, first_y, last_y = edges
    x_lo = lax.ppermute(last_x, "wide", forward_w)
    x_hi = lax.ppermute(first_x, "wide", backward_w)
    y_lo = lax.ppermute(last_y, "narrow", forward_n)
    y_hi = lax.ppermute(first_y, "narrow", backward_n)
    return x_lo, x_hi, y_lo, y_hi


def to_columns(rows):
    tz, nx = rows.shape
    eye = jnp.where(
        lax.broadcasted_iota(jnp.int32, (nx, nx), 0) == lax.broadcasted_iota(jnp.int32, (nx, nx), 1),
        1.0, 0.0,
    )
    cols = lax.dot_general(
        eye, rows, (((1,), (1,)), ((), ())),
        precision=lax.Precision.HIGHEST, preferred_element_type=jnp.float32,
    )
    return jnp.concatenate([cols[:, k : k + 1][None] for k in range(tz)], axis=0)


def x_rows(ref):
    return jnp.concatenate([ref[k : k + 1, :][None] for k in range(ref.shape[0])], axis=0)


def store_x_rows(ref, rows):
    for k in range(ref.shape[0]):
        ref[k : k + 1, :] = rows[k]


def to_rows(block):
    tz, nx, ny = block.shape
    lane = lax.broadcasted_iota(jnp.int32, (nx, 128), 1)
    pick = jnp.where(
        lax.broadcasted_iota(jnp.int32, (tz, 128), 0) == lax.broadcasted_iota(jnp.int32, (tz, 128), 1),
        1.0, 0.0,
    )
    result = []
    for column in (0, ny - 1):
        gathered = jnp.zeros((nx, 128), jnp.float32)
        for k in range(tz):
            gathered = jnp.where(lane == k, block[k, :, column : column + 1], gathered)
        result.append(
            lax.dot_general(
                pick, gathered, (((1,), (1,)), ((), ())),
                precision=lax.Precision.HIGHEST, preferred_element_type=jnp.float32,
            )
        )
    return result[0], result[1]


def edge_kernel(block_ref, xl_ref, xh_ref, yl_ref, yh_ref, *copy_ref):
    block = block_ref[...]
    if copy_ref:
        copy_ref[0][...] = block
    block = block.astype(jnp.float32)
    store_x_rows(xl_ref, block[:, :1, :])
    store_x_rows(xh_ref, block[:, -1:, :])
    yl_ref[...], yh_ref[...] = to_rows(block)


def block_edges(block, keep=False):
    depth, nx, ny = block.shape
    tz = EDGE_Z
    f32 = jnp.float32
    whole = pl.BlockSpec((tz, nx, ny), lambda c: (c, 0, 0))
    row = pl.BlockSpec((tz, ny), lambda c: (c, 0))
    col = pl.BlockSpec((tz, nx), lambda c: (c, 0))
    out_shape = [
        jax.ShapeDtypeStruct((depth, ny), f32),
        jax.ShapeDtypeStruct((depth, ny), f32),
        jax.ShapeDtypeStruct((depth, nx), f32),
        jax.ShapeDtypeStruct((depth, nx), f32),
    ]
    out_specs = [row, row, col, col]
    if keep:
        out_shape.append(jax.ShapeDtypeStruct(block.shape, block.dtype))
        out_specs.append(whole)
    return pl.pallas_call(
        edge_kernel,
        out_shape=tuple(out_shape),
        grid=(depth // tz,),
        in_specs=[whole],
        out_specs=out_specs,
        compiler_params=pltpu.CompilerParams(dimension_semantics=("arbitrary",)),
    )(block)


def update(trans, pm_ref, pb_ref, pa_ref, qxl_ref, qxh_ref, qyl_ref, qyh_ref, f_ref, outs):
    o_ref, exl_ref, exh_ref, eyl_ref, eyh_ref = outs
    t_zp, t_zm, t_xp, t_xm, t_yp, t_ym = trans
    tz, nx, ny = pm_ref.shape
    f32 = jnp.float32
    xi = lax.broadcasted_iota(jnp.int32, (tz, nx, ny), 1)
    yi = lax.broadcasted_iota(jnp.int32, (tz, nx, ny), 2)
    p = pm_ref[...].astype(f32)
    pext = jnp.concatenate([pb_ref[...].astype(f32), p, pa_ref[...].astype(f32)], axis=0)
    n_xp = jnp.where(xi == nx - 1, x_rows(qxh_ref), pltpu.roll(p, nx - 1, 1))
    n_xm = jnp.where(xi == 0, x_rows(qxl_ref), pltpu.roll(p, 1, 1))
    n_yp = jnp.where(yi == ny - 1, to_columns(qyh_ref[...]), pltpu.roll(p, ny - 1, 2))
    n_ym = jnp.where(yi == 0, to_columns(qyl_ref[...]), pltpu.roll(p, 1, 2))

    flux = t_zp * (pext[2:] - p)
    flux = flux + t_zm * (pext[:-2] - p)
    flux = flux + t_xp * (n_xp - p)
    flux = flux + t_xm * (n_xm - p)
    flux = flux + t_yp * (n_yp - p)
    flux = flux + t_ym * (n_ym - p)
    new = p + STEP_SIZE * (flux + f_ref[...]) / (1.0 + 0.5 * p * p)
    o_ref[...] = new
    store_x_rows(exl_ref, new[:, :1, :])
    store_x_rows(exh_ref, new[:, nx - 1 :, :])
    eyl_ref[...], eyh_ref[...] = to_rows(new)


def first_step_kernel(
    inside_ref, lpm_ref, lpb_ref, lpa_ref, lxl_ref, lxh_ref, lyl_ref, lyh_ref,
    pm_ref, pb_ref, pa_ref, qxl_ref, qxh_ref, qyl_ref, qyh_ref, f_ref,
    o_ref, exl_ref, exh_ref, eyl_ref, eyh_ref, tzm_ref, txm_ref, tym_ref, txp_ref, typ_ref,
):
    c = pl.program_id(0)
    last = pl.num_programs(0) - 1
    tz, nx, ny = pm_ref.shape
    f32 = jnp.float32

    def side_perm(ref, k):
        return jnp.where(inside_ref[k] > 0, permeability(ref[...].astype(f32)), 0.0)

    kxl = jnp.where(inside_ref[0] > 0, permeability(x_rows(lxl_ref)), 0.0)
    kxh = jnp.where(inside_ref[1] > 0, permeability(x_rows(lxh_ref)), 0.0)
    kyl = to_columns(side_perm(lyl_ref, 2))
    kyh = to_columns(side_perm(lyh_ref, 3))

    below = jnp.where(c == 0, 0.0, permeability(lpb_ref[...].astype(f32)))
    above = jnp.where(c == last, 0.0, permeability(lpa_ref[...].astype(f32)))
    centre = permeability(lpm_ref[...].astype(f32))
    ext = jnp.concatenate([below, centre, above], axis=0)
    faces = harmonic(ext[:-1], ext[1:])
    t_zm = faces[:-1]
    t_zp = faces[1:]

    xi = lax.broadcasted_iota(jnp.int32, (tz, nx, ny), 1)
    yi = lax.broadcasted_iota(jnp.int32, (tz, nx, ny), 2)

    fx = harmonic(centre, pltpu.roll(centre, nx - 1, 1))
    t_xp = jnp.where(xi == nx - 1, harmonic(centre[:, nx - 1 :, :], kxh), fx)
    t_xm = jnp.where(xi == 0, harmonic(centre[:, :1, :], kxl), pltpu.roll(fx, 1, 1))
    fy = harmonic(centre, pltpu.roll(centre, ny - 1, 2))
    t_yp = jnp.where(yi == ny - 1, harmonic(centre[:, :, ny - 1 :], kyh), fy)
    t_ym = jnp.where(yi == 0, harmonic(centre[:, :, :1], kyl), pltpu.roll(fy, 1, 2))

    tzm_ref[...] = t_zm
    txm_ref[...] = t_xm
    tym_ref[...] = t_ym
    store_x_rows(txp_ref, t_xp[:, nx - 1 :, :])
    typ_ref[...] = to_rows(t_yp)[1]
    update(
        (t_zp, t_zm, t_xp, t_xm, t_yp, t_ym),
        pm_ref, pb_ref, pa_ref, qxl_ref, qxh_ref, qyl_ref, qyh_ref, f_ref,
        (o_ref, exl_ref, exh_ref, eyl_ref, eyh_ref),
    )


def trans_kernel(lpm_ref, lpb_ref, lpa_ref, tzm_ref, txm_ref, tym_ref, cx0_ref, cxl_ref, cy0_ref, cyl_ref):
    c = pl.program_id(0)
    last = pl.num_programs(0) - 1
    tz, nx, ny = lpm_ref.shape
    f32 = jnp.float32
    below = jnp.where(c == 0, 0.0, permeability(lpb_ref[...].astype(f32)))
    above = jnp.where(c == last, 0.0, permeability(lpa_ref[...].astype(f32)))
    centre = permeability(lpm_ref[...].astype(f32))
    ext = jnp.concatenate([below, centre, above], axis=0)
    tzm_ref[...] = harmonic(ext[:-2], ext[1:-1])
    txm_ref[...] = pltpu.roll(harmonic(centre, pltpu.roll(centre, nx - 1, 1)), 1, 1)
    tym_ref[...] = pltpu.roll(harmonic(centre, pltpu.roll(centre, ny - 1, 2)), 1, 2)
    store_x_rows(cx0_ref, centre[:, :1, :])
    store_x_rows(cxl_ref, centre[:, nx - 1 :, :])
    cy0_ref[...], cyl_ref[...] = to_rows(centre)


def face_transmissibilities(log_perm):
    depth, nx, ny = log_perm.shape
    tz = CHUNK_Z
    f32 = jnp.float32
    main = pl.BlockSpec((tz, nx, ny), lambda c: (c, 0, 0))
    below = pl.BlockSpec((1, nx, ny), lambda c: (jnp.maximum(c * tz - 1, 0), 0, 0))
    above = pl.BlockSpec((1, nx, ny), lambda c: (jnp.minimum(c * tz + tz, depth - 1), 0, 0))
    row = pl.BlockSpec((tz, ny), lambda c: (c, 0))
    col = pl.BlockSpec((tz, nx), lambda c: (c, 0))
    full = jax.ShapeDtypeStruct((depth, nx, ny), f32)
    rows = jax.ShapeDtypeStruct((depth, ny), f32)
    cols = jax.ShapeDtypeStruct((depth, nx), f32)
    return pl.pallas_call(
        trans_kernel,
        out_shape=(full, full, full, rows, rows, cols, cols),
        grid=(depth // tz,),
        in_specs=[main, below, above],
        out_specs=[main, main, main, row, row, col, col],
        compiler_params=pltpu.CompilerParams(dimension_semantics=("arbitrary",)),
    )(log_perm, log_perm, log_perm)


def later_step_kernel(
    tzm_ref, tza_ref, txm_ref, tym_ref, txp_ref, typ_ref, bxm_ref, bym_ref,
    pm_ref, pb_ref, pa_ref, qxl_ref, qxh_ref, qyl_ref, qyh_ref, f_ref,
    o_ref, exl_ref, exh_ref, eyl_ref, eyh_ref,
):
    c = pl.program_id(0)
    last = pl.num_programs(0) - 1
    tz, nx, ny = pm_ref.shape
    xi = lax.broadcasted_iota(jnp.int32, (tz, nx, ny), 1)
    yi = lax.broadcasted_iota(jnp.int32, (tz, nx, ny), 2)
    t_zm = tzm_ref[...]
    t_zp = jnp.concatenate([t_zm[1:], jnp.where(c == last, 0.0, tza_ref[...])], axis=0)
    raw_xm = txm_ref[...]
    t_xp = jnp.where(xi == nx - 1, x_rows(txp_ref), pltpu.roll(raw_xm, nx - 1, 1))
    t_xm = jnp.where(xi == 0, x_rows(bxm_ref), raw_xm)
    raw_ym = tym_ref[...]
    t_yp = jnp.where(yi == ny - 1, to_columns(typ_ref[...]), pltpu.roll(raw_ym, ny - 1, 2))
    t_ym = jnp.where(yi == 0, to_columns(bym_ref[...]), raw_ym)
    update(
        (t_zp, t_zm, t_xp, t_xm, t_yp, t_ym),
        pm_ref, pb_ref, pa_ref, qxl_ref, qxh_ref, qyl_ref, qyh_ref, f_ref,
        (o_ref, exl_ref, exh_ref, eyl_ref, eyh_ref),
    )


def advance(stored, pressure, pressure_halos, flow, inside=None, log_perm=None, perm_halos=None):
    depth, nx, ny = pressure.shape
    tz = CHUNK_Z
    grid = (depth // tz,)
    main = pl.BlockSpec((tz, nx, ny), lambda c: (c, 0, 0))
    below = pl.BlockSpec((1, nx, ny), lambda c: (jnp.maximum(c * tz - 1, 0), 0, 0))
    above = pl.BlockSpec((1, nx, ny), lambda c: (jnp.minimum(c * tz + tz, depth - 1), 0, 0))
    row = pl.BlockSpec((tz, ny), lambda c: (c, 0))
    col = pl.BlockSpec((tz, nx), lambda c: (c, 0))
    side = [row, row, col, col]
    smem = pl.BlockSpec(memory_space=pltpu.SMEM)
    f32 = jnp.float32
    full = jax.ShapeDtypeStruct((depth, nx, ny), f32)
    rows = jax.ShapeDtypeStruct((depth, ny), f32)
    cols = jax.ShapeDtypeStruct((depth, nx), f32)
    out_shape = [full, rows, rows, cols, cols]
    out_specs = [main] + side
    pressure_args = [pressure, pressure, pressure, *pressure_halos, flow]
    pressure_specs = [main, below, above] + side + [main]
    params = pltpu.CompilerParams(dimension_semantics=("arbitrary",))
    if stored is None:
        outs = pl.pallas_call(
            first_step_kernel,
            out_shape=tuple(out_shape + [full, full, full, rows, cols]),
            grid=grid,
            in_specs=[smem, main, below, above] + side + pressure_specs,
            out_specs=out_specs + [main, main, main, row, col],
            compiler_params=params,
        )(inside, log_perm, log_perm, log_perm, *perm_halos, *pressure_args)
        return outs[0], outs[1:5], outs[5:]
    t_zm, t_xm, t_ym, t_xp, t_yp, b_xm, b_ym = stored
    outs = pl.pallas_call(
        later_step_kernel,
        out_shape=tuple(out_shape),
        grid=grid,
        in_specs=[main, above, main, main, row, col, row, col] + pressure_specs,
        out_specs=out_specs,
        compiler_params=params,
    )(t_zm, t_zm, t_xm, t_ym, t_xp, t_yp, b_xm, b_ym, *pressure_args)
    return outs[0], outs[1:5], stored


def depth_kernel(rz_ref, n_ref, o_ref):
    rz = rz_ref[...]
    for i in range(n_ref.shape[1]):
        o_ref[:, i, :] = jnp.dot(rz, n_ref[:, i, :], preferred_element_type=jnp.float32).astype(
            jnp.bfloat16
        )


def depth_transform(root_z, noise):
    depth, nx, ny = noise.shape
    bx = min(nx, DEPTH_X)
    block = pl.BlockSpec((depth, bx, ny), lambda i: (0, i, 0))
    return pl.pallas_call(
        depth_kernel,
        out_shape=jax.ShapeDtypeStruct(noise.shape, jnp.bfloat16),
        grid=(nx // bx,),
        in_specs=[pl.BlockSpec(root_z.shape, lambda i: (0, 0)), block],
        out_specs=block,
        compiler_params=pltpu.CompilerParams(dimension_semantics=("arbitrary",)),
    )(root_z, noise)


def line_kernel(g_ref, rx_ref, ry_ref, o_ref, *, count_w, count_n):
    f32 = jnp.float32
    nx = g_ref.shape[2]
    ny = g_ref.shape[3]
    rx = rx_ref[...]
    halves = []
    for n in range(count_n):
        lines = jnp.concatenate([g_ref[w * count_n + n, 0] for w in range(count_w)], axis=0)
        halves.append(jnp.dot(rx, lines, preferred_element_type=f32).astype(jnp.bfloat16))
    second = jnp.concatenate(halves, axis=1)
    third = lax.dot_general(
        second, ry_ref[...], (((1,), (1,)), ((), ())), preferred_element_type=f32
    ).astype(jnp.bfloat16)
    for w in range(count_w):
        for n in range(count_n):
            o_ref[w * count_n + n, 0] = third[w * nx : (w + 1) * nx, n * ny : (n + 1) * ny]


def line_transforms(gathered, root_x, root_y, count_w, count_n):
    groups, planes, nx, ny = gathered.shape
    block = pl.BlockSpec((groups, 1, nx, ny), lambda z: (0, z, 0, 0))
    whole_x = pl.BlockSpec(root_x.shape, lambda z: (0, 0))
    whole_y = pl.BlockSpec(root_y.shape, lambda z: (0, 0))
    return pl.pallas_call(
        functools.partial(line_kernel, count_w=count_w, count_n=count_n),
        out_shape=jax.ShapeDtypeStruct(gathered.shape, jnp.bfloat16),
        grid=(planes,),
        in_specs=[block, whole_x, whole_y],
        out_specs=block,
        compiler_params=pltpu.CompilerParams(dimension_semantics=("arbitrary",)),
    )(gathered, root_x, root_y)


def body(noise, root_z, root_x, root_y, pressure_start, well_x, well_y, well_z, well_rate):
    depth, rows_x, rows_y = noise.shape
    first = depth_transform(root_z, noise)
    count_w = lax.axis_size("wide")
    count_n = lax.axis_size("narrow")
    groups = count_w * count_n
    planes = depth // groups
    gathered = lax.all_to_all(
        first.reshape(groups, planes, rows_x, rows_y),
        ("wide", "narrow"), split_axis=0, concat_axis=0, tiled=True,
    )
    wide_at = lax.axis_index("wide")
    narrow_at = lax.axis_index("narrow")
    last_w = lax.axis_size("wide") - 1
    last_n = lax.axis_size("narrow") - 1

    local_x = well_x - wide_at * rows_x
    local_y = well_y - narrow_at * rows_y
    valid = (local_x >= 0) & (local_x < rows_x) & (local_y >= 0) & (local_y < rows_y)
    rates = jnp.where(valid, well_rate, 0.0).astype(jnp.float32)
    wells = well_x.shape[0]
    cells = well_z * rows_x + local_x
    pick_rows = jnp.where(
        lax.broadcasted_iota(jnp.int32, (depth * rows_x, wells), 0) == cells[None, :],
        rates[None, :],
        0.0,
    )
    pick_cols = (
        lax.broadcasted_iota(jnp.int32, (wells, rows_y), 1) == local_y[:, None]
    ).astype(jnp.float32)
    flow = jnp.dot(
        pick_rows, pick_cols, precision=lax.Precision.HIGHEST, preferred_element_type=jnp.float32
    ).reshape(depth, rows_x, rows_y)

    inside = jnp.stack(
        [wide_at > 0, wide_at < last_w, narrow_at > 0, narrow_at < last_n]
    ).astype(jnp.int32)
    edges = block_edges(pressure_start)
    gathered, flow, edges = lax.optimization_barrier((gathered, flow, edges))
    outgoing = line_transforms(gathered, root_x, root_y, count_w, count_n)
    log_perm = lax.all_to_all(
        outgoing, ("wide", "narrow"), split_axis=0, concat_axis=0, tiled=True,
    ).reshape(depth, rows_x, rows_y)

    *lp_edges, log_perm = block_edges(log_perm, keep=True)
    perm_halos = halos(lp_edges)
    pressure = pressure_start
    t_zm, t_xm, t_ym, c_x0, c_xl, c_y0, c_yl = face_transmissibilities(log_perm)
    k_xl, k_xh, k_yl, k_yh = perm_halos
    f32 = jnp.float32
    k_xl = jnp.where(wide_at > 0, permeability(k_xl), 0.0)
    k_xh = jnp.where(wide_at < last_w, permeability(k_xh), 0.0)
    k_yl = jnp.where(narrow_at > 0, permeability(k_yl), 0.0)
    k_yh = jnp.where(narrow_at < last_n, permeability(k_yh), 0.0)
    stored = (
        t_zm, t_xm, t_ym,
        harmonic(c_xl, k_xh), harmonic(c_yl, k_yh), harmonic(c_x0, k_xl), harmonic(c_y0, k_yl),
    )
    for step in range(STEPS):
        pressure, edges, stored = advance(
            stored, pressure, halos(edges), flow, inside, log_perm, perm_halos
        )
    return (log_perm, pressure)


def solution(mesh):
    in_specs = (
        P("member", "wide", "narrow"),
        P(),
        P(),
        P(),
        P("member", "wide", "narrow"),
        P("member"),
        P("member"),
        P("member"),
        P("member"),
    )
    out_specs = (P("member", "wide", "narrow"), P("member", "wide", "narrow"))
    return jax.shard_map(body, mesh=mesh, in_specs=in_specs, out_specs=out_specs, check_vma=False)
```

```python
import functools

import jax
import jax.numpy as jnp
from jax import lax
from jax.experimental import pallas as pl
from jax.experimental.pallas import tpu as pltpu
from jax.sharding import PartitionSpec as P

STEPS = 2


STEP_SIZE = 0.03
CAP_LOG = 1.5
CHUNK_Z = 16
EDGE_Z = 64
DEPTH_X = 16


def permeability(values):
    return jnp.exp(CAP_LOG * jnp.tanh(values / CAP_LOG))


def harmonic(a, b):
    return 2.0 * a * b / (a + b)


def halos(edges):
    forward_w = [(i, i + 1) for i in range(lax.axis_size("wide") - 1)]
    backward_w = [(j, i) for i, j in forward_w]
    forward_n = [(i, i + 1) for i in range(lax.axis_size("narrow") - 1)]
    backward_n = [(j, i) for i, j in forward_n]
    first_x, last_x, first_y, last_y = edges
    x_lo = lax.ppermute(last_x, "wide", forward_w)
    x_hi = lax.ppermute(first_x, "wide", backward_w)
    y_lo = lax.ppermute(last_y, "narrow", forward_n)
    y_hi = lax.ppermute(first_y, "narrow", backward_n)
    return x_lo, x_hi, y_lo, y_hi


def to_columns(rows):
    tz, nx = rows.shape
    eye = jnp.where(
        lax.broadcasted_iota(jnp.int32, (nx, nx), 0) == lax.broadcasted_iota(jnp.int32, (nx, nx), 1),
        1.0, 0.0,
    )
    cols = lax.dot_general(
        eye, rows, (((1,), (1,)), ((), ())),
        precision=lax.Precision.HIGHEST, preferred_element_type=jnp.float32,
    )
    return jnp.concatenate([cols[:, k : k + 1][None] for k in range(tz)], axis=0)


def x_rows(ref):
    return jnp.concatenate([ref[k : k + 1, :][None] for k in range(ref.shape[0])], axis=0)


def store_x_rows(ref, rows):
    for k in range(ref.shape[0]):
        ref[k : k + 1, :] = rows[k]


def to_rows(block, last_only=False):
    tz, nx, ny = block.shape
    lane = lax.broadcasted_iota(jnp.int32, (nx, 128), 1)
    pick = jnp.where(
        lax.broadcasted_iota(jnp.int32, (tz, 128), 0) == lax.broadcasted_iota(jnp.int32, (tz, 128), 1),
        1.0, 0.0,
    )
    result = []
    for column in ((ny - 1,) if last_only else (0, ny - 1)):
        gathered = jnp.zeros((nx, 128), jnp.float32)
        for k in range(tz):
            gathered = jnp.where(lane == k, block[k, :, column : column + 1], gathered)
        result.append(
            lax.dot_general(
                pick, gathered, (((1,), (1,)), ((), ())),
                precision=lax.Precision.HIGHEST, preferred_element_type=jnp.float32,
            )
        )
    return tuple(result)


def edge_kernel(block_ref, xl_ref, xh_ref, yl_ref, yh_ref, *copy_ref):
    block = block_ref[...]
    if copy_ref:
        copy_ref[0][...] = block
    block = block.astype(jnp.float32)
    store_x_rows(xl_ref, block[:, :1, :])
    store_x_rows(xh_ref, block[:, -1:, :])
    yl_ref[...], yh_ref[...] = to_rows(block)


def block_edges(block, keep=False):
    depth, nx, ny = block.shape
    tz = EDGE_Z
    f32 = jnp.float32
    whole = pl.BlockSpec((tz, nx, ny), lambda c: (c, 0, 0))
    row = pl.BlockSpec((tz, ny), lambda c: (c, 0))
    col = pl.BlockSpec((tz, nx), lambda c: (c, 0))
    out_shape = [
        jax.ShapeDtypeStruct((depth, ny), f32),
        jax.ShapeDtypeStruct((depth, ny), f32),
        jax.ShapeDtypeStruct((depth, nx), f32),
        jax.ShapeDtypeStruct((depth, nx), f32),
    ]
    out_specs = [row, row, col, col]
    if keep:
        out_shape.append(jax.ShapeDtypeStruct(block.shape, block.dtype))
        out_specs.append(whole)
    return pl.pallas_call(
        edge_kernel,
        out_shape=tuple(out_shape),
        grid=(depth // tz,),
        in_specs=[whole],
        out_specs=out_specs,
        compiler_params=pltpu.CompilerParams(dimension_semantics=("arbitrary",)),
    )(block)


def update(trans, pm_ref, pb_ref, pa_ref, qxl_ref, qxh_ref, qyl_ref, qyh_ref, f_ref, outs):
    o_ref, exl_ref, exh_ref, eyl_ref, eyh_ref = outs
    t_zp, t_zm, t_xp, t_xm, t_yp, t_ym = trans
    tz, nx, ny = pm_ref.shape
    f32 = jnp.float32
    xi = lax.broadcasted_iota(jnp.int32, (tz, nx, ny), 1)
    yi = lax.broadcasted_iota(jnp.int32, (tz, nx, ny), 2)
    p = pm_ref[...].astype(f32)
    pext = jnp.concatenate([pb_ref[...].astype(f32), p, pa_ref[...].astype(f32)], axis=0)
    n_xp = jnp.where(xi == nx - 1, x_rows(qxh_ref), pltpu.roll(p, nx - 1, 1))
    n_xm = jnp.where(xi == 0, x_rows(qxl_ref), pltpu.roll(p, 1, 1))
    n_yp = jnp.where(yi == ny - 1, to_columns(qyh_ref[...]), pltpu.roll(p, ny - 1, 2))
    n_ym = jnp.where(yi == 0, to_columns(qyl_ref[...]), pltpu.roll(p, 1, 2))

    flux = t_zp * (pext[2:] - p)
    flux = flux + t_zm * (pext[:-2] - p)
    flux = flux + t_xp * (n_xp - p)
    flux = flux + t_xm * (n_xm - p)
    flux = flux + t_yp * (n_yp - p)
    flux = flux + t_ym * (n_ym - p)
    new = p + STEP_SIZE * (flux + f_ref[...]) / (1.0 + 0.5 * p * p)
    o_ref[...] = new
    store_x_rows(exl_ref, new[:, :1, :])
    store_x_rows(exh_ref, new[:, nx - 1 :, :])
    eyl_ref[...], eyh_ref[...] = to_rows(new)


def first_step_kernel(
    inside_ref, lpm_ref, lpb_ref, lpa_ref, lxl_ref, lxh_ref, lyl_ref, lyh_ref,
    pm_ref, pb_ref, pa_ref, qxl_ref, qxh_ref, qyl_ref, qyh_ref, f_ref,
    o_ref, exl_ref, exh_ref, eyl_ref, eyh_ref, tzm_ref, txm_ref, tym_ref, txp_ref, typ_ref,
):
    c = pl.program_id(0)
    last = pl.num_programs(0) - 1
    tz, nx, ny = pm_ref.shape
    f32 = jnp.float32

    def side_perm(ref, k):
        return jnp.where(inside_ref[k] > 0, permeability(ref[...].astype(f32)), 0.0)

    kxl = jnp.where(inside_ref[0] > 0, permeability(x_rows(lxl_ref)), 0.0)
    kxh = jnp.where(inside_ref[1] > 0, permeability(x_rows(lxh_ref)), 0.0)
    kyl = to_columns(side_perm(lyl_ref, 2))
    kyh = to_columns(side_perm(lyh_ref, 3))

    below = jnp.where(c == 0, 0.0, permeability(lpb_ref[...].astype(f32)))
    above = jnp.where(c == last, 0.0, permeability(lpa_ref[...].astype(f32)))
    centre = permeability(lpm_ref[...].astype(f32))
    ext = jnp.concatenate([below, centre, above], axis=0)
    faces = harmonic(ext[:-1], ext[1:])
    t_zm = faces[:-1]
    t_zp = faces[1:]

    xi = lax.broadcasted_iota(jnp.int32, (tz, nx, ny), 1)
    yi = lax.broadcasted_iota(jnp.int32, (tz, nx, ny), 2)

    fx = harmonic(centre, pltpu.roll(centre, nx - 1, 1))
    t_xp = jnp.where(xi == nx - 1, harmonic(centre[:, nx - 1 :, :], kxh), fx)
    t_xm = jnp.where(xi == 0, harmonic(centre[:, :1, :], kxl), pltpu.roll(fx, 1, 1))
    fy = harmonic(centre, pltpu.roll(centre, ny - 1, 2))
    t_yp = jnp.where(yi == ny - 1, harmonic(centre[:, :, ny - 1 :], kyh), fy)
    t_ym = jnp.where(yi == 0, harmonic(centre[:, :, :1], kyl), pltpu.roll(fy, 1, 2))

    tzm_ref[...] = t_zm
    txm_ref[...] = t_xm
    tym_ref[...] = t_ym
    store_x_rows(txp_ref, t_xp[:, nx - 1 :, :])
    typ_ref[...] = to_rows(t_yp, last_only=True)[0]
    update(
        (t_zp, t_zm, t_xp, t_xm, t_yp, t_ym),
        pm_ref, pb_ref, pa_ref, qxl_ref, qxh_ref, qyl_ref, qyh_ref, f_ref,
        (o_ref, exl_ref, exh_ref, eyl_ref, eyh_ref),
    )


def later_step_kernel(
    tzm_ref, tza_ref, txm_ref, tym_ref, txp_ref, typ_ref,
    pm_ref, pb_ref, pa_ref, qxl_ref, qxh_ref, qyl_ref, qyh_ref, f_ref,
    o_ref, exl_ref, exh_ref, eyl_ref, eyh_ref,
):
    c = pl.program_id(0)
    last = pl.num_programs(0) - 1
    tz, nx, ny = pm_ref.shape
    xi = lax.broadcasted_iota(jnp.int32, (tz, nx, ny), 1)
    yi = lax.broadcasted_iota(jnp.int32, (tz, nx, ny), 2)
    t_zm = tzm_ref[...]
    t_zp = jnp.concatenate([t_zm[1:], jnp.where(c == last, 0.0, tza_ref[...])], axis=0)
    t_xm = txm_ref[...]
    t_xp = jnp.where(xi == nx - 1, x_rows(txp_ref), pltpu.roll(t_xm, nx - 1, 1))
    t_ym = tym_ref[...]
    t_yp = jnp.where(yi == ny - 1, to_columns(typ_ref[...]), pltpu.roll(t_ym, ny - 1, 2))
    update(
        (t_zp, t_zm, t_xp, t_xm, t_yp, t_ym),
        pm_ref, pb_ref, pa_ref, qxl_ref, qxh_ref, qyl_ref, qyh_ref, f_ref,
        (o_ref, exl_ref, exh_ref, eyl_ref, eyh_ref),
    )


def advance(stored, pressure, pressure_halos, flow, inside=None, log_perm=None, perm_halos=None):
    depth, nx, ny = pressure.shape
    tz = CHUNK_Z
    grid = (depth // tz,)
    main = pl.BlockSpec((tz, nx, ny), lambda c: (c, 0, 0))
    below = pl.BlockSpec((1, nx, ny), lambda c: (jnp.maximum(c * tz - 1, 0), 0, 0))
    above = pl.BlockSpec((1, nx, ny), lambda c: (jnp.minimum(c * tz + tz, depth - 1), 0, 0))
    row = pl.BlockSpec((tz, ny), lambda c: (c, 0))
    col = pl.BlockSpec((tz, nx), lambda c: (c, 0))
    side = [row, row, col, col]
    smem = pl.BlockSpec(memory_space=pltpu.SMEM)
    f32 = jnp.float32
    full = jax.ShapeDtypeStruct((depth, nx, ny), f32)
    rows = jax.ShapeDtypeStruct((depth, ny), f32)
    cols = jax.ShapeDtypeStruct((depth, nx), f32)
    out_shape = [full, rows, rows, cols, cols]
    out_specs = [main] + side
    pressure_args = [pressure, pressure, pressure, *pressure_halos, flow]
    pressure_specs = [main, below, above] + side + [main]
    params = pltpu.CompilerParams(dimension_semantics=("arbitrary",))
    if stored is None:
        outs = pl.pallas_call(
            first_step_kernel,
            out_shape=tuple(out_shape + [full, full, full, rows, cols]),
            grid=grid,
            in_specs=[smem, main, below, above] + side + pressure_specs,
            out_specs=out_specs + [main, main, main, row, col],
            compiler_params=params,
        )(inside, log_perm, log_perm, log_perm, *perm_halos, *pressure_args)
        return outs[0], outs[1:5], outs[5:]
    t_zm, t_xm, t_ym, t_xp, t_yp = stored
    outs = pl.pallas_call(
        later_step_kernel,
        out_shape=tuple(out_shape),
        grid=grid,
        in_specs=[main, above, main, main, row, col] + pressure_specs,
        out_specs=out_specs,
        compiler_params=params,
    )(t_zm, t_zm, t_xm, t_ym, t_xp, t_yp, *pressure_args)
    return outs[0], outs[1:5], stored


def depth_kernel(rz_ref, n_ref, o_ref):
    rz = rz_ref[...]
    for i in range(n_ref.shape[1]):
        o_ref[:, i, :] = jnp.dot(rz, n_ref[:, i, :], preferred_element_type=jnp.float32).astype(
            jnp.bfloat16
        )


def depth_transform(root_z, noise):
    depth, nx, ny = noise.shape
    bx = min(nx, DEPTH_X)
    block = pl.BlockSpec((depth, bx, ny), lambda i: (0, i, 0))
    return pl.pallas_call(
        depth_kernel,
        out_shape=jax.ShapeDtypeStruct(noise.shape, jnp.bfloat16),
        grid=(nx // bx,),
        in_specs=[pl.BlockSpec(root_z.shape, lambda i: (0, 0)), block],
        out_specs=block,
        compiler_params=pltpu.CompilerParams(dimension_semantics=("arbitrary",)),
    )(root_z, noise)


def line_kernel(g_ref, rx_ref, ry_ref, o_ref, *, count_w, count_n):
    f32 = jnp.float32
    nx = g_ref.shape[2]
    ny = g_ref.shape[3]
    rx = rx_ref[...]
    halves = []
    for n in range(count_n):
        lines = jnp.concatenate([g_ref[w * count_n + n, 0] for w in range(count_w)], axis=0)
        halves.append(jnp.dot(rx, lines, preferred_element_type=f32).astype(jnp.bfloat16))
    second = jnp.concatenate(halves, axis=1)
    third = lax.dot_general(
        second, ry_ref[...], (((1,), (1,)), ((), ())), preferred_element_type=f32
    ).astype(jnp.bfloat16)
    for w in range(count_w):
        for n in range(count_n):
            o_ref[w * count_n + n, 0] = third[w * nx : (w + 1) * nx, n * ny : (n + 1) * ny]


def line_transforms(gathered, root_x, root_y, count_w, count_n):
    groups, planes, nx, ny = gathered.shape
    block = pl.BlockSpec((groups, 1, nx, ny), lambda z: (0, z, 0, 0))
    whole_x = pl.BlockSpec(root_x.shape, lambda z: (0, 0))
    whole_y = pl.BlockSpec(root_y.shape, lambda z: (0, 0))
    return pl.pallas_call(
        functools.partial(line_kernel, count_w=count_w, count_n=count_n),
        out_shape=jax.ShapeDtypeStruct(gathered.shape, jnp.bfloat16),
        grid=(planes,),
        in_specs=[block, whole_x, whole_y],
        out_specs=block,
        compiler_params=pltpu.CompilerParams(dimension_semantics=("arbitrary",)),
    )(gathered, root_x, root_y)


def body(noise, root_z, root_x, root_y, pressure_start, well_x, well_y, well_z, well_rate):
    depth, rows_x, rows_y = noise.shape
    first = depth_transform(root_z, noise)
    count_w = lax.axis_size("wide")
    count_n = lax.axis_size("narrow")
    groups = count_w * count_n
    planes = depth // groups
    gathered = lax.all_to_all(
        first.reshape(groups, planes, rows_x, rows_y),
        ("wide", "narrow"), split_axis=0, concat_axis=0, tiled=True,
    )
    wide_at = lax.axis_index("wide")
    narrow_at = lax.axis_index("narrow")
    last_w = lax.axis_size("wide") - 1
    last_n = lax.axis_size("narrow") - 1

    local_x = well_x - wide_at * rows_x
    local_y = well_y - narrow_at * rows_y
    valid = (local_x >= 0) & (local_x < rows_x) & (local_y >= 0) & (local_y < rows_y)
    rates = jnp.where(valid, well_rate, 0.0).astype(jnp.float32)
    wells = well_x.shape[0]
    cells = well_z * rows_x + local_x
    pick_rows = jnp.where(
        lax.broadcasted_iota(jnp.int32, (depth * rows_x, wells), 0) == cells[None, :],
        rates[None, :],
        0.0,
    )
    pick_cols = (
        lax.broadcasted_iota(jnp.int32, (wells, rows_y), 1) == local_y[:, None]
    ).astype(jnp.float32)
    flow = jnp.dot(
        pick_rows, pick_cols, precision=lax.Precision.HIGHEST, preferred_element_type=jnp.float32
    ).reshape(depth, rows_x, rows_y)

    inside = jnp.stack(
        [wide_at > 0, wide_at < last_w, narrow_at > 0, narrow_at < last_n]
    ).astype(jnp.int32)
    edges = block_edges(pressure_start)
    gathered, flow, edges = lax.optimization_barrier((gathered, flow, edges))
    outgoing = line_transforms(gathered, root_x, root_y, count_w, count_n)
    log_perm = lax.all_to_all(
        outgoing, ("wide", "narrow"), split_axis=0, concat_axis=0, tiled=True,
    ).reshape(depth, rows_x, rows_y)

    *lp_edges, log_perm = block_edges(log_perm, keep=True)
    perm_halos = halos(lp_edges)
    pressure = pressure_start
    stored = None
    for step in range(STEPS):
        pressure, edges, stored = advance(
            stored, pressure, halos(edges), flow, inside, log_perm, perm_halos
        )
    return (log_perm, pressure)


def solution(mesh):
    in_specs = (
        P("member", "wide", "narrow"),
        P(),
        P(),
        P(),
        P("member", "wide", "narrow"),
        P("member"),
        P("member"),
        P("member"),
        P("member"),
    )
    out_specs = (P("member", "wide", "narrow"), P("member", "wide", "narrow"))
    return jax.shard_map(body, mesh=mesh, in_specs=in_specs, out_specs=out_specs, check_vma=False)
```

```python
import functools

import jax
import jax.numpy as jnp
from jax import lax
from jax.experimental import pallas as pl
from jax.experimental.pallas import tpu as pltpu
from jax.sharding import PartitionSpec as P

STEPS = 2


STEP_SIZE = 0.03
CAP_LOG = 1.5
CHUNK_Z = 16
EDGE_Z = 64
DEPTH_X = 16


def permeability(values):
    return jnp.exp(CAP_LOG * jnp.tanh(values / CAP_LOG))


def harmonic(a, b):
    return 2.0 * a * b / (a + b)


def halos(edges):
    forward_w = [(i, i + 1) for i in range(lax.axis_size("wide") - 1)]
    backward_w = [(j, i) for i, j in forward_w]
    forward_n = [(i, i + 1) for i in range(lax.axis_size("narrow") - 1)]
    backward_n = [(j, i) for i, j in forward_n]
    first_x, last_x, first_y, last_y = edges
    x_lo = lax.ppermute(last_x, "wide", forward_w)
    x_hi = lax.ppermute(first_x, "wide", backward_w)
    y_lo = lax.ppermute(last_y, "narrow", forward_n)
    y_hi = lax.ppermute(first_y, "narrow", backward_n)
    return x_lo, x_hi, y_lo, y_hi


def to_columns(rows):
    tz, nx = rows.shape
    eye = jnp.where(
        lax.broadcasted_iota(jnp.int32, (nx, nx), 0) == lax.broadcasted_iota(jnp.int32, (nx, nx), 1),
        1.0, 0.0,
    )
    cols = lax.dot_general(
        eye, rows, (((1,), (1,)), ((), ())),
        precision=lax.Precision.HIGHEST, preferred_element_type=jnp.float32,
    )
    return jnp.concatenate([cols[:, k : k + 1][None] for k in range(tz)], axis=0)


def x_rows(ref):
    return jnp.concatenate([ref[k : k + 1, :][None] for k in range(ref.shape[0])], axis=0)


def store_x_rows(ref, rows):
    for k in range(ref.shape[0]):
        ref[k : k + 1, :] = rows[k]


def to_rows(block):
    tz, nx, ny = block.shape
    lane = lax.broadcasted_iota(jnp.int32, (nx, 128), 1)
    pick = jnp.where(
        lax.broadcasted_iota(jnp.int32, (tz, 128), 0) == lax.broadcasted_iota(jnp.int32, (tz, 128), 1),
        1.0, 0.0,
    )
    result = []
    for column in (0, ny - 1):
        gathered = jnp.zeros((nx, 128), jnp.float32)
        for k in range(tz):
            gathered = jnp.where(lane == k, block[k, :, column : column + 1], gathered)
        result.append(
            lax.dot_general(
                pick, gathered, (((1,), (1,)), ((), ())),
                precision=lax.Precision.HIGHEST, preferred_element_type=jnp.float32,
            )
        )
    return result[0], result[1]


def edge_kernel(block_ref, xl_ref, xh_ref, yl_ref, yh_ref, *copy_ref):
    block = block_ref[...]
    if copy_ref:
        copy_ref[0][...] = block
    block = block.astype(jnp.float32)
    store_x_rows(xl_ref, block[:, :1, :])
    store_x_rows(xh_ref, block[:, -1:, :])
    yl_ref[...], yh_ref[...] = to_rows(block)


def block_edges(block, keep=False):
    depth, nx, ny = block.shape
    tz = EDGE_Z
    f32 = jnp.float32
    whole = pl.BlockSpec((tz, nx, ny), lambda c: (c, 0, 0))
    row = pl.BlockSpec((tz, ny), lambda c: (c, 0))
    col = pl.BlockSpec((tz, nx), lambda c: (c, 0))
    out_shape = [
        jax.ShapeDtypeStruct((depth, ny), f32),
        jax.ShapeDtypeStruct((depth, ny), f32),
        jax.ShapeDtypeStruct((depth, nx), f32),
        jax.ShapeDtypeStruct((depth, nx), f32),
    ]
    out_specs = [row, row, col, col]
    if keep:
        out_shape.append(jax.ShapeDtypeStruct(block.shape, block.dtype))
        out_specs.append(whole)
    return pl.pallas_call(
        edge_kernel,
        out_shape=tuple(out_shape),
        grid=(depth // tz,),
        in_specs=[whole],
        out_specs=out_specs,
        compiler_params=pltpu.CompilerParams(dimension_semantics=("arbitrary",)),
    )(block)


def update(trans, pm_ref, pb_ref, pa_ref, qxl_ref, qxh_ref, qyl_ref, qyh_ref, f_ref, outs):
    o_ref, exl_ref, exh_ref, eyl_ref, eyh_ref = outs
    t_zp, t_zm, t_xp, t_xm, t_yp, t_ym = trans
    tz, nx, ny = pm_ref.shape
    f32 = jnp.float32
    xi = lax.broadcasted_iota(jnp.int32, (tz, nx, ny), 1)
    yi = lax.broadcasted_iota(jnp.int32, (tz, nx, ny), 2)
    p = pm_ref[...].astype(f32)
    pext = jnp.concatenate([pb_ref[...].astype(f32), p, pa_ref[...].astype(f32)], axis=0)
    n_xp = jnp.where(xi == nx - 1, x_rows(qxh_ref), pltpu.roll(p, nx - 1, 1))
    n_xm = jnp.where(xi == 0, x_rows(qxl_ref), pltpu.roll(p, 1, 1))
    n_yp = jnp.where(yi == ny - 1, to_columns(qyh_ref[...]), pltpu.roll(p, ny - 1, 2))
    n_ym = jnp.where(yi == 0, to_columns(qyl_ref[...]), pltpu.roll(p, 1, 2))

    flux = t_zp * (pext[2:] - p)
    flux = flux + t_zm * (pext[:-2] - p)
    flux = flux + t_xp * (n_xp - p)
    flux = flux + t_xm * (n_xm - p)
    flux = flux + t_yp * (n_yp - p)
    flux = flux + t_ym * (n_ym - p)
    new = p + STEP_SIZE * (flux + f_ref[...]) / (1.0 + 0.5 * p * p)
    o_ref[...] = new
    store_x_rows(exl_ref, new[:, :1, :])
    store_x_rows(exh_ref, new[:, nx - 1 :, :])
    eyl_ref[...], eyh_ref[...] = to_rows(new)


def first_step_kernel(
    inside_ref, lpm_ref, lpb_ref, lpa_ref, lxl_ref, lxh_ref, lyl_ref, lyh_ref,
    pm_ref, pb_ref, pa_ref, qxl_ref, qxh_ref, qyl_ref, qyh_ref, f_ref,
    o_ref, exl_ref, exh_ref, eyl_ref, eyh_ref, tzm_ref, txm_ref, tym_ref, txp_ref, typ_ref,
):
    c = pl.program_id(0)
    last = pl.num_programs(0) - 1
    tz, nx, ny = pm_ref.shape
    f32 = jnp.float32

    def side_perm(ref, k):
        return jnp.where(inside_ref[k] > 0, permeability(ref[...].astype(f32)), 0.0)

    kxl = jnp.where(inside_ref[0] > 0, permeability(x_rows(lxl_ref)), 0.0)
    kxh = jnp.where(inside_ref[1] > 0, permeability(x_rows(lxh_ref)), 0.0)
    kyl = to_columns(side_perm(lyl_ref, 2))
    kyh = to_columns(side_perm(lyh_ref, 3))

    below = jnp.where(c == 0, 0.0, permeability(lpb_ref[...].astype(f32)))
    above = jnp.where(c == last, 0.0, permeability(lpa_ref[...].astype(f32)))
    centre = permeability(lpm_ref[...].astype(f32))
    ext = jnp.concatenate([below, centre, above], axis=0)
    faces = harmonic(ext[:-1], ext[1:])
    t_zm = faces[:-1]
    t_zp = faces[1:]

    xi = lax.broadcasted_iota(jnp.int32, (tz, nx, ny), 1)
    yi = lax.broadcasted_iota(jnp.int32, (tz, nx, ny), 2)

    fx = harmonic(centre, pltpu.roll(centre, nx - 1, 1))
    t_xp = jnp.where(xi == nx - 1, harmonic(centre[:, nx - 1 :, :], kxh), fx)
    t_xm = jnp.where(xi == 0, harmonic(centre[:, :1, :], kxl), pltpu.roll(fx, 1, 1))
    fy = harmonic(centre, pltpu.roll(centre, ny - 1, 2))
    t_yp = jnp.where(yi == ny - 1, harmonic(centre[:, :, ny - 1 :], kyh), fy)
    t_ym = jnp.where(yi == 0, harmonic(centre[:, :, :1], kyl), pltpu.roll(fy, 1, 2))

    tzm_ref[...] = t_zm
    txm_ref[...] = t_xm
    tym_ref[...] = t_ym
    store_x_rows(txp_ref, t_xp[:, nx - 1 :, :])
    typ_ref[...] = to_rows(t_yp)[1]
    update(
        (t_zp, t_zm, t_xp, t_xm, t_yp, t_ym),
        pm_ref, pb_ref, pa_ref, qxl_ref, qxh_ref, qyl_ref, qyh_ref, f_ref,
        (o_ref, exl_ref, exh_ref, eyl_ref, eyh_ref),
    )


def later_step_kernel(
    tzm_ref, tza_ref, txm_ref, tym_ref, txp_ref, typ_ref,
    pm_ref, pb_ref, pa_ref, qxl_ref, qxh_ref, qyl_ref, qyh_ref, f_ref,
    o_ref, exl_ref, exh_ref, eyl_ref, eyh_ref,
):
    c = pl.program_id(0)
    last = pl.num_programs(0) - 1
    tz, nx, ny = pm_ref.shape
    xi = lax.broadcasted_iota(jnp.int32, (tz, nx, ny), 1)
    yi = lax.broadcasted_iota(jnp.int32, (tz, nx, ny), 2)
    t_zm = tzm_ref[...]
    t_zp = jnp.concatenate([t_zm[1:], jnp.where(c == last, 0.0, tza_ref[...])], axis=0)
    t_xm = txm_ref[...]
    t_xp = jnp.where(xi == nx - 1, x_rows(txp_ref), pltpu.roll(t_xm, nx - 1, 1))
    t_ym = tym_ref[...]
    t_yp = jnp.where(yi == ny - 1, to_columns(typ_ref[...]), pltpu.roll(t_ym, ny - 1, 2))
    update(
        (t_zp, t_zm, t_xp, t_xm, t_yp, t_ym),
        pm_ref, pb_ref, pa_ref, qxl_ref, qxh_ref, qyl_ref, qyh_ref, f_ref,
        (o_ref, exl_ref, exh_ref, eyl_ref, eyh_ref),
    )


def advance(stored, pressure, pressure_halos, flow, inside=None, log_perm=None, perm_halos=None):
    depth, nx, ny = pressure.shape
    tz = CHUNK_Z
    grid = (depth // tz,)
    main = pl.BlockSpec((tz, nx, ny), lambda c: (c, 0, 0))
    below = pl.BlockSpec((1, nx, ny), lambda c: (jnp.maximum(c * tz - 1, 0), 0, 0))
    above = pl.BlockSpec((1, nx, ny), lambda c: (jnp.minimum(c * tz + tz, depth - 1), 0, 0))
    row = pl.BlockSpec((tz, ny), lambda c: (c, 0))
    col = pl.BlockSpec((tz, nx), lambda c: (c, 0))
    side = [row, row, col, col]
    smem = pl.BlockSpec(memory_space=pltpu.SMEM)
    f32 = jnp.float32
    full = jax.ShapeDtypeStruct((depth, nx, ny), f32)
    rows = jax.ShapeDtypeStruct((depth, ny), f32)
    cols = jax.ShapeDtypeStruct((depth, nx), f32)
    out_shape = [full, rows, rows, cols, cols]
    out_specs = [main] + side
    pressure_args = [pressure, pressure, pressure, *pressure_halos, flow]
    pressure_specs = [main, below, above] + side + [main]
    params = pltpu.CompilerParams(dimension_semantics=("arbitrary",))
    if stored is None:
        outs = pl.pallas_call(
            first_step_kernel,
            out_shape=tuple(out_shape + [full, full, full, rows, cols]),
            grid=grid,
            in_specs=[smem, main, below, above] + side + pressure_specs,
            out_specs=out_specs + [main, main, main, row, col],
            compiler_params=params,
        )(inside, log_perm, log_perm, log_perm, *perm_halos, *pressure_args)
        return outs[0], outs[1:5], outs[5:]
    t_zm, t_xm, t_ym, t_xp, t_yp = stored
    outs = pl.pallas_call(
        later_step_kernel,
        out_shape=tuple(out_shape),
        grid=grid,
        in_specs=[main, above, main, main, row, col] + pressure_specs,
        out_specs=out_specs,
        compiler_params=params,
    )(t_zm, t_zm, t_xm, t_ym, t_xp, t_yp, *pressure_args)
    return outs[0], outs[1:5], stored


def depth_kernel(rz_ref, n_ref, o_ref):
    rz = rz_ref[...]
    for i in range(n_ref.shape[1]):
        o_ref[:, i, :] = jnp.dot(rz, n_ref[:, i, :], preferred_element_type=jnp.float32).astype(
            jnp.bfloat16
        )


def depth_transform(root_z, noise):
    depth, nx, ny = noise.shape
    bx = min(nx, DEPTH_X)
    block = pl.BlockSpec((depth, bx, ny), lambda i: (0, i, 0))
    return pl.pallas_call(
        depth_kernel,
        out_shape=jax.ShapeDtypeStruct(noise.shape, jnp.bfloat16),
        grid=(nx // bx,),
        in_specs=[pl.BlockSpec(root_z.shape, lambda i: (0, 0)), block],
        out_specs=block,
        compiler_params=pltpu.CompilerParams(dimension_semantics=("arbitrary",)),
    )(root_z, noise)


def line_kernel(g_ref, rx_ref, ry_ref, o_ref, *, count_w, count_n):
    f32 = jnp.float32
    nx = g_ref.shape[2]
    ny = g_ref.shape[3]
    rx = rx_ref[...]
    for z in range(g_ref.shape[1]):
        halves = []
        for n in range(count_n):
            lines = jnp.concatenate([g_ref[w * count_n + n, z] for w in range(count_w)], axis=0)
            halves.append(jnp.dot(rx, lines, preferred_element_type=f32).astype(jnp.bfloat16))
        second = jnp.concatenate(halves, axis=1)
        third = lax.dot_general(
            second, ry_ref[...], (((1,), (1,)), ((), ())), preferred_element_type=f32
        ).astype(jnp.bfloat16)
        for w in range(count_w):
            for n in range(count_n):
                o_ref[w * count_n + n, z] = third[w * nx : (w + 1) * nx, n * ny : (n + 1) * ny]


def line_transforms(gathered, root_x, root_y, count_w, count_n):
    groups, planes, nx, ny = gathered.shape
    step = 2 if planes % 2 == 0 else 1
    block = pl.BlockSpec((groups, step, nx, ny), lambda z: (0, z, 0, 0))
    whole_x = pl.BlockSpec(root_x.shape, lambda z: (0, 0))
    whole_y = pl.BlockSpec(root_y.shape, lambda z: (0, 0))
    return pl.pallas_call(
        functools.partial(line_kernel, count_w=count_w, count_n=count_n),
        out_shape=jax.ShapeDtypeStruct(gathered.shape, jnp.bfloat16),
        grid=(planes // step,),
        in_specs=[block, whole_x, whole_y],
        out_specs=block,
        compiler_params=pltpu.CompilerParams(dimension_semantics=("arbitrary",)),
    )(gathered, root_x, root_y)


def body(noise, root_z, root_x, root_y, pressure_start, well_x, well_y, well_z, well_rate):
    depth, rows_x, rows_y = noise.shape
    first = depth_transform(root_z, noise)
    count_w = lax.axis_size("wide")
    count_n = lax.axis_size("narrow")
    groups = count_w * count_n
    planes = depth // groups
    gathered = lax.all_to_all(
        first.reshape(groups, planes, rows_x, rows_y),
        ("wide", "narrow"), split_axis=0, concat_axis=0, tiled=True,
    )
    wide_at = lax.axis_index("wide")
    narrow_at = lax.axis_index("narrow")
    last_w = lax.axis_size("wide") - 1
    last_n = lax.axis_size("narrow") - 1

    local_x = well_x - wide_at * rows_x
    local_y = well_y - narrow_at * rows_y
    valid = (local_x >= 0) & (local_x < rows_x) & (local_y >= 0) & (local_y < rows_y)
    rates = jnp.where(valid, well_rate, 0.0).astype(jnp.float32)
    wells = well_x.shape[0]
    cells = well_z * rows_x + local_x
    pick_rows = jnp.where(
        lax.broadcasted_iota(jnp.int32, (depth * rows_x, wells), 0) == cells[None, :],
        rates[None, :],
        0.0,
    )
    pick_cols = (
        lax.broadcasted_iota(jnp.int32, (wells, rows_y), 1) == local_y[:, None]
    ).astype(jnp.float32)
    flow = jnp.dot(
        pick_rows, pick_cols, precision=lax.Precision.HIGHEST, preferred_element_type=jnp.float32
    ).reshape(depth, rows_x, rows_y)

    inside = jnp.stack(
        [wide_at > 0, wide_at < last_w, narrow_at > 0, narrow_at < last_n]
    ).astype(jnp.int32)
    edges = block_edges(pressure_start)
    gathered, flow, edges = lax.optimization_barrier((gathered, flow, edges))
    outgoing = line_transforms(gathered, root_x, root_y, count_w, count_n)
    log_perm = lax.all_to_all(
        outgoing, ("wide", "narrow"), split_axis=0, concat_axis=0, tiled=True,
    ).reshape(depth, rows_x, rows_y)

    *lp_edges, log_perm = block_edges(log_perm, keep=True)
    perm_halos = halos(lp_edges)
    pressure = pressure_start
    stored = None
    for step in range(STEPS):
        pressure, edges, stored = advance(
            stored, pressure, halos(edges), flow, inside, log_perm, perm_halos
        )
    return (log_perm, pressure)


def solution(mesh):
    in_specs = (
        P("member", "wide", "narrow"),
        P(),
        P(),
        P(),
        P("member", "wide", "narrow"),
        P("member"),
        P("member"),
        P("member"),
        P("member"),
    )
    out_specs = (P("member", "wide", "narrow"), P("member", "wide", "narrow"))
    return jax.shard_map(body, mesh=mesh, in_specs=in_specs, out_specs=out_specs, check_vma=False)
```

```python
import functools

import jax
import jax.numpy as jnp
from jax import lax
from jax.experimental import pallas as pl
from jax.experimental.pallas import tpu as pltpu
from jax.sharding import PartitionSpec as P

STEPS = 2


STEP_SIZE = 0.03
CAP_LOG = 1.5
CHUNK_Z = 16
EDGE_Z = 64
DEPTH_X = 16


def permeability(values):
    return jnp.exp(CAP_LOG * jnp.tanh(values / CAP_LOG))


def harmonic(a, b):
    return 2.0 * a * b / (a + b)


def halos(edges):
    forward_w = [(i, i + 1) for i in range(lax.axis_size("wide") - 1)]
    backward_w = [(j, i) for i, j in forward_w]
    forward_n = [(i, i + 1) for i in range(lax.axis_size("narrow") - 1)]
    backward_n = [(j, i) for i, j in forward_n]
    first_x, last_x, first_y, last_y = edges
    x_lo = lax.ppermute(last_x, "wide", forward_w)
    x_hi = lax.ppermute(first_x, "wide", backward_w)
    y_lo = lax.ppermute(last_y, "narrow", forward_n)
    y_hi = lax.ppermute(first_y, "narrow", backward_n)
    return x_lo, x_hi, y_lo, y_hi


def to_columns(rows):
    tz, nx = rows.shape
    eye = jnp.where(
        lax.broadcasted_iota(jnp.int32, (nx, nx), 0) == lax.broadcasted_iota(jnp.int32, (nx, nx), 1),
        1.0, 0.0,
    )
    cols = lax.dot_general(
        eye, rows, (((1,), (1,)), ((), ())),
        precision=lax.Precision.HIGHEST, preferred_element_type=jnp.float32,
    )
    return jnp.concatenate([cols[:, k : k + 1][None] for k in range(tz)], axis=0)


def x_rows(ref):
    return jnp.concatenate([ref[k : k + 1, :][None] for k in range(ref.shape[0])], axis=0)


def store_x_rows(ref, rows):
    for k in range(ref.shape[0]):
        ref[k : k + 1, :] = rows[k]


def to_rows(block):
    tz, nx, ny = block.shape
    lane = lax.broadcasted_iota(jnp.int32, (nx, 128), 1)
    pick = jnp.where(
        lax.broadcasted_iota(jnp.int32, (tz, 128), 0) == lax.broadcasted_iota(jnp.int32, (tz, 128), 1),
        1.0, 0.0,
    )
    result = []
    for column in (0, ny - 1):
        gathered = jnp.zeros((nx, 128), jnp.float32)
        for k in range(tz):
            gathered = jnp.where(lane == k, block[k, :, column : column + 1], gathered)
        result.append(
            lax.dot_general(
                pick, gathered, (((1,), (1,)), ((), ())),
                precision=lax.Precision.HIGHEST, preferred_element_type=jnp.float32,
            )
        )
    return result[0], result[1]


def edge_kernel(block_ref, xl_ref, xh_ref, yl_ref, yh_ref, *copy_ref):
    block = block_ref[...]
    if copy_ref:
        copy_ref[0][...] = block
    block = block.astype(jnp.float32)
    store_x_rows(xl_ref, block[:, :1, :])
    store_x_rows(xh_ref, block[:, -1:, :])
    yl_ref[...], yh_ref[...] = to_rows(block)


def block_edges(block, keep=False):
    depth, nx, ny = block.shape
    tz = EDGE_Z
    f32 = jnp.float32
    whole = pl.BlockSpec((tz, nx, ny), lambda c: (c, 0, 0))
    row = pl.BlockSpec((tz, ny), lambda c: (c, 0))
    col = pl.BlockSpec((tz, nx), lambda c: (c, 0))
    out_shape = [
        jax.ShapeDtypeStruct((depth, ny), f32),
        jax.ShapeDtypeStruct((depth, ny), f32),
        jax.ShapeDtypeStruct((depth, nx), f32),
        jax.ShapeDtypeStruct((depth, nx), f32),
    ]
    out_specs = [row, row, col, col]
    if keep:
        out_shape.append(jax.ShapeDtypeStruct(block.shape, block.dtype))
        out_specs.append(whole)
    return pl.pallas_call(
        edge_kernel,
        out_shape=tuple(out_shape),
        grid=(depth // tz,),
        in_specs=[whole],
        out_specs=out_specs,
        compiler_params=pltpu.CompilerParams(dimension_semantics=("arbitrary",)),
    )(block)


def update(trans, pm_ref, pb_ref, pa_ref, qxl_ref, qxh_ref, qyl_ref, qyh_ref, f_ref, outs):
    o_ref, exl_ref, exh_ref, eyl_ref, eyh_ref = outs
    t_zp, t_zm, t_xp, t_xm, t_yp, t_ym = trans
    tz, nx, ny = pm_ref.shape
    f32 = jnp.float32
    xi = lax.broadcasted_iota(jnp.int32, (tz, nx, ny), 1)
    yi = lax.broadcasted_iota(jnp.int32, (tz, nx, ny), 2)
    p = pm_ref[...].astype(f32)
    pext = jnp.concatenate([pb_ref[...].astype(f32), p, pa_ref[...].astype(f32)], axis=0)
    n_xp = jnp.where(xi == nx - 1, x_rows(qxh_ref), pltpu.roll(p, nx - 1, 1))
    n_xm = jnp.where(xi == 0, x_rows(qxl_ref), pltpu.roll(p, 1, 1))
    n_yp = jnp.where(yi == ny - 1, to_columns(qyh_ref[...]), pltpu.roll(p, ny - 1, 2))
    n_ym = jnp.where(yi == 0, to_columns(qyl_ref[...]), pltpu.roll(p, 1, 2))

    flux = t_zp * (pext[2:] - p)
    flux = flux + t_zm * (pext[:-2] - p)
    flux = flux + t_xp * (n_xp - p)
    flux = flux + t_xm * (n_xm - p)
    flux = flux + t_yp * (n_yp - p)
    flux = flux + t_ym * (n_ym - p)
    new = p + STEP_SIZE * (flux + f_ref[...]) / (1.0 + 0.5 * p * p)
    o_ref[...] = new
    store_x_rows(exl_ref, new[:, :1, :])
    store_x_rows(exh_ref, new[:, nx - 1 :, :])
    eyl_ref[...], eyh_ref[...] = to_rows(new)


def first_step_kernel(
    inside_ref, lpm_ref, lpb_ref, lpa_ref, lxl_ref, lxh_ref, lyl_ref, lyh_ref,
    pm_ref, pb_ref, pa_ref, qxl_ref, qxh_ref, qyl_ref, qyh_ref, f_ref,
    o_ref, exl_ref, exh_ref, eyl_ref, eyh_ref, tzm_ref, txm_ref, tym_ref, txp_ref, typ_ref,
):
    c = pl.program_id(0)
    last = pl.num_programs(0) - 1
    tz, nx, ny = pm_ref.shape
    f32 = jnp.float32

    def side_perm(ref, k):
        return jnp.where(inside_ref[k] > 0, permeability(ref[...].astype(f32)), 0.0)

    kxl = jnp.where(inside_ref[0] > 0, permeability(x_rows(lxl_ref)), 0.0)
    kxh = jnp.where(inside_ref[1] > 0, permeability(x_rows(lxh_ref)), 0.0)
    kyl = to_columns(side_perm(lyl_ref, 2))
    kyh = to_columns(side_perm(lyh_ref, 3))

    below = jnp.where(c == 0, 0.0, permeability(lpb_ref[...].astype(f32)))
    above = jnp.where(c == last, 0.0, permeability(lpa_ref[...].astype(f32)))
    centre = permeability(lpm_ref[...].astype(f32))
    ext = jnp.concatenate([below, centre, above], axis=0)
    faces = harmonic(ext[:-1], ext[1:])
    t_zm = faces[:-1]
    t_zp = faces[1:]

    xi = lax.broadcasted_iota(jnp.int32, (tz, nx, ny), 1)
    yi = lax.broadcasted_iota(jnp.int32, (tz, nx, ny), 2)

    fx = harmonic(centre, pltpu.roll(centre, nx - 1, 1))
    t_xp = jnp.where(xi == nx - 1, harmonic(centre[:, nx - 1 :, :], kxh), fx)
    t_xm = jnp.where(xi == 0, harmonic(centre[:, :1, :], kxl), pltpu.roll(fx, 1, 1))
    fy = harmonic(centre, pltpu.roll(centre, ny - 1, 2))
    t_yp = jnp.where(yi == ny - 1, harmonic(centre[:, :, ny - 1 :], kyh), fy)
    t_ym = jnp.where(yi == 0, harmonic(centre[:, :, :1], kyl), pltpu.roll(fy, 1, 2))

    tzm_ref[...] = t_zm
    txm_ref[...] = t_xm
    tym_ref[...] = t_ym
    store_x_rows(txp_ref, t_xp[:, nx - 1 :, :])
    typ_ref[...] = to_rows(t_yp)[1]
    update(
        (t_zp, t_zm, t_xp, t_xm, t_yp, t_ym),
        pm_ref, pb_ref, pa_ref, qxl_ref, qxh_ref, qyl_ref, qyh_ref, f_ref,
        (o_ref, exl_ref, exh_ref, eyl_ref, eyh_ref),
    )


def later_step_kernel(
    tzm_ref, tza_ref, txm_ref, tym_ref, txp_ref, typ_ref,
    pm_ref, pb_ref, pa_ref, qxl_ref, qxh_ref, qyl_ref, qyh_ref, f_ref,
    o_ref, exl_ref, exh_ref, eyl_ref, eyh_ref,
):
    c = pl.program_id(0)
    last = pl.num_programs(0) - 1
    tz, nx, ny = pm_ref.shape
    xi = lax.broadcasted_iota(jnp.int32, (tz, nx, ny), 1)
    yi = lax.broadcasted_iota(jnp.int32, (tz, nx, ny), 2)
    t_zm = tzm_ref[...]
    t_zp = jnp.concatenate([t_zm[1:], jnp.where(c == last, 0.0, tza_ref[...])], axis=0)
    t_xm = txm_ref[...]
    t_xp = jnp.where(xi == nx - 1, x_rows(txp_ref), pltpu.roll(t_xm, nx - 1, 1))
    t_ym = tym_ref[...]
    t_yp = jnp.where(yi == ny - 1, to_columns(typ_ref[...]), pltpu.roll(t_ym, ny - 1, 2))
    update(
        (t_zp, t_zm, t_xp, t_xm, t_yp, t_ym),
        pm_ref, pb_ref, pa_ref, qxl_ref, qxh_ref, qyl_ref, qyh_ref, f_ref,
        (o_ref, exl_ref, exh_ref, eyl_ref, eyh_ref),
    )


def advance(stored, pressure, pressure_halos, flow, inside=None, log_perm=None, perm_halos=None):
    depth, nx, ny = pressure.shape
    tz = CHUNK_Z
    grid = (depth // tz,)
    main = pl.BlockSpec((tz, nx, ny), lambda c: (c, 0, 0))
    below = pl.BlockSpec((1, nx, ny), lambda c: (jnp.maximum(c * tz - 1, 0), 0, 0))
    above = pl.BlockSpec((1, nx, ny), lambda c: (jnp.minimum(c * tz + tz, depth - 1), 0, 0))
    row = pl.BlockSpec((tz, ny), lambda c: (c, 0))
    col = pl.BlockSpec((tz, nx), lambda c: (c, 0))
    side = [row, row, col, col]
    smem = pl.BlockSpec(memory_space=pltpu.SMEM)
    f32 = jnp.float32
    full = jax.ShapeDtypeStruct((depth, nx, ny), f32)
    rows = jax.ShapeDtypeStruct((depth, ny), f32)
    cols = jax.ShapeDtypeStruct((depth, nx), f32)
    out_shape = [full, rows, rows, cols, cols]
    out_specs = [main] + side
    pressure_args = [pressure, pressure, pressure, *pressure_halos, flow]
    pressure_specs = [main, below, above] + side + [main]
    params = pltpu.CompilerParams(dimension_semantics=("arbitrary",))
    if stored is None:
        outs = pl.pallas_call(
            first_step_kernel,
            out_shape=tuple(out_shape + [full, full, full, rows, cols]),
            grid=grid,
            in_specs=[smem, main, below, above] + side + pressure_specs,
            out_specs=out_specs + [main, main, main, row, col],
            compiler_params=params,
        )(inside, log_perm, log_perm, log_perm, *perm_halos, *pressure_args)
        return outs[0], outs[1:5], outs[5:]
    t_zm, t_xm, t_ym, t_xp, t_yp = stored
    outs = pl.pallas_call(
        later_step_kernel,
        out_shape=tuple(out_shape),
        grid=grid,
        in_specs=[main, above, main, main, row, col] + pressure_specs,
        out_specs=out_specs,
        compiler_params=params,
    )(t_zm, t_zm, t_xm, t_ym, t_xp, t_yp, *pressure_args)
    return outs[0], outs[1:5], stored


def depth_kernel(rz_ref, n_ref, o_ref):
    rz = rz_ref[...]
    for i in range(n_ref.shape[1]):
        o_ref[:, i, :] = jnp.dot(rz, n_ref[:, i, :], preferred_element_type=jnp.float32).astype(
            jnp.bfloat16
        )


def depth_transform(root_z, noise):
    depth, nx, ny = noise.shape
    bx = min(nx, DEPTH_X)
    block = pl.BlockSpec((depth, bx, ny), lambda i: (0, i, 0))
    return pl.pallas_call(
        depth_kernel,
        out_shape=jax.ShapeDtypeStruct(noise.shape, jnp.bfloat16),
        grid=(nx // bx,),
        in_specs=[pl.BlockSpec(root_z.shape, lambda i: (0, 0)), block],
        out_specs=block,
        compiler_params=pltpu.CompilerParams(dimension_semantics=("arbitrary",)),
    )(root_z, noise)


def line_kernel(g_ref, rx_ref, ry_ref, o_ref, *, count_w, count_n):
    f32 = jnp.float32
    nx = g_ref.shape[2]
    ny = g_ref.shape[3]
    rx = rx_ref[...]
    for z in range(g_ref.shape[1]):
        halves = []
        for n in range(count_n):
            lines = jnp.concatenate([g_ref[w * count_n + n, z] for w in range(count_w)], axis=0)
            halves.append(jnp.dot(rx, lines, preferred_element_type=f32).astype(jnp.bfloat16))
        second = jnp.concatenate(halves, axis=1)
        third = lax.dot_general(
            second, ry_ref[...], (((1,), (1,)), ((), ())), preferred_element_type=f32
        ).astype(jnp.bfloat16)
        for w in range(count_w):
            for n in range(count_n):
                o_ref[w * count_n + n, z] = third[w * nx : (w + 1) * nx, n * ny : (n + 1) * ny]


def line_transforms(gathered, root_x, root_y, count_w, count_n):
    groups, planes, nx, ny = gathered.shape
    step = 4 if planes % 4 == 0 else (2 if planes % 2 == 0 else 1)
    block = pl.BlockSpec((groups, step, nx, ny), lambda z: (0, z, 0, 0))
    whole_x = pl.BlockSpec(root_x.shape, lambda z: (0, 0))
    whole_y = pl.BlockSpec(root_y.shape, lambda z: (0, 0))
    return pl.pallas_call(
        functools.partial(line_kernel, count_w=count_w, count_n=count_n),
        out_shape=jax.ShapeDtypeStruct(gathered.shape, jnp.bfloat16),
        grid=(planes // step,),
        in_specs=[block, whole_x, whole_y],
        out_specs=block,
        compiler_params=pltpu.CompilerParams(dimension_semantics=("arbitrary",)),
    )(gathered, root_x, root_y)


def body(noise, root_z, root_x, root_y, pressure_start, well_x, well_y, well_z, well_rate):
    depth, rows_x, rows_y = noise.shape
    first = depth_transform(root_z, noise)
    count_w = lax.axis_size("wide")
    count_n = lax.axis_size("narrow")
    groups = count_w * count_n
    planes = depth // groups
    gathered = lax.all_to_all(
        first.reshape(groups, planes, rows_x, rows_y),
        ("wide", "narrow"), split_axis=0, concat_axis=0, tiled=True,
    )
    wide_at = lax.axis_index("wide")
    narrow_at = lax.axis_index("narrow")
    last_w = lax.axis_size("wide") - 1
    last_n = lax.axis_size("narrow") - 1

    local_x = well_x - wide_at * rows_x
    local_y = well_y - narrow_at * rows_y
    valid = (local_x >= 0) & (local_x < rows_x) & (local_y >= 0) & (local_y < rows_y)
    rates = jnp.where(valid, well_rate, 0.0).astype(jnp.float32)
    wells = well_x.shape[0]
    cells = well_z * rows_x + local_x
    pick_rows = jnp.where(
        lax.broadcasted_iota(jnp.int32, (depth * rows_x, wells), 0) == cells[None, :],
        rates[None, :],
        0.0,
    )
    pick_cols = (
        lax.broadcasted_iota(jnp.int32, (wells, rows_y), 1) == local_y[:, None]
    ).astype(jnp.float32)
    flow = jnp.dot(
        pick_rows, pick_cols, precision=lax.Precision.HIGHEST, preferred_element_type=jnp.float32
    ).reshape(depth, rows_x, rows_y)

    inside = jnp.stack(
        [wide_at > 0, wide_at < last_w, narrow_at > 0, narrow_at < last_n]
    ).astype(jnp.int32)
    edges = block_edges(pressure_start)
    gathered, flow, edges = lax.optimization_barrier((gathered, flow, edges))
    outgoing = line_transforms(gathered, root_x, root_y, count_w, count_n)
    log_perm = lax.all_to_all(
        outgoing, ("wide", "narrow"), split_axis=0, concat_axis=0, tiled=True,
    ).reshape(depth, rows_x, rows_y)

    *lp_edges, log_perm = block_edges(log_perm, keep=True)
    perm_halos = halos(lp_edges)
    pressure = pressure_start
    stored = None
    for step in range(STEPS):
        pressure, edges, stored = advance(
            stored, pressure, halos(edges), flow, inside, log_perm, perm_halos
        )
    return (log_perm, pressure)


def solution(mesh):
    in_specs = (
        P("member", "wide", "narrow"),
        P(),
        P(),
        P(),
        P("member", "wide", "narrow"),
        P("member"),
        P("member"),
        P("member"),
        P("member"),
    )
    out_specs = (P("member", "wide", "narrow"), P("member", "wide", "narrow"))
    return jax.shard_map(body, mesh=mesh, in_specs=in_specs, out_specs=out_specs, check_vma=False)
```
